32 devices in a mesh: groups: 2 (over x), expert: 16 (over z, y, core).
Axes of the slice: x: 2, y: 2, z: 4, core: 2. Of those that a mesh axis runs over, the one named last changes fastest.
Arguments:
- tokens: bfloat16 [4096, 2048], P(('groups', 'expert')), parts along dimension 0, may hold values from -12 to 12
- out_grad: bfloat16 [4096, 2048], P(('groups', 'expert')), parts along dimension 0, may hold values from -6 to 6
- cluster_ids: int32 [4096], P(('groups', 'expert')), parts along dimension 0, may hold values from 0 to 31, as said below
- routes: int32 [1024, 8], P(('groups', 'expert')), parts along dimension 0, may hold values from 0 to 15, all different within a row; in each aligned block of 32 rows (0 to 31, 32 to 63, ...) at most 32 rows name the same one
- route_weights: float32 [1024, 8], P(('groups', 'expert')), parts along dimension 0, may hold values from 0.05 to 0.5
- gate_weight: bfloat16 [16, 2048, 768], P('expert'), may hold values from -0.125 to 0.125
- up_weight: bfloat16 [16, 2048, 768], P('expert'), may hold values from -0.125 to 0.125
- down_weight: bfloat16 [16, 768, 2048], P('expert'), may hold values from -0.21875 to 0.21875
Outputs:
- layer_out: float32 [4096, 2048], P(('groups', 'expert')), parts along dimension 0
- token_grad: float32 [4096, 2048], P(('groups', 'expert')), parts along dimension 0
The draws below stay inside these ranges and needn't reach their ends.
There are 2 independent parts, one for each index of `groups`. The reference program is written for one: setup_inputs(seed, part) draws one part's arguments, and reference() takes and returns one part's arrays. A program takes and returns all parts, laid end to end along the dimension named above; an argument that names none is the same for every part. Nothing has to cross between parts.
Inputs may be any that keep to these rules, and one draw needn't show every extreme that they name: `cluster_ids`: within each block of 128 tokens every one of the 32 cluster numbers occurs at least once. `routes`: each row names 8 different experts. Among the 32 rows of one index of expert no expert is named more than 32 times, and in some such blocks one expert is named exactly 32 times.
All inputs are finite; a program needn't handle non-finite values.
Results may differ from the reference program's by a relative error of at most 0.0027.
Values may be sent and summed in bfloat16 or wider, within the bound.
No kernel may reach another device: no remote copies, remote signals or barrier semaphores. Data moves between devices by JAX's collectives and lax.ppermute only.
A program may use at most 64 MiB of HBM per device.

```python
import math
import jax
import jax.numpy as jnp
import numpy as np
from jax import lax

D = 2048
FF = 768
TOP = 8
CENT_DEV = 32
TOK_DEV = 128
EXPERTS = 16
TOKENS = 2048
CENTROIDS = 512
CAP = 32
N_EXPERT = 16


def draw_cluster_ids(key, part):
    blocks = TOKENS // TOK_DEV
    key_fill = jax.random.fold_in(key, 11)
    key_order = jax.random.fold_in(key, 23)
    extra = jax.random.randint(key_fill, (blocks, TOK_DEV - CENT_DEV), 0, CENT_DEV, dtype=jnp.int32)
    every_one = jnp.broadcast_to(jnp.arange(CENT_DEV, dtype=jnp.int32)[None, :], (blocks, CENT_DEV))
    joined = jnp.concatenate([every_one, extra], axis=1)
    order_keys = jax.random.split(key_order, blocks)
    shuffled = jax.vmap(lambda one_key, one_row: jax.random.permutation(one_key, one_row))(order_keys, joined)
    return shuffled.reshape(TOKENS).astype(jnp.int32)


def steps_of(stream_key, shape, pieces, least, top_value):
    factor_of = 1.0
    for dim, blocks in pieces:
        heights = jax.random.uniform(jax.random.fold_in(jax.random.fold_in(stream_key, 6), dim), (blocks,), jnp.float32, least / len(pieces), top_value / len(pieces))
        factor_of = factor_of * jnp.repeat(jnp.exp(heights), shape[dim] // blocks).reshape((-1,) + (1,) * (len(shape) - 1 - dim))
    return factor_of


def assign_block(key, own, number, rows, amount, top, bound, slope):
    ranking = jax.random.permutation(key, amount)
    packed, ordinary = portions_of(amount, rows * top, bound, slope, True), portions_of(amount, rows * top, bound, slope, False)
    places = jnp.arange(amount)

    def named(lengths, turn):
        used = int((lengths > 0).sum())
        fixed = max(1, used // 4)
        shifted = fixed + (places - fixed + turn * (used - fixed)) % max(1, amount - fixed)
        return jnp.zeros((amount,), jnp.int32).at[ranking[jnp.where(places < fixed, places, shifted)]].set(jnp.asarray(lengths, jnp.int32))

    lengths = jnp.where(number % 4 == 0, named(packed, number // 4), named(ordinary, number - number // 4 - 1))
    mixed = jax.random.permutation(jax.random.fold_in(own, 3), amount)
    giver, taker = mixed[0:amount // 2 * 2:2], mixed[1:amount // 2 * 2:2]
    margin = jnp.minimum(lengths[giver] - 1, bound - lengths[taker]) // 2
    margin = jnp.where((giver == ranking[0]) | (taker == ranking[0]) | (lengths[taker] == 0), 0, jnp.maximum(margin, 0))
    shifted = jax.random.randint(jax.random.fold_in(own, 4), (amount // 2,), 0, 1 << 20) % (margin + 1)
    lengths = lengths.at[giver].add(-shifted).at[taker].add(shifted)
    items = jnp.searchsorted(jnp.cumsum(lengths), jnp.arange(rows * top), side="right").astype(jnp.int32)
    table = items.reshape(top, rows).T
    table = table[jax.random.permutation(jax.random.fold_in(own, 1), rows)]
    turn = jax.random.randint(jax.random.fold_in(own, 2), (rows, 1), 0, top)
    return jnp.take_along_axis(table, (jnp.arange(top)[None, :] + turn) % top, axis=1)


def portions_of(count, total, most, slope, full):
    weights = [(1 << 20) // math.isqrt(standing ** slope) + 1 for standing in range(1, count + 1)]
    largest = most if full else min(most, max(-(-total // count), total * weights[0] // sum(weights)))
    least = 1 if total - largest >= count - 1 else 0
    holding, spare = [largest] + [least] * (count - 1), total - largest - least * (count - 1)
    while spare > 0:
        candidates = [i for i in range(1, count) if holding[i] < largest] or [i for i in range(1, count) if holding[i] < most]
        pool, remaining = sum([weights[i] for i in candidates]), spare
        for i in candidates:
            addition = min(most - holding[i], max(1, remaining * weights[i] // pool), spare)
            holding[i] = holding[i] + addition
            spare = spare - addition
    return np.array(holding)


def centred(rng, extent, deviation, most, cuts=(), kind=jnp.bfloat16):
    factor_of = steps_of(rng, extent, cuts, -0.22, 0.18) if cuts else 1.0
    entries = jax.random.normal(rng, extent, jnp.float32) * deviation * factor_of
    return jnp.minimum(jnp.maximum(entries, -most), most).astype(kind)


def setup_inputs(seed: int = 0, part: int = 0) -> dict:
    key_of = jax.random.split(jax.random.key(seed), 9)
    part_keys = jax.random.split(jax.random.fold_in(key_of[8], part), 9)
    tokens = centred(part_keys[0], (TOKENS, D), 2.0, 12.0, ((0, 16),))
    out_grad = centred(part_keys[1], (TOKENS, D), 1.0, 6.0, ((0, 16),))
    cluster_ids = draw_cluster_ids(jax.random.fold_in(jax.random.fold_in(key_of[8], part), 71), part)
    routes_keys = jax.random.split(jax.random.fold_in(part_keys[3], 1), CENTROIDS // CENT_DEV)
    routes_turns = jax.random.permutation(jax.random.fold_in(part_keys[3], 3), CENTROIDS // CENT_DEV)
    routes = jax.vmap(lambda own, number: assign_block(jax.random.fold_in(part_keys[3], 2), own, number, CENT_DEV, EXPERTS, TOP, CAP, 2))(routes_keys, routes_turns).reshape((CENTROIDS, TOP))
    route_weights = jnp.clip(jnp.exp(math.log(0.5) - 2.3025851 * jax.random.uniform(part_keys[4], (CENTROIDS, TOP), jnp.float32) ** steps_of(part_keys[4], (CENTROIDS, TOP), ((0, 16),), -0.2, 0.2)), 0.05, 0.5)
    gate_weight = centred(key_of[5], (EXPERTS, D, FF), D ** -0.5, 0.125, ((0, 16),))
    up_weight = centred(key_of[6], (EXPERTS, D, FF), D ** -0.5, 0.125, ((0, 16),))
    down_weight = centred(key_of[7], (EXPERTS, FF, D), FF ** -0.5, 0.21875, ((0, 16),))
    return {"tokens": tokens, "out_grad": out_grad, "cluster_ids": cluster_ids, "routes": routes, "route_weights": route_weights, "gate_weight": gate_weight, "up_weight": up_weight, "down_weight": down_weight}


def reference(tokens, out_grad, cluster_ids, routes, route_weights, gate_weight, up_weight, down_weight):
    blocks = N_EXPERT
    pair_count = CENT_DEV * TOP
    tok_blocks = tokens.reshape(blocks, TOK_DEV, D)
    grad_blocks = out_grad.reshape(blocks, TOK_DEV, D)
    cluster_blocks = cluster_ids.reshape(blocks, TOK_DEV)
    member = (cluster_blocks[:, :, None] == jnp.arange(CENT_DEV, dtype=jnp.int32)[None, None, :]).astype(jnp.float32)
    counts = jnp.sum(member, axis=1)
    centroid = jnp.einsum('ntc,ntd->ncd', member, tok_blocks.astype(jnp.float32)) / counts[:, :, None]
    grad_sum = jnp.einsum('ntc,ntd->ncd', member, grad_blocks.astype(jnp.float32))
    cent_in = centroid.astype(jnp.bfloat16)
    grad_in = grad_sum.astype(jnp.bfloat16)
    routed = routes.reshape(blocks, pair_count).astype(jnp.int32)
    matches = (routed[:, :, None] == jnp.arange(EXPERTS, dtype=jnp.int32)[None, None, :]).astype(jnp.int32)
    earlier = jnp.cumsum(matches, axis=1) - matches
    position = jnp.sum(earlier * matches, axis=2).astype(jnp.int32)
    slot_of = routed * CAP + position
    block_index = jnp.broadcast_to(jnp.arange(blocks, dtype=jnp.int32)[:, None], (blocks, pair_count))
    centroid_index = jnp.broadcast_to((jnp.arange(pair_count, dtype=jnp.int32) // TOP)[None, :], (blocks, pair_count))
    holders = jnp.full((blocks, EXPERTS * CAP), CENT_DEV, jnp.int32).at[block_index, slot_of].set(centroid_index)
    holders = jnp.transpose(holders.reshape(blocks, EXPERTS, CAP), (1, 0, 2))
    padded_cent = jnp.concatenate([cent_in, jnp.zeros((blocks, 1, D), jnp.bfloat16)], axis=1)
    padded_grad = jnp.concatenate([grad_in, jnp.zeros((blocks, 1, D), jnp.bfloat16)], axis=1)
    block_column = jnp.arange(blocks, dtype=jnp.int32)[:, None]

    def expert_step(bundle):
        holder, gate_mat, up_mat, down_mat = bundle
        inputs = padded_cent[block_column, holder].reshape(-1, D)
        incoming = padded_grad[block_column, holder].reshape(-1, D)
        gate_act = jnp.dot(inputs, gate_mat, preferred_element_type=jnp.float32)
        up_act = jnp.dot(inputs, up_mat, preferred_element_type=jnp.float32)
        sigmoid_gate = jax.nn.sigmoid(gate_act)
        hidden = (gate_act * sigmoid_gate * up_act).astype(jnp.bfloat16)
        output = jnp.dot(hidden, down_mat, preferred_element_type=jnp.float32).astype(jnp.bfloat16)
        hidden_grad = jnp.dot(incoming, down_mat.T, preferred_element_type=jnp.float32)
        gate_grad = (hidden_grad * up_act * sigmoid_gate * (1.0 + gate_act * (1.0 - sigmoid_gate))).astype(jnp.bfloat16)
        up_grad = (hidden_grad * gate_act * sigmoid_gate).astype(jnp.bfloat16)
        summed = jnp.dot(gate_grad, gate_mat.T, preferred_element_type=jnp.float32) + jnp.dot(up_grad, up_mat.T, preferred_element_type=jnp.float32)
        return output.reshape(blocks, CAP, D), summed.astype(jnp.bfloat16).reshape(blocks, CAP, D)

    outputs_all, grads_all = lax.map(expert_step, (holders, gate_weight, up_weight, down_weight))
    returned = outputs_all[routed, block_index, position].reshape(blocks, CENT_DEV, TOP, D)
    returned_grad = grads_all[routed, block_index, position].reshape(blocks, CENT_DEV, TOP, D)
    weights = route_weights.reshape(blocks, CENT_DEV, TOP)
    combined = jnp.sum(weights[:, :, :, None] * returned.astype(jnp.float32), axis=2)
    centroid_grad = jnp.sum(weights[:, :, :, None] * returned_grad.astype(jnp.float32), axis=2) - grad_sum
    layer_out = tok_blocks.astype(jnp.float32) + (combined - centroid)[block_column, cluster_blocks]
    token_grad = grad_blocks.astype(jnp.float32) + (centroid_grad / counts[:, :, None])[block_column, cluster_blocks]
    return layer_out.reshape(TOKENS, D), token_grad.reshape(TOKENS, D)
```

```python
import jax
import jax.numpy as jnp
from jax import lax
from jax.sharding import PartitionSpec as P


def expert_forward(inputs, gate_mat, up_mat, down_mat):
    gate_act = jnp.dot(inputs, gate_mat, preferred_element_type=jnp.float32)
    up_act = jnp.dot(inputs, up_mat, preferred_element_type=jnp.float32)
    sigmoid_gate = jax.nn.sigmoid(gate_act)
    hidden = (gate_act * sigmoid_gate * up_act).astype(jnp.bfloat16)
    output = jnp.dot(hidden, down_mat, preferred_element_type=jnp.float32).astype(jnp.bfloat16)
    return (output, gate_act, up_act)


def expert_backward(incoming, gate_act, up_act, gate_mat, up_mat, down_mat):
    against = (((1,), (1,)), ((), ()))
    hidden_grad = lax.dot_general(incoming, down_mat, against, preferred_element_type=jnp.float32)
    sigmoid_gate = jax.nn.sigmoid(gate_act)
    gate_grad = (
        hidden_grad * up_act * sigmoid_gate * (1.0 + gate_act * (1.0 - sigmoid_gate))
    ).astype(jnp.bfloat16)
    up_grad = (hidden_grad * gate_act * sigmoid_gate).astype(jnp.bfloat16)
    summed = lax.dot_general(gate_grad, gate_mat, against, preferred_element_type=jnp.float32)
    summed = summed + lax.dot_general(up_grad, up_mat, against, preferred_element_type=jnp.float32)
    return summed.astype(jnp.bfloat16)


def per_device_slots(
    tokens, out_grad, cluster_ids, routes, route_weights, gate_weight, up_weight, down_weight
):
    model_width = tokens.shape[1]
    cent_rows = routes.shape[0]
    fanout = routes.shape[1]
    experts = lax.axis_size("expert")
    capacity = min(cent_rows, 2 * cent_rows * fanout // experts)
    member = (cluster_ids[:, None] == jnp.arange(cent_rows, dtype=jnp.int32)[None, :]).astype(
        jnp.bfloat16
    )
    counts = jnp.sum(member.astype(jnp.float32), axis=0)
    contract = (((0,), (0,)), ((), ()))
    centroid = (
        lax.dot_general(member, tokens, contract, preferred_element_type=jnp.float32)
        / counts[:, None]
    )
    grad_sum = lax.dot_general(member, out_grad, contract, preferred_element_type=jnp.float32)
    pair_ids = routes.reshape(-1)
    matches = (pair_ids[:, None] == jnp.arange(experts, dtype=jnp.int32)[None, :]).astype(jnp.int32)
    earlier = jnp.cumsum(matches, axis=0) - matches
    position = jnp.sum(earlier * matches, axis=1)
    slot_of = (pair_ids * capacity + position).reshape(cent_rows, fanout)
    slot_range = jnp.arange(experts * capacity, dtype=jnp.int32)
    placing = jnp.any(slot_of[None, :, :] == slot_range[:, None, None], axis=2).astype(jnp.bfloat16)
    send_cent = jnp.dot(placing, centroid.astype(jnp.bfloat16), preferred_element_type=jnp.float32)
    send_cent = send_cent.astype(jnp.bfloat16).reshape(experts, capacity, model_width)
    send_grad = jnp.dot(placing, grad_sum.astype(jnp.bfloat16), preferred_element_type=jnp.float32)
    send_grad = send_grad.astype(jnp.bfloat16).reshape(experts, capacity, model_width)
    gate_mat = gate_weight[0]
    up_mat = up_weight[0]
    down_mat = down_weight[0]
    arrived = lax.all_to_all(send_cent, "expert", split_axis=0, concat_axis=0, tiled=True)
    output, gate_act, up_act = expert_forward(
        arrived.reshape(-1, model_width), gate_mat, up_mat, down_mat
    )
    results = lax.all_to_all(
        output.reshape(experts, capacity, model_width),
        "expert",
        split_axis=0,
        concat_axis=0,
        tiled=True,
    )
    arrived_grad = lax.all_to_all(send_grad, "expert", split_axis=0, concat_axis=0, tiled=True)
    input_grad = expert_backward(
        arrived_grad.reshape(-1, model_width), gate_act, up_act, gate_mat, up_mat, down_mat
    )
    results_grad = lax.all_to_all(
        input_grad.reshape(experts, capacity, model_width),
        "expert",
        split_axis=0,
        concat_axis=0,
        tiled=True,
    )
    returned = results.reshape(-1, model_width)[slot_of]
    returned_grad = results_grad.reshape(-1, model_width)[slot_of]
    combined = jnp.sum(route_weights[:, :, None] * returned.astype(jnp.float32), axis=1)
    centroid_grad = (
        jnp.sum(route_weights[:, :, None] * returned_grad.astype(jnp.float32), axis=1) - grad_sum
    )
    layer_out = tokens.astype(jnp.float32) + jnp.take(combined - centroid, cluster_ids, axis=0)
    token_grad = out_grad.astype(jnp.float32) + jnp.take(
        centroid_grad / counts[:, None], cluster_ids, axis=0
    )
    return (layer_out, token_grad)


def expert_dense(cent_in, grad_in, gate_mat, up_mat, down_mat):
    against = (((1,), (1,)), ((), ()))
    gate_act = jnp.dot(cent_in, gate_mat, preferred_element_type=jnp.float32)
    up_act = jnp.dot(cent_in, up_mat, preferred_element_type=jnp.float32)
    sigmoid_gate = jax.nn.sigmoid(gate_act)
    hidden = (gate_act * sigmoid_gate * up_act).astype(jnp.bfloat16)
    output = jnp.dot(hidden, down_mat, preferred_element_type=jnp.float32).astype(jnp.bfloat16)
    hidden_grad = lax.dot_general(grad_in, down_mat, against, preferred_element_type=jnp.float32)
    gate_grad = (
        hidden_grad * up_act * sigmoid_gate * (1.0 + gate_act * (1.0 - sigmoid_gate))
    ).astype(jnp.bfloat16)
    up_grad = (hidden_grad * gate_act * sigmoid_gate).astype(jnp.bfloat16)
    summed = lax.dot_general(gate_grad, gate_mat, against, preferred_element_type=jnp.float32)
    summed = summed + lax.dot_general(up_grad, up_mat, against, preferred_element_type=jnp.float32)
    return output, summed.astype(jnp.bfloat16)


def per_device_dense(
    tokens, out_grad, cluster_ids, routes, route_weights, gate_weight, up_weight, down_weight
):
    cent_rows = routes.shape[0]
    me = lax.axis_index("expert")
    member = (cluster_ids[:, None] == jnp.arange(cent_rows, dtype=jnp.int32)[None, :]).astype(
        jnp.bfloat16
    )
    counts = jnp.sum(member.astype(jnp.float32), axis=0)
    contract = (((0,), (0,)), ((), ()))
    centroid = (
        lax.dot_general(member, tokens, contract, preferred_element_type=jnp.float32)
        / counts[:, None]
    )
    grad_sum = lax.dot_general(member, out_grad, contract, preferred_element_type=jnp.float32)
    both = jnp.stack([centroid.astype(jnp.bfloat16), grad_sum.astype(jnp.bfloat16)])
    gathered = lax.all_gather(both, "expert", axis=1, tiled=True)
    all_routes = lax.all_gather(routes, "expert", axis=0, tiled=True)
    all_weights = lax.all_gather(route_weights, "expert", axis=0, tiled=True)
    mine = jnp.sum(jnp.where(all_routes == me, all_weights, 0.0), axis=1)
    output, input_grad = expert_dense(
        gathered[0], gathered[1], gate_weight[0], up_weight[0], down_weight[0]
    )
    parts = jnp.stack(
        [
            (mine[:, None] * output.astype(jnp.float32)).astype(jnp.bfloat16),
            (mine[:, None] * input_grad.astype(jnp.float32)).astype(jnp.bfloat16),
        ]
    )
    summed = lax.psum_scatter(parts, "expert", scatter_dimension=1, tiled=True)
    combined = summed[0].astype(jnp.float32)
    centroid_grad = summed[1].astype(jnp.float32) - grad_sum
    layer_out = tokens.astype(jnp.float32) + jnp.take(combined - centroid, cluster_ids, axis=0)
    token_grad = out_grad.astype(jnp.float32) + jnp.take(
        centroid_grad / counts[:, None], cluster_ids, axis=0
    )
    return (layer_out, token_grad)


def per_device(*args):
    routes = args[3]
    cent_rows, fanout = routes.shape
    experts = lax.axis_size("expert")
    capacity = min(cent_rows, 2 * cent_rows * fanout // experts)
    if capacity == cent_rows:
        return per_device_dense(*args)
    return per_device_slots(*args)


def solution(mesh):
    placed = (
        P(("groups", "expert"), None),
        P(("groups", "expert"), None),
        P(("groups", "expert")),
        P(("groups", "expert"), None),
        P(("groups", "expert"), None),
        P("expert", None, None),
        P("expert", None, None),
        P("expert", None, None),
    )
    return jax.shard_map(
        per_device,
        mesh=mesh,
        in_specs=placed,
        out_specs=(P(("groups", "expert"), None), P(("groups", "expert"), None)),
        check_vma=False,
    )
```

```python
import jax
import jax.numpy as jnp
from jax import lax
from jax.sharding import PartitionSpec as P


def expert_forward(inputs, gate_mat, up_mat, down_mat):
    gate_act = jnp.dot(inputs, gate_mat, preferred_element_type=jnp.float32)
    up_act = jnp.dot(inputs, up_mat, preferred_element_type=jnp.float32)
    sigmoid_gate = jax.nn.sigmoid(gate_act)
    hidden = (gate_act * sigmoid_gate * up_act).astype(jnp.bfloat16)
    output = jnp.dot(hidden, down_mat, preferred_element_type=jnp.float32).astype(jnp.bfloat16)
    return (output, gate_act, up_act)


def expert_backward(incoming, gate_act, up_act, gate_mat, up_mat, down_mat):
    against = (((1,), (1,)), ((), ()))
    hidden_grad = lax.dot_general(incoming, down_mat, against, preferred_element_type=jnp.float32)
    sigmoid_gate = jax.nn.sigmoid(gate_act)
    gate_grad = (
        hidden_grad * up_act * sigmoid_gate * (1.0 + gate_act * (1.0 - sigmoid_gate))
    ).astype(jnp.bfloat16)
    up_grad = (hidden_grad * gate_act * sigmoid_gate).astype(jnp.bfloat16)
    summed = lax.dot_general(gate_grad, gate_mat, against, preferred_element_type=jnp.float32)
    summed = summed + lax.dot_general(up_grad, up_mat, against, preferred_element_type=jnp.float32)
    return summed.astype(jnp.bfloat16)


def per_device_slots(
    tokens, out_grad, cluster_ids, routes, route_weights, gate_weight, up_weight, down_weight
):
    model_width = tokens.shape[1]
    cent_rows = routes.shape[0]
    fanout = routes.shape[1]
    experts = lax.axis_size("expert")
    capacity = min(cent_rows, 2 * cent_rows * fanout // experts)
    member = (cluster_ids[:, None] == jnp.arange(cent_rows, dtype=jnp.int32)[None, :]).astype(
        jnp.bfloat16
    )
    counts = jnp.sum(member.astype(jnp.float32), axis=0)
    contract = (((0,), (0,)), ((), ()))
    centroid = (
        lax.dot_general(member, tokens, contract, preferred_element_type=jnp.float32)
        / counts[:, None]
    )
    grad_sum = lax.dot_general(member, out_grad, contract, preferred_element_type=jnp.float32)
    pair_ids = routes.reshape(-1)
    matches = (pair_ids[:, None] == jnp.arange(experts, dtype=jnp.int32)[None, :]).astype(jnp.int32)
    earlier = jnp.cumsum(matches, axis=0) - matches
    position = jnp.sum(earlier * matches, axis=1)
    slot_of = (pair_ids * capacity + position).reshape(cent_rows, fanout)
    slot_range = jnp.arange(experts * capacity, dtype=jnp.int32)
    placing = jnp.any(slot_of[None, :, :] == slot_range[:, None, None], axis=2).astype(jnp.bfloat16)
    send_cent = jnp.dot(placing, centroid.astype(jnp.bfloat16), preferred_element_type=jnp.float32)
    send_cent = send_cent.astype(jnp.bfloat16).reshape(experts, capacity, model_width)
    send_grad = jnp.dot(placing, grad_sum.astype(jnp.bfloat16), preferred_element_type=jnp.float32)
    send_grad = send_grad.astype(jnp.bfloat16).reshape(experts, capacity, model_width)
    gate_mat = gate_weight[0]
    up_mat = up_weight[0]
    down_mat = down_weight[0]
    arrived = lax.all_to_all(send_cent, "expert", split_axis=0, concat_axis=0, tiled=True)
    output, gate_act, up_act = expert_forward(
        arrived.reshape(-1, model_width), gate_mat, up_mat, down_mat
    )
    results = lax.all_to_all(
        output.reshape(experts, capacity, model_width),
        "expert",
        split_axis=0,
        concat_axis=0,
        tiled=True,
    )
    arrived_grad = lax.all_to_all(send_grad, "expert", split_axis=0, concat_axis=0, tiled=True)
    input_grad = expert_backward(
        arrived_grad.reshape(-1, model_width), gate_act, up_act, gate_mat, up_mat, down_mat
    )
    results_grad = lax.all_to_all(
        input_grad.reshape(experts, capacity, model_width),
        "expert",
        split_axis=0,
        concat_axis=0,
        tiled=True,
    )
    returned = results.reshape(-1, model_width)[slot_of]
    returned_grad = results_grad.reshape(-1, model_width)[slot_of]
    combined = jnp.sum(route_weights[:, :, None] * returned.astype(jnp.float32), axis=1)
    centroid_grad = (
        jnp.sum(route_weights[:, :, None] * returned_grad.astype(jnp.float32), axis=1) - grad_sum
    )
    layer_out = tokens.astype(jnp.float32) + jnp.take(combined - centroid, cluster_ids, axis=0)
    token_grad = out_grad.astype(jnp.float32) + jnp.take(
        centroid_grad / counts[:, None], cluster_ids, axis=0
    )
    return (layer_out, token_grad)


def expert_dense(cent_in, grad_in, gate_mat, up_mat, down_mat):
    against = (((1,), (1,)), ((), ()))
    gate_act = jnp.dot(cent_in, gate_mat, preferred_element_type=jnp.float32)
    up_act = jnp.dot(cent_in, up_mat, preferred_element_type=jnp.float32)
    sigmoid_gate = jax.nn.sigmoid(gate_act)
    hidden = (gate_act * sigmoid_gate * up_act).astype(jnp.bfloat16)
    output = jnp.dot(hidden, down_mat, preferred_element_type=jnp.float32).astype(jnp.bfloat16)
    hidden_grad = lax.dot_general(grad_in, down_mat, against, preferred_element_type=jnp.float32)
    gate_grad = (
        hidden_grad * up_act * sigmoid_gate * (1.0 + gate_act * (1.0 - sigmoid_gate))
    ).astype(jnp.bfloat16)
    up_grad = (hidden_grad * gate_act * sigmoid_gate).astype(jnp.bfloat16)
    summed = lax.dot_general(gate_grad, gate_mat, against, preferred_element_type=jnp.float32)
    summed = summed + lax.dot_general(up_grad, up_mat, against, preferred_element_type=jnp.float32)
    return output, summed.astype(jnp.bfloat16)


def per_device_dense(
    tokens, out_grad, cluster_ids, routes, route_weights, gate_weight, up_weight, down_weight
):
    cent_rows = routes.shape[0]
    me = lax.axis_index("expert")
    member = (cluster_ids[:, None] == jnp.arange(cent_rows, dtype=jnp.int32)[None, :]).astype(
        jnp.bfloat16
    )
    counts = jnp.sum(member.astype(jnp.float32), axis=0)
    contract = (((0,), (0,)), ((), ()))
    centroid = (
        lax.dot_general(member, tokens, contract, preferred_element_type=jnp.float32)
        / counts[:, None]
    )
    grad_sum = lax.dot_general(member, out_grad, contract, preferred_element_type=jnp.float32)
    experts = lax.axis_size("expert")
    model_width = tokens.shape[1]
    picked = routes[:, :, None] == jnp.arange(experts, dtype=jnp.int32)[None, None, :]
    per_expert = jnp.sum(jnp.where(picked, route_weights[:, :, None], 0.0), axis=1)
    weight_hi = per_expert.astype(jnp.bfloat16)
    weight_lo = (per_expert - weight_hi.astype(jnp.float32)).astype(jnp.bfloat16)
    side = jnp.concatenate([weight_hi, weight_lo], axis=1)
    side_width = -(-side.shape[1] // 128) * 128
    side = jnp.pad(side, ((0, 0), (0, side_width - side.shape[1])))
    payload = jnp.concatenate(
        [centroid.astype(jnp.bfloat16), grad_sum.astype(jnp.bfloat16), side], axis=1
    )
    gathered = lax.all_gather(payload, "expert", axis=0, tiled=True)
    cent_all = gathered[:, :model_width]
    grad_all = gathered[:, model_width : 2 * model_width]
    side_all = gathered[:, 2 * model_width : 2 * model_width + 2 * experts].astype(jnp.float32)
    column = jnp.arange(experts, dtype=jnp.int32)[None, :]
    mine = jnp.sum(jnp.where(column == me, side_all[:, :experts] + side_all[:, experts:], 0.0), axis=1)
    output, input_grad = expert_dense(
        cent_all, grad_all, gate_weight[0], up_weight[0], down_weight[0]
    )
    parts = jnp.stack(
        [
            (mine[:, None] * output.astype(jnp.float32)).astype(jnp.bfloat16),
            (mine[:, None] * input_grad.astype(jnp.float32)).astype(jnp.bfloat16),
        ]
    )
    summed = lax.psum_scatter(parts, "expert", scatter_dimension=1, tiled=True)
    combined = summed[0].astype(jnp.float32)
    centroid_grad = summed[1].astype(jnp.float32) - grad_sum
    layer_out = tokens.astype(jnp.float32) + jnp.take(combined - centroid, cluster_ids, axis=0)
    token_grad = out_grad.astype(jnp.float32) + jnp.take(
        centroid_grad / counts[:, None], cluster_ids, axis=0
    )
    return (layer_out, token_grad)


def per_device(*args):
    routes = args[3]
    cent_rows, fanout = routes.shape
    experts = lax.axis_size("expert")
    capacity = min(cent_rows, 2 * cent_rows * fanout // experts)
    if capacity == cent_rows:
        return per_device_dense(*args)
    return per_device_slots(*args)


def solution(mesh):
    placed = (
        P(("groups", "expert"), None),
        P(("groups", "expert"), None),
        P(("groups", "expert")),
        P(("groups", "expert"), None),
        P(("groups", "expert"), None),
        P("expert", None, None),
        P("expert", None, None),
        P("expert", None, None),
    )
    return jax.shard_map(
        per_device,
        mesh=mesh,
        in_specs=placed,
        out_specs=(P(("groups", "expert"), None), P(("groups", "expert"), None)),
        check_vma=False,
    )
```

```python
import jax
import jax.numpy as jnp
from jax import lax
from jax.sharding import PartitionSpec as P


def expert_forward(inputs, gate_mat, up_mat, down_mat):
    gate_act = jnp.dot(inputs, gate_mat, preferred_element_type=jnp.float32)
    up_act = jnp.dot(inputs, up_mat, preferred_element_type=jnp.float32)
    sigmoid_gate = jax.nn.sigmoid(gate_act)
    hidden = (gate_act * sigmoid_gate * up_act).astype(jnp.bfloat16)
    output = jnp.dot(hidden, down_mat, preferred_element_type=jnp.float32).astype(jnp.bfloat16)
    return (output, gate_act, up_act)


def expert_backward(incoming, gate_act, up_act, gate_mat, up_mat, down_mat):
    against = (((1,), (1,)), ((), ()))
    hidden_grad = lax.dot_general(incoming, down_mat, against, preferred_element_type=jnp.float32)
    sigmoid_gate = jax.nn.sigmoid(gate_act)
    gate_grad = (
        hidden_grad * up_act * sigmoid_gate * (1.0 + gate_act * (1.0 - sigmoid_gate))
    ).astype(jnp.bfloat16)
    up_grad = (hidden_grad * gate_act * sigmoid_gate).astype(jnp.bfloat16)
    summed = lax.dot_general(gate_grad, gate_mat, against, preferred_element_type=jnp.float32)
    summed = summed + lax.dot_general(up_grad, up_mat, against, preferred_element_type=jnp.float32)
    return summed.astype(jnp.bfloat16)


def per_device_slots(
    tokens, out_grad, cluster_ids, routes, route_weights, gate_weight, up_weight, down_weight
):
    model_width = tokens.shape[1]
    cent_rows = routes.shape[0]
    fanout = routes.shape[1]
    experts = lax.axis_size("expert")
    capacity = min(cent_rows, 2 * cent_rows * fanout // experts)
    member = (cluster_ids[:, None] == jnp.arange(cent_rows, dtype=jnp.int32)[None, :]).astype(
        jnp.bfloat16
    )
    counts = jnp.sum(member.astype(jnp.float32), axis=0)
    contract = (((0,), (0,)), ((), ()))
    centroid = (
        lax.dot_general(member, tokens, contract, preferred_element_type=jnp.float32)
        / counts[:, None]
    )
    grad_sum = lax.dot_general(member, out_grad, contract, preferred_element_type=jnp.float32)
    pair_ids = routes.reshape(-1)
    matches = (pair_ids[:, None] == jnp.arange(experts, dtype=jnp.int32)[None, :]).astype(jnp.int32)
    earlier = jnp.cumsum(matches, axis=0) - matches
    position = jnp.sum(earlier * matches, axis=1)
    slot_of = (pair_ids * capacity + position).reshape(cent_rows, fanout)
    slot_range = jnp.arange(experts * capacity, dtype=jnp.int32)
    placing = jnp.any(slot_of[None, :, :] == slot_range[:, None, None], axis=2).astype(jnp.bfloat16)
    send_cent = jnp.dot(placing, centroid.astype(jnp.bfloat16), preferred_element_type=jnp.float32)
    send_cent = send_cent.astype(jnp.bfloat16).reshape(experts, capacity, model_width)
    send_grad = jnp.dot(placing, grad_sum.astype(jnp.bfloat16), preferred_element_type=jnp.float32)
    send_grad = send_grad.astype(jnp.bfloat16).reshape(experts, capacity, model_width)
    gate_mat = gate_weight[0]
    up_mat = up_weight[0]
    down_mat = down_weight[0]
    arrived = lax.all_to_all(send_cent, "expert", split_axis=0, concat_axis=0, tiled=True)
    output, gate_act, up_act = expert_forward(
        arrived.reshape(-1, model_width), gate_mat, up_mat, down_mat
    )
    results = lax.all_to_all(
        output.reshape(experts, capacity, model_width),
        "expert",
        split_axis=0,
        concat_axis=0,
        tiled=True,
    )
    arrived_grad = lax.all_to_all(send_grad, "expert", split_axis=0, concat_axis=0, tiled=True)
    input_grad = expert_backward(
        arrived_grad.reshape(-1, model_width), gate_act, up_act, gate_mat, up_mat, down_mat
    )
    results_grad = lax.all_to_all(
        input_grad.reshape(experts, capacity, model_width),
        "expert",
        split_axis=0,
        concat_axis=0,
        tiled=True,
    )
    returned = results.reshape(-1, model_width)[slot_of]
    returned_grad = results_grad.reshape(-1, model_width)[slot_of]
    combined = jnp.sum(route_weights[:, :, None] * returned.astype(jnp.float32), axis=1)
    centroid_grad = (
        jnp.sum(route_weights[:, :, None] * returned_grad.astype(jnp.float32), axis=1) - grad_sum
    )
    layer_out = tokens.astype(jnp.float32) + jnp.take(combined - centroid, cluster_ids, axis=0)
    token_grad = out_grad.astype(jnp.float32) + jnp.take(
        centroid_grad / counts[:, None], cluster_ids, axis=0
    )
    return (layer_out, token_grad)


def expert_dense(cent_in, grad_in, gate_mat, up_mat, down_mat):
    against = (((1,), (1,)), ((), ()))
    gate_act = jnp.dot(cent_in, gate_mat, preferred_element_type=jnp.float32)
    up_act = jnp.dot(cent_in, up_mat, preferred_element_type=jnp.float32)
    sigmoid_gate = jax.nn.sigmoid(gate_act)
    hidden = (gate_act * sigmoid_gate * up_act).astype(jnp.bfloat16)
    output = jnp.dot(hidden, down_mat, preferred_element_type=jnp.float32).astype(jnp.bfloat16)
    hidden_grad = lax.dot_general(grad_in, down_mat, against, preferred_element_type=jnp.float32)
    gate_grad = (
        hidden_grad * up_act * sigmoid_gate * (1.0 + gate_act * (1.0 - sigmoid_gate))
    ).astype(jnp.bfloat16)
    up_grad = (hidden_grad * gate_act * sigmoid_gate).astype(jnp.bfloat16)
    summed = lax.dot_general(gate_grad, gate_mat, against, preferred_element_type=jnp.float32)
    summed = summed + lax.dot_general(up_grad, up_mat, against, preferred_element_type=jnp.float32)
    return output, summed.astype(jnp.bfloat16)


def per_device_dense(
    tokens, out_grad, cluster_ids, routes, route_weights, gate_weight, up_weight, down_weight
):
    cent_rows = routes.shape[0]
    me = lax.axis_index("expert")
    member = (cluster_ids[:, None] == jnp.arange(cent_rows, dtype=jnp.int32)[None, :]).astype(
        jnp.bfloat16
    )
    counts = jnp.sum(member.astype(jnp.float32), axis=0)
    contract = (((0,), (0,)), ((), ()))
    centroid = (
        lax.dot_general(member, tokens, contract, preferred_element_type=jnp.float32)
        / counts[:, None]
    )
    grad_sum = lax.dot_general(member, out_grad, contract, preferred_element_type=jnp.float32)
    experts = lax.axis_size("expert")
    model_width = tokens.shape[1]
    picked = routes[:, :, None] == jnp.arange(experts, dtype=jnp.int32)[None, None, :]
    per_expert = jnp.sum(jnp.where(picked, route_weights[:, :, None], 0.0), axis=1)
    weight_hi = per_expert.astype(jnp.bfloat16)
    weight_lo = (per_expert - weight_hi.astype(jnp.float32)).astype(jnp.bfloat16)
    side = jnp.concatenate([weight_hi, weight_lo], axis=1)
    side_width = -(-side.shape[1] // 128) * 128
    side = jnp.pad(side, ((0, 0), (0, side_width - side.shape[1])))
    payload = jnp.concatenate([centroid.astype(jnp.bfloat16), side], axis=1)
    gathered = lax.all_gather(payload, "expert", axis=0, tiled=True)
    grad_all = lax.all_gather(grad_sum.astype(jnp.bfloat16), "expert", axis=0, tiled=True)
    cent_all = gathered[:, :model_width]
    side_all = gathered[:, model_width : model_width + 2 * experts].astype(jnp.float32)
    column = jnp.arange(experts, dtype=jnp.int32)[None, :]
    mine = jnp.sum(jnp.where(column == me, side_all[:, :experts] + side_all[:, experts:], 0.0), axis=1)
    output, input_grad = expert_dense(
        cent_all, grad_all, gate_weight[0], up_weight[0], down_weight[0]
    )
    weighted_out = (mine[:, None] * output.astype(jnp.float32)).astype(jnp.bfloat16)
    weighted_grad = (mine[:, None] * input_grad.astype(jnp.float32)).astype(jnp.bfloat16)
    summed_out = lax.psum_scatter(weighted_out, "expert", scatter_dimension=0, tiled=True)
    summed_grad = lax.psum_scatter(weighted_grad, "expert", scatter_dimension=0, tiled=True)
    combined = summed_out.astype(jnp.float32)
    centroid_grad = summed_grad.astype(jnp.float32) - grad_sum
    layer_out = tokens.astype(jnp.float32) + jnp.take(combined - centroid, cluster_ids, axis=0)
    token_grad = out_grad.astype(jnp.float32) + jnp.take(
        centroid_grad / counts[:, None], cluster_ids, axis=0
    )
    return (layer_out, token_grad)


def per_device(*args):
    routes = args[3]
    cent_rows, fanout = routes.shape
    experts = lax.axis_size("expert")
    capacity = min(cent_rows, 2 * cent_rows * fanout // experts)
    if capacity == cent_rows:
        return per_device_dense(*args)
    return per_device_slots(*args)


def solution(mesh):
    placed = (
        P(("groups", "expert"), None),
        P(("groups", "expert"), None),
        P(("groups", "expert")),
        P(("groups", "expert"), None),
        P(("groups", "expert"), None),
        P("expert", None, None),
        P("expert", None, None),
        P("expert", None, None),
    )
    return jax.shard_map(
        per_device,
        mesh=mesh,
        in_specs=placed,
        out_specs=(P(("groups", "expert"), None), P(("groups", "expert"), None)),
        check_vma=False,
    )
```

```python
import jax
import jax.numpy as jnp
from jax import lax
from jax.sharding import PartitionSpec as P


def expert_forward(inputs, gate_mat, up_mat, down_mat):
    gate_act = jnp.dot(inputs, gate_mat, preferred_element_type=jnp.float32)
    up_act = jnp.dot(inputs, up_mat, preferred_element_type=jnp.float32)
    sigmoid_gate = jax.nn.sigmoid(gate_act)
    hidden = (gate_act * sigmoid_gate * up_act).astype(jnp.bfloat16)
    output = jnp.dot(hidden, down_mat, preferred_element_type=jnp.float32).astype(jnp.bfloat16)
    return (output, gate_act, up_act)


def expert_backward(incoming, gate_act, up_act, gate_mat, up_mat, down_mat):
    against = (((1,), (1,)), ((), ()))
    hidden_grad = lax.dot_general(incoming, down_mat, against, preferred_element_type=jnp.float32)
    sigmoid_gate = jax.nn.sigmoid(gate_act)
    gate_grad = (
        hidden_grad * up_act * sigmoid_gate * (1.0 + gate_act * (1.0 - sigmoid_gate))
    ).astype(jnp.bfloat16)
    up_grad = (hidden_grad * gate_act * sigmoid_gate).astype(jnp.bfloat16)
    summed = lax.dot_general(gate_grad, gate_mat, against, preferred_element_type=jnp.float32)
    summed = summed + lax.dot_general(up_grad, up_mat, against, preferred_element_type=jnp.float32)
    return summed.astype(jnp.bfloat16)


def per_device_slots(
    tokens, out_grad, cluster_ids, routes, route_weights, gate_weight, up_weight, down_weight
):
    model_width = tokens.shape[1]
    cent_rows = routes.shape[0]
    fanout = routes.shape[1]
    experts = lax.axis_size("expert")
    capacity = min(cent_rows, 2 * cent_rows * fanout // experts)
    member = (cluster_ids[:, None] == jnp.arange(cent_rows, dtype=jnp.int32)[None, :]).astype(
        jnp.bfloat16
    )
    counts = jnp.sum(member.astype(jnp.float32), axis=0)
    contract = (((0,), (0,)), ((), ()))
    centroid = (
        lax.dot_general(member, tokens, contract, preferred_element_type=jnp.float32)
        / counts[:, None]
    )
    grad_sum = lax.dot_general(member, out_grad, contract, preferred_element_type=jnp.float32)
    pair_ids = routes.reshape(-1)
    matches = (pair_ids[:, None] == jnp.arange(experts, dtype=jnp.int32)[None, :]).astype(jnp.int32)
    earlier = jnp.cumsum(matches, axis=0) - matches
    position = jnp.sum(earlier * matches, axis=1)
    slot_of = (pair_ids * capacity + position).reshape(cent_rows, fanout)
    slot_range = jnp.arange(experts * capacity, dtype=jnp.int32)
    placing = jnp.any(slot_of[None, :, :] == slot_range[:, None, None], axis=2).astype(jnp.bfloat16)
    send_cent = jnp.dot(placing, centroid.astype(jnp.bfloat16), preferred_element_type=jnp.float32)
    send_cent = send_cent.astype(jnp.bfloat16).reshape(experts, capacity, model_width)
    send_grad = jnp.dot(placing, grad_sum.astype(jnp.bfloat16), preferred_element_type=jnp.float32)
    send_grad = send_grad.astype(jnp.bfloat16).reshape(experts, capacity, model_width)
    gate_mat = gate_weight[0]
    up_mat = up_weight[0]
    down_mat = down_weight[0]
    arrived = lax.all_to_all(send_cent, "expert", split_axis=0, concat_axis=0, tiled=True)
    output, gate_act, up_act = expert_forward(
        arrived.reshape(-1, model_width), gate_mat, up_mat, down_mat
    )
    results = lax.all_to_all(
        output.reshape(experts, capacity, model_width),
        "expert",
        split_axis=0,
        concat_axis=0,
        tiled=True,
    )
    arrived_grad = lax.all_to_all(send_grad, "expert", split_axis=0, concat_axis=0, tiled=True)
    input_grad = expert_backward(
        arrived_grad.reshape(-1, model_width), gate_act, up_act, gate_mat, up_mat, down_mat
    )
    results_grad = lax.all_to_all(
        input_grad.reshape(experts, capacity, model_width),
        "expert",
        split_axis=0,
        concat_axis=0,
        tiled=True,
    )
    returned = results.reshape(-1, model_width)[slot_of]
    returned_grad = results_grad.reshape(-1, model_width)[slot_of]
    combined = jnp.sum(route_weights[:, :, None] * returned.astype(jnp.float32), axis=1)
    centroid_grad = (
        jnp.sum(route_weights[:, :, None] * returned_grad.astype(jnp.float32), axis=1) - grad_sum
    )
    layer_out = tokens.astype(jnp.float32) + jnp.take(combined - centroid, cluster_ids, axis=0)
    token_grad = out_grad.astype(jnp.float32) + jnp.take(
        centroid_grad / counts[:, None], cluster_ids, axis=0
    )
    return (layer_out, token_grad)


def pick(index, options):
    chosen = options[-1]
    for position in range(len(options) - 2, -1, -1):
        chosen = jnp.where(index == position, options[position], chosen)
    return chosen


def line_gather(shard, stride, lines, experts):
    me = lax.axis_index("expert")
    line = me // stride
    here = [(shard, line)]
    ahead, behind = shard, shard
    for step in range(1, lines):
        ahead = lax.ppermute(
            ahead,
            "expert",
            [(j, j + stride) for j in range(experts) if step - 1 <= j // stride < lines - 1],
        )
        behind = lax.ppermute(
            behind,
            "expert",
            [(j, j - stride) for j in range(experts) if 1 <= j // stride <= lines - step],
        )
        here.append((ahead, line - step))
        here.append((behind, line + step))
    slot = lax.broadcasted_iota(jnp.int32, (lines,) + (1,) * shard.ndim, 0)
    stacked = jnp.zeros((lines,) + shard.shape, shard.dtype)
    for piece, origin in here:
        stacked = jnp.where(slot == origin, piece[None], stacked)
    return stacked


def topo_all_gather(shard, experts):
    lines = experts // 4
    me = lax.axis_index("expert")
    column = line_gather(shard, 4, lines, experts)
    across = lax.ppermute(column, "expert", [(j, j ^ 2) for j in range(experts)])
    in_row = (me // 2) % 2
    plane = jnp.stack([pick(in_row, [column, across]), pick(in_row, [across, column])], axis=1)
    partner = lax.ppermute(plane, "expert", [(j, j ^ 1) for j in range(experts)])
    on_chip = me % 2
    full = jnp.stack([pick(on_chip, [plane, partner]), pick(on_chip, [partner, plane])], axis=2)
    return full.reshape((experts * shard.shape[0],) + shard.shape[1:])


def topo_reduce_scatter(blocks, experts):
    lines = experts // 4
    me = lax.axis_index("expert")
    rows = blocks.shape[0] // experts
    cube = blocks.reshape((lines, 2, 2, rows) + blocks.shape[1:])
    on_chip = me % 2
    keep = pick(on_chip, [cube[:, :, 0], cube[:, :, 1]])
    give = pick(on_chip, [cube[:, :, 1], cube[:, :, 0]])
    got = lax.ppermute(give.astype(jnp.bfloat16), "expert", [(j, j ^ 1) for j in range(experts)])
    plane = keep.astype(jnp.float32) + got.astype(jnp.float32)
    in_row = (me // 2) % 2
    keep = pick(in_row, [plane[:, 0], plane[:, 1]])
    give = pick(in_row, [plane[:, 1], plane[:, 0]])
    got = lax.ppermute(give.astype(jnp.bfloat16), "expert", [(j, j ^ 2) for j in range(experts)])
    column = keep + got.astype(jnp.float32)
    line = me // 4
    total = lax.dynamic_index_in_dim(column, line, 0, keepdims=False)
    ahead = jnp.zeros_like(total)
    behind = jnp.zeros_like(total)
    for step in range(1, lines):
        target = jnp.clip(line + lines - step, 0, lines - 1)
        ahead = ahead + lax.dynamic_index_in_dim(column, target, 0, keepdims=False)
        ahead = lax.ppermute(
            ahead.astype(jnp.bfloat16),
            "expert",
            [(j, j + 4) for j in range(experts) if j // 4 <= step - 1],
        ).astype(jnp.float32)
        target = jnp.clip(line - lines + step, 0, lines - 1)
        behind = behind + lax.dynamic_index_in_dim(column, target, 0, keepdims=False)
        behind = lax.ppermute(
            behind.astype(jnp.bfloat16),
            "expert",
            [(j, j - 4) for j in range(experts) if j // 4 >= lines - step],
        ).astype(jnp.float32)
    return total + ahead + behind


def expert_dense(cent_in, grad_in, gate_mat, up_mat, down_mat):
    against = (((1,), (1,)), ((), ()))
    gate_act = jnp.dot(cent_in, gate_mat, preferred_element_type=jnp.float32)
    up_act = jnp.dot(cent_in, up_mat, preferred_element_type=jnp.float32)
    sigmoid_gate = jax.nn.sigmoid(gate_act)
    hidden = (gate_act * sigmoid_gate * up_act).astype(jnp.bfloat16)
    output = jnp.dot(hidden, down_mat, preferred_element_type=jnp.float32).astype(jnp.bfloat16)
    hidden_grad = lax.dot_general(grad_in, down_mat, against, preferred_element_type=jnp.float32)
    gate_grad = (
        hidden_grad * up_act * sigmoid_gate * (1.0 + gate_act * (1.0 - sigmoid_gate))
    ).astype(jnp.bfloat16)
    up_grad = (hidden_grad * gate_act * sigmoid_gate).astype(jnp.bfloat16)
    summed = lax.dot_general(gate_grad, gate_mat, against, preferred_element_type=jnp.float32)
    summed = summed + lax.dot_general(up_grad, up_mat, against, preferred_element_type=jnp.float32)
    return output, summed.astype(jnp.bfloat16)


def per_device_dense(
    tokens, out_grad, cluster_ids, routes, route_weights, gate_weight, up_weight, down_weight
):
    cent_rows = routes.shape[0]
    me = lax.axis_index("expert")
    member = (cluster_ids[:, None] == jnp.arange(cent_rows, dtype=jnp.int32)[None, :]).astype(
        jnp.bfloat16
    )
    counts = jnp.sum(member.astype(jnp.float32), axis=0)
    contract = (((0,), (0,)), ((), ()))
    centroid = (
        lax.dot_general(member, tokens, contract, preferred_element_type=jnp.float32)
        / counts[:, None]
    )
    grad_sum = lax.dot_general(member, out_grad, contract, preferred_element_type=jnp.float32)
    experts = lax.axis_size("expert")
    model_width = tokens.shape[1]
    picked = routes[:, :, None] == jnp.arange(experts, dtype=jnp.int32)[None, None, :]
    per_expert = jnp.sum(jnp.where(picked, route_weights[:, :, None], 0.0), axis=1)
    weight_hi = per_expert.astype(jnp.bfloat16)
    weight_lo = (per_expert - weight_hi.astype(jnp.float32)).astype(jnp.bfloat16)
    side = jnp.concatenate([weight_hi, weight_lo], axis=1)
    side_width = -(-side.shape[1] // 128) * 128
    side = jnp.pad(side, ((0, 0), (0, side_width - side.shape[1])))
    payload = jnp.concatenate(
        [centroid.astype(jnp.bfloat16), grad_sum.astype(jnp.bfloat16), side], axis=1
    )
    gathered = topo_all_gather(payload, experts)
    cent_all = gathered[:, :model_width]
    grad_all = gathered[:, model_width : 2 * model_width]
    side_all = gathered[:, 2 * model_width : 2 * model_width + 2 * experts].astype(jnp.float32)
    column = jnp.arange(experts, dtype=jnp.int32)[None, :]
    mine = jnp.sum(jnp.where(column == me, side_all[:, :experts] + side_all[:, experts:], 0.0), axis=1)
    output, input_grad = expert_dense(
        cent_all, grad_all, gate_weight[0], up_weight[0], down_weight[0]
    )
    parts = jnp.concatenate(
        [
            (mine[:, None] * output.astype(jnp.float32)).astype(jnp.bfloat16),
            (mine[:, None] * input_grad.astype(jnp.float32)).astype(jnp.bfloat16),
        ],
        axis=1,
    )
    summed = topo_reduce_scatter(parts, experts)
    combined = summed[:, :model_width]
    centroid_grad = summed[:, model_width:] - grad_sum
    layer_out = tokens.astype(jnp.float32) + jnp.take(combined - centroid, cluster_ids, axis=0)
    token_grad = out_grad.astype(jnp.float32) + jnp.take(
        centroid_grad / counts[:, None], cluster_ids, axis=0
    )
    return (layer_out, token_grad)


def per_device(*args):
    routes = args[3]
    cent_rows, fanout = routes.shape
    experts = lax.axis_size("expert")
    capacity = min(cent_rows, 2 * cent_rows * fanout // experts)
    if capacity == cent_rows and experts % 4 == 0:
        return per_device_dense(*args)
    return per_device_slots(*args)


def solution(mesh):
    placed = (
        P(("groups", "expert"), None),
        P(("groups", "expert"), None),
        P(("groups", "expert")),
        P(("groups", "expert"), None),
        P(("groups", "expert"), None),
        P("expert", None, None),
        P("expert", None, None),
        P("expert", None, None),
    )
    return jax.shard_map(
        per_device,
        mesh=mesh,
        in_specs=placed,
        out_specs=(P(("groups", "expert"), None), P(("groups", "expert"), None)),
        check_vma=False,
    )
```

```python
import jax
import jax.numpy as jnp
from jax import lax
from jax.sharding import PartitionSpec as P


def expert_forward(inputs, gate_mat, up_mat, down_mat):
    gate_act = jnp.dot(inputs, gate_mat, preferred_element_type=jnp.float32)
    up_act = jnp.dot(inputs, up_mat, preferred_element_type=jnp.float32)
    sigmoid_gate = jax.nn.sigmoid(gate_act)
    hidden = (gate_act * sigmoid_gate * up_act).astype(jnp.bfloat16)
    output = jnp.dot(hidden, down_mat, preferred_element_type=jnp.float32).astype(jnp.bfloat16)
    return (output, gate_act, up_act)


def expert_backward(incoming, gate_act, up_act, gate_mat, up_mat, down_mat):
    against = (((1,), (1,)), ((), ()))
    hidden_grad = lax.dot_general(incoming, down_mat, against, preferred_element_type=jnp.float32)
    sigmoid_gate = jax.nn.sigmoid(gate_act)
    gate_grad = (
        hidden_grad * up_act * sigmoid_gate * (1.0 + gate_act * (1.0 - sigmoid_gate))
    ).astype(jnp.bfloat16)
    up_grad = (hidden_grad * gate_act * sigmoid_gate).astype(jnp.bfloat16)
    summed = lax.dot_general(gate_grad, gate_mat, against, preferred_element_type=jnp.float32)
    summed = summed + lax.dot_general(up_grad, up_mat, against, preferred_element_type=jnp.float32)
    return summed.astype(jnp.bfloat16)


def per_device_slots(
    tokens, out_grad, cluster_ids, routes, route_weights, gate_weight, up_weight, down_weight
):
    model_width = tokens.shape[1]
    cent_rows = routes.shape[0]
    fanout = routes.shape[1]
    experts = lax.axis_size("expert")
    capacity = min(cent_rows, 2 * cent_rows * fanout // experts)
    member = (cluster_ids[:, None] == jnp.arange(cent_rows, dtype=jnp.int32)[None, :]).astype(
        jnp.bfloat16
    )
    counts = jnp.sum(member.astype(jnp.float32), axis=0)
    contract = (((0,), (0,)), ((), ()))
    centroid = (
        lax.dot_general(member, tokens, contract, preferred_element_type=jnp.float32)
        / counts[:, None]
    )
    grad_sum = lax.dot_general(member, out_grad, contract, preferred_element_type=jnp.float32)
    pair_ids = routes.reshape(-1)
    matches = (pair_ids[:, None] == jnp.arange(experts, dtype=jnp.int32)[None, :]).astype(jnp.int32)
    earlier = jnp.cumsum(matches, axis=0) - matches
    position = jnp.sum(earlier * matches, axis=1)
    slot_of = (pair_ids * capacity + position).reshape(cent_rows, fanout)
    slot_range = jnp.arange(experts * capacity, dtype=jnp.int32)
    placing = jnp.any(slot_of[None, :, :] == slot_range[:, None, None], axis=2).astype(jnp.bfloat16)
    send_cent = jnp.dot(placing, centroid.astype(jnp.bfloat16), preferred_element_type=jnp.float32)
    send_cent = send_cent.astype(jnp.bfloat16).reshape(experts, capacity, model_width)
    send_grad = jnp.dot(placing, grad_sum.astype(jnp.bfloat16), preferred_element_type=jnp.float32)
    send_grad = send_grad.astype(jnp.bfloat16).reshape(experts, capacity, model_width)
    gate_mat = gate_weight[0]
    up_mat = up_weight[0]
    down_mat = down_weight[0]
    arrived = lax.all_to_all(send_cent, "expert", split_axis=0, concat_axis=0, tiled=True)
    output, gate_act, up_act = expert_forward(
        arrived.reshape(-1, model_width), gate_mat, up_mat, down_mat
    )
    results = lax.all_to_all(
        output.reshape(experts, capacity, model_width),
        "expert",
        split_axis=0,
        concat_axis=0,
        tiled=True,
    )
    arrived_grad = lax.all_to_all(send_grad, "expert", split_axis=0, concat_axis=0, tiled=True)
    input_grad = expert_backward(
        arrived_grad.reshape(-1, model_width), gate_act, up_act, gate_mat, up_mat, down_mat
    )
    results_grad = lax.all_to_all(
        input_grad.reshape(experts, capacity, model_width),
        "expert",
        split_axis=0,
        concat_axis=0,
        tiled=True,
    )
    returned = results.reshape(-1, model_width)[slot_of]
    returned_grad = results_grad.reshape(-1, model_width)[slot_of]
    combined = jnp.sum(route_weights[:, :, None] * returned.astype(jnp.float32), axis=1)
    centroid_grad = (
        jnp.sum(route_weights[:, :, None] * returned_grad.astype(jnp.float32), axis=1) - grad_sum
    )
    layer_out = tokens.astype(jnp.float32) + jnp.take(combined - centroid, cluster_ids, axis=0)
    token_grad = out_grad.astype(jnp.float32) + jnp.take(
        centroid_grad / counts[:, None], cluster_ids, axis=0
    )
    return (layer_out, token_grad)


def pick(index, options):
    chosen = options[-1]
    for position in range(len(options) - 2, -1, -1):
        chosen = jnp.where(index == position, options[position], chosen)
    return chosen


def place(pieces, lines, like):
    slot = lax.broadcasted_iota(jnp.int32, (lines,) + (1,) * like.ndim, 0)
    stacked = jnp.zeros((lines,) + like.shape, like.dtype)
    for piece, origin in pieces:
        stacked = jnp.where(slot == origin, piece[None], stacked)
    return stacked


def topo_all_gather(shard, experts):
    lines = experts // 4
    me = lax.axis_index("expert")
    line = me // 4
    swap_row = [(j, j ^ 2) for j in range(experts)]
    here = [(shard, line)]
    there = [(lax.ppermute(shard, "expert", swap_row), line)]
    ahead, behind = shard, shard
    for step in range(1, lines):
        ahead = lax.ppermute(
            ahead,
            "expert",
            [(j, j + 4) for j in range(experts) if step - 1 <= j // 4 < lines - 1],
        )
        behind = lax.ppermute(
            behind,
            "expert",
            [(j, j - 4) for j in range(experts) if 1 <= j // 4 <= lines - step],
        )
        here.append((ahead, line - step))
        here.append((behind, line + step))
        ahead_row = [(j, j ^ 2) for j in range(experts) if j // 4 >= step]
        behind_row = [(j, j ^ 2) for j in range(experts) if j // 4 <= lines - 1 - step]
        there.append((lax.ppermute(ahead, "expert", ahead_row), line - step))
        there.append((lax.ppermute(behind, "expert", behind_row), line + step))
    column = place(here, lines, shard)
    across = place(there, lines, shard)
    swap_core = [(j, j ^ 1) for j in range(experts)]
    column_pair = lax.ppermute(column, "expert", swap_core)
    across_pair = lax.ppermute(across, "expert", swap_core)
    in_row = (me // 2) % 2
    on_chip = me % 2
    mine = jnp.stack([pick(in_row, [column, across]), pick(in_row, [across, column])], axis=1)
    pair = jnp.stack(
        [pick(in_row, [column_pair, across_pair]), pick(in_row, [across_pair, column_pair])], axis=1
    )
    full = jnp.stack([pick(on_chip, [mine, pair]), pick(on_chip, [pair, mine])], axis=2)
    return full.reshape((experts * shard.shape[0],) + shard.shape[1:])


def topo_reduce_scatter(blocks, experts):
    lines = experts // 4
    me = lax.axis_index("expert")
    rows = blocks.shape[0] // experts
    cube = blocks.reshape((lines, 2, 2, rows) + blocks.shape[1:])
    on_chip = me % 2
    keep = pick(on_chip, [cube[:, :, 0], cube[:, :, 1]])
    give = pick(on_chip, [cube[:, :, 1], cube[:, :, 0]])
    got = lax.ppermute(give.astype(jnp.bfloat16), "expert", [(j, j ^ 1) for j in range(experts)])
    plane = keep.astype(jnp.float32) + got.astype(jnp.float32)
    in_row = (me // 2) % 2
    keep = pick(in_row, [plane[:, 0], plane[:, 1]])
    give = pick(in_row, [plane[:, 1], plane[:, 0]])
    line = me // 4

    def row_sum(target, senders):
        mine = lax.dynamic_index_in_dim(keep, target, 0, keepdims=False)
        theirs = lax.dynamic_index_in_dim(give, target, 0, keepdims=False)
        pairs = [(j, j ^ 2) for j in range(experts) if senders(j // 4)]
        got = lax.ppermute(theirs.astype(jnp.bfloat16), "expert", pairs)
        return mine + got.astype(jnp.float32)

    ahead = jnp.zeros(keep.shape[1:], jnp.float32)
    behind = jnp.zeros(keep.shape[1:], jnp.float32)
    for step in range(1, lines):
        target = jnp.clip(line + lines - step, 0, lines - 1)
        ahead = ahead + row_sum(target, lambda z, s=step: z <= s - 1)
        ahead = lax.ppermute(
            ahead.astype(jnp.bfloat16),
            "expert",
            [(j, j + 4) for j in range(experts) if j // 4 <= step - 1],
        ).astype(jnp.float32)
        target = jnp.clip(line - lines + step, 0, lines - 1)
        behind = behind + row_sum(target, lambda z, s=step: z >= lines - s)
        behind = lax.ppermute(
            behind.astype(jnp.bfloat16),
            "expert",
            [(j, j - 4) for j in range(experts) if j // 4 >= lines - step],
        ).astype(jnp.float32)
    return row_sum(line, lambda z: True) + ahead + behind


def expert_dense(cent_in, grad_in, gate_mat, up_mat, down_mat):
    against = (((1,), (1,)), ((), ()))
    gate_act = jnp.dot(cent_in, gate_mat, preferred_element_type=jnp.float32)
    up_act = jnp.dot(cent_in, up_mat, preferred_element_type=jnp.float32)
    sigmoid_gate = jax.nn.sigmoid(gate_act)
    hidden = (gate_act * sigmoid_gate * up_act).astype(jnp.bfloat16)
    output = jnp.dot(hidden, down_mat, preferred_element_type=jnp.float32).astype(jnp.bfloat16)
    hidden_grad = lax.dot_general(grad_in, down_mat, against, preferred_element_type=jnp.float32)
    gate_grad = (
        hidden_grad * up_act * sigmoid_gate * (1.0 + gate_act * (1.0 - sigmoid_gate))
    ).astype(jnp.bfloat16)
    up_grad = (hidden_grad * gate_act * sigmoid_gate).astype(jnp.bfloat16)
    summed = lax.dot_general(gate_grad, gate_mat, against, preferred_element_type=jnp.float32)
    summed = summed + lax.dot_general(up_grad, up_mat, against, preferred_element_type=jnp.float32)
    return output, summed.astype(jnp.bfloat16)


def per_device_dense(
    tokens, out_grad, cluster_ids, routes, route_weights, gate_weight, up_weight, down_weight
):
    cent_rows = routes.shape[0]
    me = lax.axis_index("expert")
    member = (cluster_ids[:, None] == jnp.arange(cent_rows, dtype=jnp.int32)[None, :]).astype(
        jnp.bfloat16
    )
    counts = jnp.sum(member.astype(jnp.float32), axis=0)
    contract = (((0,), (0,)), ((), ()))
    centroid = (
        lax.dot_general(member, tokens, contract, preferred_element_type=jnp.float32)
        / counts[:, None]
    )
    grad_sum = lax.dot_general(member, out_grad, contract, preferred_element_type=jnp.float32)
    experts = lax.axis_size("expert")
    model_width = tokens.shape[1]
    picked = routes[:, :, None] == jnp.arange(experts, dtype=jnp.int32)[None, None, :]
    per_expert = jnp.sum(jnp.where(picked, route_weights[:, :, None], 0.0), axis=1)
    weight_hi = per_expert.astype(jnp.bfloat16)
    weight_lo = (per_expert - weight_hi.astype(jnp.float32)).astype(jnp.bfloat16)
    side = jnp.concatenate([weight_hi, weight_lo], axis=1)
    side_width = -(-side.shape[1] // 128) * 128
    side = jnp.pad(side, ((0, 0), (0, side_width - side.shape[1])))
    payload = jnp.concatenate(
        [centroid.astype(jnp.bfloat16), grad_sum.astype(jnp.bfloat16), side], axis=1
    )
    gathered = topo_all_gather(payload, experts)
    cent_all = gathered[:, :model_width]
    grad_all = gathered[:, model_width : 2 * model_width]
    side_all = gathered[:, 2 * model_width : 2 * model_width + 2 * experts].astype(jnp.float32)
    column = jnp.arange(experts, dtype=jnp.int32)[None, :]
    mine = jnp.sum(jnp.where(column == me, side_all[:, :experts] + side_all[:, experts:], 0.0), axis=1)
    output, input_grad = expert_dense(
        cent_all, grad_all, gate_weight[0], up_weight[0], down_weight[0]
    )
    parts = jnp.concatenate(
        [
            (mine[:, None] * output.astype(jnp.float32)).astype(jnp.bfloat16),
            (mine[:, None] * input_grad.astype(jnp.float32)).astype(jnp.bfloat16),
        ],
        axis=1,
    )
    summed = topo_reduce_scatter(parts, experts)
    combined = summed[:, :model_width]
    centroid_grad = summed[:, model_width:] - grad_sum
    layer_out = tokens.astype(jnp.float32) + jnp.take(combined - centroid, cluster_ids, axis=0)
    token_grad = out_grad.astype(jnp.float32) + jnp.take(
        centroid_grad / counts[:, None], cluster_ids, axis=0
    )
    return (layer_out, token_grad)


def per_device(*args):
    routes = args[3]
    cent_rows, fanout = routes.shape
    experts = lax.axis_size("expert")
    capacity = min(cent_rows, 2 * cent_rows * fanout // experts)
    if capacity == cent_rows and experts % 4 == 0:
        return per_device_dense(*args)
    return per_device_slots(*args)


def solution(mesh):
    placed = (
        P(("groups", "expert"), None),
        P(("groups", "expert"), None),
        P(("groups", "expert")),
        P(("groups", "expert"), None),
        P(("groups", "expert"), None),
        P("expert", None, None),
        P("expert", None, None),
        P("expert", None, None),
    )
    return jax.shard_map(
        per_device,
        mesh=mesh,
        in_specs=placed,
        out_specs=(P(("groups", "expert"), None), P(("groups", "expert"), None)),
        check_vma=False,
    )
```

```python
import jax
import jax.numpy as jnp
from jax import lax
from jax.sharding import PartitionSpec as P


def expert_forward(inputs, gate_mat, up_mat, down_mat):
    gate_act = jnp.dot(inputs, gate_mat, preferred_element_type=jnp.float32)
    up_act = jnp.dot(inputs, up_mat, preferred_element_type=jnp.float32)
    sigmoid_gate = jax.nn.sigmoid(gate_act)
    hidden = (gate_act * sigmoid_gate * up_act).astype(jnp.bfloat16)
    output = jnp.dot(hidden, down_mat, preferred_element_type=jnp.float32).astype(jnp.bfloat16)
    return (output, gate_act, up_act)


def expert_backward(incoming, gate_act, up_act, gate_mat, up_mat, down_mat):
    against = (((1,), (1,)), ((), ()))
    hidden_grad = lax.dot_general(incoming, down_mat, against, preferred_element_type=jnp.float32)
    sigmoid_gate = jax.nn.sigmoid(gate_act)
    gate_grad = (
        hidden_grad * up_act * sigmoid_gate * (1.0 + gate_act * (1.0 - sigmoid_gate))
    ).astype(jnp.bfloat16)
    up_grad = (hidden_grad * gate_act * sigmoid_gate).astype(jnp.bfloat16)
    summed = lax.dot_general(gate_grad, gate_mat, against, preferred_element_type=jnp.float32)
    summed = summed + lax.dot_general(up_grad, up_mat, against, preferred_element_type=jnp.float32)
    return summed.astype(jnp.bfloat16)


def per_device_slots(
    tokens, out_grad, cluster_ids, routes, route_weights, gate_weight, up_weight, down_weight
):
    model_width = tokens.shape[1]
    cent_rows = routes.shape[0]
    fanout = routes.shape[1]
    experts = lax.axis_size("expert")
    capacity = min(cent_rows, 2 * cent_rows * fanout // experts)
    member = (cluster_ids[:, None] == jnp.arange(cent_rows, dtype=jnp.int32)[None, :]).astype(
        jnp.bfloat16
    )
    counts = jnp.sum(member.astype(jnp.float32), axis=0)
    contract = (((0,), (0,)), ((), ()))
    centroid = (
        lax.dot_general(member, tokens, contract, preferred_element_type=jnp.float32)
        / counts[:, None]
    )
    grad_sum = lax.dot_general(member, out_grad, contract, preferred_element_type=jnp.float32)
    pair_ids = routes.reshape(-1)
    matches = (pair_ids[:, None] == jnp.arange(experts, dtype=jnp.int32)[None, :]).astype(jnp.int32)
    earlier = jnp.cumsum(matches, axis=0) - matches
    position = jnp.sum(earlier * matches, axis=1)
    slot_of = (pair_ids * capacity + position).reshape(cent_rows, fanout)
    slot_range = jnp.arange(experts * capacity, dtype=jnp.int32)
    placing = jnp.any(slot_of[None, :, :] == slot_range[:, None, None], axis=2).astype(jnp.bfloat16)
    send_cent = jnp.dot(placing, centroid.astype(jnp.bfloat16), preferred_element_type=jnp.float32)
    send_cent = send_cent.astype(jnp.bfloat16).reshape(experts, capacity, model_width)
    send_grad = jnp.dot(placing, grad_sum.astype(jnp.bfloat16), preferred_element_type=jnp.float32)
    send_grad = send_grad.astype(jnp.bfloat16).reshape(experts, capacity, model_width)
    gate_mat = gate_weight[0]
    up_mat = up_weight[0]
    down_mat = down_weight[0]
    arrived = lax.all_to_all(send_cent, "expert", split_axis=0, concat_axis=0, tiled=True)
    output, gate_act, up_act = expert_forward(
        arrived.reshape(-1, model_width), gate_mat, up_mat, down_mat
    )
    results = lax.all_to_all(
        output.reshape(experts, capacity, model_width),
        "expert",
        split_axis=0,
        concat_axis=0,
        tiled=True,
    )
    arrived_grad = lax.all_to_all(send_grad, "expert", split_axis=0, concat_axis=0, tiled=True)
    input_grad = expert_backward(
        arrived_grad.reshape(-1, model_width), gate_act, up_act, gate_mat, up_mat, down_mat
    )
    results_grad = lax.all_to_all(
        input_grad.reshape(experts, capacity, model_width),
        "expert",
        split_axis=0,
        concat_axis=0,
        tiled=True,
    )
    returned = results.reshape(-1, model_width)[slot_of]
    returned_grad = results_grad.reshape(-1, model_width)[slot_of]
    combined = jnp.sum(route_weights[:, :, None] * returned.astype(jnp.float32), axis=1)
    centroid_grad = (
        jnp.sum(route_weights[:, :, None] * returned_grad.astype(jnp.float32), axis=1) - grad_sum
    )
    layer_out = tokens.astype(jnp.float32) + jnp.take(combined - centroid, cluster_ids, axis=0)
    token_grad = out_grad.astype(jnp.float32) + jnp.take(
        centroid_grad / counts[:, None], cluster_ids, axis=0
    )
    return (layer_out, token_grad)


def pick(index, options):
    chosen = options[-1]
    for position in range(len(options) - 2, -1, -1):
        chosen = jnp.where(index == position, options[position], chosen)
    return chosen


def place(pieces, lines, like):
    slot = lax.broadcasted_iota(jnp.int32, (lines,) + (1,) * like.ndim, 0)
    stacked = jnp.zeros((lines,) + like.shape, like.dtype)
    for piece, origin in pieces:
        stacked = jnp.where(slot == origin, piece[None], stacked)
    return stacked


def topo_all_gather(shard, experts):
    lines = experts // 4
    me = lax.axis_index("expert")
    line = me // 4
    swap_row = [(j, j ^ 2) for j in range(experts)]
    here = [(shard, line)]
    there = [(lax.ppermute(shard, "expert", swap_row), line)]
    ahead, behind = shard, shard
    for step in range(1, lines):
        ahead = lax.ppermute(
            ahead,
            "expert",
            [(j, j + 4) for j in range(experts) if step - 1 <= j // 4 < lines - 1],
        )
        behind = lax.ppermute(
            behind,
            "expert",
            [(j, j - 4) for j in range(experts) if 1 <= j // 4 <= lines - step],
        )
        here.append((ahead, line - step))
        here.append((behind, line + step))
        ahead_row = [(j, j ^ 2) for j in range(experts) if j // 4 >= step]
        behind_row = [(j, j ^ 2) for j in range(experts) if j // 4 <= lines - 1 - step]
        there.append((lax.ppermute(ahead, "expert", ahead_row), line - step))
        there.append((lax.ppermute(behind, "expert", behind_row), line + step))
    column = place(here, lines, shard)
    across = place(there, lines, shard)
    swap_core = [(j, j ^ 1) for j in range(experts)]
    column_pair = lax.ppermute(column, "expert", swap_core)
    across_pair = lax.ppermute(across, "expert", swap_core)
    in_row = (me // 2) % 2
    on_chip = me % 2
    mine = jnp.stack([pick(in_row, [column, across]), pick(in_row, [across, column])], axis=1)
    pair = jnp.stack(
        [pick(in_row, [column_pair, across_pair]), pick(in_row, [across_pair, column_pair])], axis=1
    )
    full = jnp.stack([pick(on_chip, [mine, pair]), pick(on_chip, [pair, mine])], axis=2)
    return full.reshape((experts * shard.shape[0],) + shard.shape[1:])


def topo_reduce_scatter(blocks, experts):
    lines = experts // 4
    me = lax.axis_index("expert")
    rows = blocks.shape[0] // experts
    cube = blocks.reshape((lines, 2, 2, rows) + blocks.shape[1:])
    on_chip = me % 2
    keep = pick(on_chip, [cube[:, :, 0], cube[:, :, 1]])
    give = pick(on_chip, [cube[:, :, 1], cube[:, :, 0]])
    got = lax.ppermute(give.astype(jnp.bfloat16), "expert", [(j, j ^ 1) for j in range(experts)])
    plane = keep.astype(jnp.float32) + got.astype(jnp.float32)
    in_row = (me // 2) % 2
    keep = pick(in_row, [plane[:, 0], plane[:, 1]])
    give = pick(in_row, [plane[:, 1], plane[:, 0]])
    line = me // 4

    def row_sum(target, senders):
        mine = lax.dynamic_index_in_dim(keep, target, 0, keepdims=False)
        theirs = lax.dynamic_index_in_dim(give, target, 0, keepdims=False)
        pairs = [(j, j ^ 2) for j in range(experts) if senders(j // 4)]
        got = lax.ppermute(theirs.astype(jnp.bfloat16), "expert", pairs)
        return mine + got.astype(jnp.float32)

    ahead = jnp.zeros(keep.shape[1:], jnp.float32)
    behind = jnp.zeros(keep.shape[1:], jnp.float32)
    for step in range(1, lines):
        target = jnp.clip(line + lines - step, 0, lines - 1)
        ahead = ahead + row_sum(target, lambda z, s=step: z <= s - 1)
        ahead = lax.ppermute(
            ahead.astype(jnp.bfloat16),
            "expert",
            [(j, j + 4) for j in range(experts) if j // 4 <= step - 1],
        ).astype(jnp.float32)
        target = jnp.clip(line - lines + step, 0, lines - 1)
        behind = behind + row_sum(target, lambda z, s=step: z >= lines - s)
        behind = lax.ppermute(
            behind.astype(jnp.bfloat16),
            "expert",
            [(j, j - 4) for j in range(experts) if j // 4 >= lines - step],
        ).astype(jnp.float32)
    return row_sum(line, lambda z: True) + ahead + behind


def expert_dense(cent_in, grad_in, gate_mat, up_mat, down_mat):
    against = (((1,), (1,)), ((), ()))
    gate_act = jnp.dot(cent_in, gate_mat, preferred_element_type=jnp.float32)
    up_act = jnp.dot(cent_in, up_mat, preferred_element_type=jnp.float32)
    sigmoid_gate = jax.nn.sigmoid(gate_act)
    hidden = (gate_act * sigmoid_gate * up_act).astype(jnp.bfloat16)
    output = jnp.dot(hidden, down_mat, preferred_element_type=jnp.float32).astype(jnp.bfloat16)
    hidden_grad = lax.dot_general(grad_in, down_mat, against, preferred_element_type=jnp.float32)
    gate_grad = (
        hidden_grad * up_act * sigmoid_gate * (1.0 + gate_act * (1.0 - sigmoid_gate))
    ).astype(jnp.bfloat16)
    up_grad = (hidden_grad * gate_act * sigmoid_gate).astype(jnp.bfloat16)
    summed = lax.dot_general(gate_grad, gate_mat, against, preferred_element_type=jnp.float32)
    summed = summed + lax.dot_general(up_grad, up_mat, against, preferred_element_type=jnp.float32)
    return output, summed.astype(jnp.bfloat16)


def per_device_dense(
    tokens, out_grad, cluster_ids, routes, route_weights, gate_weight, up_weight, down_weight
):
    cent_rows = routes.shape[0]
    me = lax.axis_index("expert")
    member = (cluster_ids[:, None] == jnp.arange(cent_rows, dtype=jnp.int32)[None, :]).astype(
        jnp.bfloat16
    )
    counts = jnp.sum(member.astype(jnp.float32), axis=0)
    contract = (((0,), (0,)), ((), ()))
    centroid = (
        lax.dot_general(member, tokens, contract, preferred_element_type=jnp.float32)
        / counts[:, None]
    )
    grad_sum = lax.dot_general(member, out_grad, contract, preferred_element_type=jnp.float32)
    experts = lax.axis_size("expert")
    model_width = tokens.shape[1]
    picked = routes[:, :, None] == jnp.arange(experts, dtype=jnp.int32)[None, None, :]
    per_expert = jnp.sum(jnp.where(picked, route_weights[:, :, None], 0.0), axis=1)
    weight_hi = per_expert.astype(jnp.bfloat16)
    weight_lo = (per_expert - weight_hi.astype(jnp.float32)).astype(jnp.bfloat16)
    side = jnp.concatenate([weight_hi, weight_lo], axis=1)
    side_width = -(-side.shape[1] // 128) * 128
    side = jnp.pad(side, ((0, 0), (0, side_width - side.shape[1])))
    payload = jnp.concatenate([centroid.astype(jnp.bfloat16), side], axis=1)
    gathered = topo_all_gather(payload, experts)
    grad_all = topo_all_gather(grad_sum.astype(jnp.bfloat16), experts)
    cent_all = gathered[:, :model_width]
    side_all = gathered[:, model_width : model_width + 2 * experts].astype(jnp.float32)
    column = jnp.arange(experts, dtype=jnp.int32)[None, :]
    mine = jnp.sum(jnp.where(column == me, side_all[:, :experts] + side_all[:, experts:], 0.0), axis=1)
    output, input_grad = expert_dense(
        cent_all, grad_all, gate_weight[0], up_weight[0], down_weight[0]
    )
    weighted_out = (mine[:, None] * output.astype(jnp.float32)).astype(jnp.bfloat16)
    weighted_grad = (mine[:, None] * input_grad.astype(jnp.float32)).astype(jnp.bfloat16)
    combined = topo_reduce_scatter(weighted_out, experts)
    centroid_grad = topo_reduce_scatter(weighted_grad, experts) - grad_sum
    layer_out = tokens.astype(jnp.float32) + jnp.take(combined - centroid, cluster_ids, axis=0)
    token_grad = out_grad.astype(jnp.float32) + jnp.take(
        centroid_grad / counts[:, None], cluster_ids, axis=0
    )
    return (layer_out, token_grad)


def per_device(*args):
    routes = args[3]
    cent_rows, fanout = routes.shape
    experts = lax.axis_size("expert")
    capacity = min(cent_rows, 2 * cent_rows * fanout // experts)
    if capacity == cent_rows and experts % 4 == 0:
        return per_device_dense(*args)
    return per_device_slots(*args)


def solution(mesh):
    placed = (
        P(("groups", "expert"), None),
        P(("groups", "expert"), None),
        P(("groups", "expert")),
        P(("groups", "expert"), None),
        P(("groups", "expert"), None),
        P("expert", None, None),
        P("expert", None, None),
        P("expert", None, None),
    )
    return jax.shard_map(
        per_device,
        mesh=mesh,
        in_specs=placed,
        out_specs=(P(("groups", "expert"), None), P(("groups", "expert"), None)),
        check_vma=False,
    )
```

```python
import jax
import jax.numpy as jnp
from jax import lax
from jax.sharding import PartitionSpec as P


def expert_forward(inputs, gate_mat, up_mat, down_mat):
    gate_act = jnp.dot(inputs, gate_mat, preferred_element_type=jnp.float32)
    up_act = jnp.dot(inputs, up_mat, preferred_element_type=jnp.float32)
    sigmoid_gate = jax.nn.sigmoid(gate_act)
    hidden = (gate_act * sigmoid_gate * up_act).astype(jnp.bfloat16)
    output = jnp.dot(hidden, down_mat, preferred_element_type=jnp.float32).astype(jnp.bfloat16)
    return (output, gate_act, up_act)


def expert_backward(incoming, gate_act, up_act, gate_mat, up_mat, down_mat):
    against = (((1,), (1,)), ((), ()))
    hidden_grad = lax.dot_general(incoming, down_mat, against, preferred_element_type=jnp.float32)
    sigmoid_gate = jax.nn.sigmoid(gate_act)
    gate_grad = (
        hidden_grad * up_act * sigmoid_gate * (1.0 + gate_act * (1.0 - sigmoid_gate))
    ).astype(jnp.bfloat16)
    up_grad = (hidden_grad * gate_act * sigmoid_gate).astype(jnp.bfloat16)
    summed = lax.dot_general(gate_grad, gate_mat, against, preferred_element_type=jnp.float32)
    summed = summed + lax.dot_general(up_grad, up_mat, against, preferred_element_type=jnp.float32)
    return summed.astype(jnp.bfloat16)


def per_device_slots(
    tokens, out_grad, cluster_ids, routes, route_weights, gate_weight, up_weight, down_weight
):
    model_width = tokens.shape[1]
    cent_rows = routes.shape[0]
    fanout = routes.shape[1]
    experts = lax.axis_size("expert")
    capacity = min(cent_rows, 2 * cent_rows * fanout // experts)
    member = (cluster_ids[:, None] == jnp.arange(cent_rows, dtype=jnp.int32)[None, :]).astype(
        jnp.bfloat16
    )
    counts = jnp.sum(member.astype(jnp.float32), axis=0)
    contract = (((0,), (0,)), ((), ()))
    centroid = (
        lax.dot_general(member, tokens, contract, preferred_element_type=jnp.float32)
        / counts[:, None]
    )
    grad_sum = lax.dot_general(member, out_grad, contract, preferred_element_type=jnp.float32)
    pair_ids = routes.reshape(-1)
    matches = (pair_ids[:, None] == jnp.arange(experts, dtype=jnp.int32)[None, :]).astype(jnp.int32)
    earlier = jnp.cumsum(matches, axis=0) - matches
    position = jnp.sum(earlier * matches, axis=1)
    slot_of = (pair_ids * capacity + position).reshape(cent_rows, fanout)
    slot_range = jnp.arange(experts * capacity, dtype=jnp.int32)
    placing = jnp.any(slot_of[None, :, :] == slot_range[:, None, None], axis=2).astype(jnp.bfloat16)
    send_cent = jnp.dot(placing, centroid.astype(jnp.bfloat16), preferred_element_type=jnp.float32)
    send_cent = send_cent.astype(jnp.bfloat16).reshape(experts, capacity, model_width)
    send_grad = jnp.dot(placing, grad_sum.astype(jnp.bfloat16), preferred_element_type=jnp.float32)
    send_grad = send_grad.astype(jnp.bfloat16).reshape(experts, capacity, model_width)
    gate_mat = gate_weight[0]
    up_mat = up_weight[0]
    down_mat = down_weight[0]
    arrived = lax.all_to_all(send_cent, "expert", split_axis=0, concat_axis=0, tiled=True)
    output, gate_act, up_act = expert_forward(
        arrived.reshape(-1, model_width), gate_mat, up_mat, down_mat
    )
    results = lax.all_to_all(
        output.reshape(experts, capacity, model_width),
        "expert",
        split_axis=0,
        concat_axis=0,
        tiled=True,
    )
    arrived_grad = lax.all_to_all(send_grad, "expert", split_axis=0, concat_axis=0, tiled=True)
    input_grad = expert_backward(
        arrived_grad.reshape(-1, model_width), gate_act, up_act, gate_mat, up_mat, down_mat
    )
    results_grad = lax.all_to_all(
        input_grad.reshape(experts, capacity, model_width),
        "expert",
        split_axis=0,
        concat_axis=0,
        tiled=True,
    )
    returned = results.reshape(-1, model_width)[slot_of]
    returned_grad = results_grad.reshape(-1, model_width)[slot_of]
    combined = jnp.sum(route_weights[:, :, None] * returned.astype(jnp.float32), axis=1)
    centroid_grad = (
        jnp.sum(route_weights[:, :, None] * returned_grad.astype(jnp.float32), axis=1) - grad_sum
    )
    layer_out = tokens.astype(jnp.float32) + jnp.take(combined - centroid, cluster_ids, axis=0)
    token_grad = out_grad.astype(jnp.float32) + jnp.take(
        centroid_grad / counts[:, None], cluster_ids, axis=0
    )
    return (layer_out, token_grad)


def pick(index, options):
    chosen = options[-1]
    for position in range(len(options) - 2, -1, -1):
        chosen = jnp.where(index == position, options[position], chosen)
    return chosen


def place(pieces, lines, like):
    slot = lax.broadcasted_iota(jnp.int32, (lines,) + (1,) * like.ndim, 0)
    stacked = jnp.zeros((lines,) + like.shape, like.dtype)
    for piece, origin in pieces:
        stacked = jnp.where(slot == origin, piece[None], stacked)
    return stacked


def topo_all_gather(shard, experts):
    lines = experts // 4
    me = lax.axis_index("expert")
    line = me // 4
    swap_row = [(j, j ^ 2) for j in range(experts)]
    here = [(shard, line)]
    there = [(lax.ppermute(shard, "expert", swap_row), line)]
    ahead, behind = shard, shard
    for step in range(1, lines):
        ahead = lax.ppermute(
            ahead,
            "expert",
            [(j, j + 4) for j in range(experts) if step - 1 <= j // 4 < lines - 1],
        )
        behind = lax.ppermute(
            behind,
            "expert",
            [(j, j - 4) for j in range(experts) if 1 <= j // 4 <= lines - step],
        )
        here.append((ahead, line - step))
        here.append((behind, line + step))
        ahead_row = [(j, j ^ 2) for j in range(experts) if j // 4 >= step]
        behind_row = [(j, j ^ 2) for j in range(experts) if j // 4 <= lines - 1 - step]
        there.append((lax.ppermute(ahead, "expert", ahead_row), line - step))
        there.append((lax.ppermute(behind, "expert", behind_row), line + step))
    column = place(here, lines, shard)
    across = place(there, lines, shard)
    swap_core = [(j, j ^ 1) for j in range(experts)]
    column_pair = lax.ppermute(column, "expert", swap_core)
    across_pair = lax.ppermute(across, "expert", swap_core)
    in_row = (me // 2) % 2
    on_chip = me % 2
    mine = jnp.stack([pick(in_row, [column, across]), pick(in_row, [across, column])], axis=1)
    pair = jnp.stack(
        [pick(in_row, [column_pair, across_pair]), pick(in_row, [across_pair, column_pair])], axis=1
    )
    full = jnp.stack([pick(on_chip, [mine, pair]), pick(on_chip, [pair, mine])], axis=2)
    return full.reshape((experts * shard.shape[0],) + shard.shape[1:])


def topo_reduce_scatter(blocks, experts):
    lines = experts // 4
    me = lax.axis_index("expert")
    rows = blocks.shape[0] // experts
    cube = blocks.reshape((lines, 2, 2, rows) + blocks.shape[1:])
    on_chip = me % 2
    keep = pick(on_chip, [cube[:, :, 0], cube[:, :, 1]])
    give = pick(on_chip, [cube[:, :, 1], cube[:, :, 0]])
    got = lax.ppermute(give.astype(jnp.bfloat16), "expert", [(j, j ^ 1) for j in range(experts)])
    plane = keep.astype(jnp.float32) + got.astype(jnp.float32)
    in_row = (me // 2) % 2
    keep = pick(in_row, [plane[:, 0], plane[:, 1]])
    give = pick(in_row, [plane[:, 1], plane[:, 0]])
    line = me // 4

    def row_sum(target, senders):
        mine = lax.dynamic_index_in_dim(keep, target, 0, keepdims=False)
        theirs = lax.dynamic_index_in_dim(give, target, 0, keepdims=False)
        pairs = [(j, j ^ 2) for j in range(experts) if senders(j // 4)]
        got = lax.ppermute(theirs.astype(jnp.bfloat16), "expert", pairs)
        return mine + got.astype(jnp.float32)

    ahead = jnp.zeros(keep.shape[1:], jnp.float32)
    behind = jnp.zeros(keep.shape[1:], jnp.float32)
    for step in range(1, lines):
        target = jnp.clip(line + lines - step, 0, lines - 1)
        ahead = ahead + row_sum(target, lambda z, s=step: z <= s - 1)
        ahead = lax.ppermute(
            ahead.astype(jnp.bfloat16),
            "expert",
            [(j, j + 4) for j in range(experts) if j // 4 <= step - 1],
        ).astype(jnp.float32)
        target = jnp.clip(line - lines + step, 0, lines - 1)
        behind = behind + row_sum(target, lambda z, s=step: z >= lines - s)
        behind = lax.ppermute(
            behind.astype(jnp.bfloat16),
            "expert",
            [(j, j - 4) for j in range(experts) if j // 4 >= lines - step],
        ).astype(jnp.float32)
    return row_sum(line, lambda z: True) + ahead + behind


def expert_dense(cent_in, grad_in, gate_mat, up_mat, down_mat):
    against = (((1,), (1,)), ((), ()))
    gate_act = jnp.dot(cent_in, gate_mat, preferred_element_type=jnp.float32)
    up_act = jnp.dot(cent_in, up_mat, preferred_element_type=jnp.float32)
    sigmoid_gate = jax.nn.sigmoid(gate_act)
    hidden = (gate_act * sigmoid_gate * up_act).astype(jnp.bfloat16)
    output = jnp.dot(hidden, down_mat, preferred_element_type=jnp.float32).astype(jnp.bfloat16)
    hidden_grad = lax.dot_general(grad_in, down_mat, against, preferred_element_type=jnp.float32)
    gate_grad = (
        hidden_grad * up_act * sigmoid_gate * (1.0 + gate_act * (1.0 - sigmoid_gate))
    ).astype(jnp.bfloat16)
    up_grad = (hidden_grad * gate_act * sigmoid_gate).astype(jnp.bfloat16)
    summed = lax.dot_general(gate_grad, gate_mat, against, preferred_element_type=jnp.float32)
    summed = summed + lax.dot_general(up_grad, up_mat, against, preferred_element_type=jnp.float32)
    return output, summed.astype(jnp.bfloat16)


def per_device_dense(
    tokens, out_grad, cluster_ids, routes, route_weights, gate_weight, up_weight, down_weight
):
    cent_rows = routes.shape[0]
    me = lax.axis_index("expert")
    member = (cluster_ids[:, None] == jnp.arange(cent_rows, dtype=jnp.int32)[None, :]).astype(
        jnp.bfloat16
    )
    counts = jnp.sum(member.astype(jnp.float32), axis=0)
    contract = (((0,), (0,)), ((), ()))
    centroid = (
        lax.dot_general(member, tokens, contract, preferred_element_type=jnp.float32)
        / counts[:, None]
    )
    grad_sum = lax.dot_general(member, out_grad, contract, preferred_element_type=jnp.float32)
    experts = lax.axis_size("expert")
    model_width = tokens.shape[1]
    picked = routes[:, :, None] == jnp.arange(experts, dtype=jnp.int32)[None, None, :]
    per_expert = jnp.sum(jnp.where(picked, route_weights[:, :, None], 0.0), axis=1)
    weight_hi = per_expert.astype(jnp.bfloat16)
    weight_lo = (per_expert - weight_hi.astype(jnp.float32)).astype(jnp.bfloat16)
    side = jnp.concatenate([weight_hi, weight_lo], axis=1)
    side_width = -(-side.shape[1] // 128) * 128
    side = jnp.pad(side, ((0, 0), (0, side_width - side.shape[1])))
    grad_all = lax.all_gather(grad_sum.astype(jnp.bfloat16), "expert", axis=0, tiled=True)
    payload = jnp.concatenate([centroid.astype(jnp.bfloat16), side], axis=1)
    gathered = topo_all_gather(payload, experts)
    cent_all = gathered[:, :model_width]
    side_all = gathered[:, model_width : model_width + 2 * experts].astype(jnp.float32)
    column = jnp.arange(experts, dtype=jnp.int32)[None, :]
    mine = jnp.sum(jnp.where(column == me, side_all[:, :experts] + side_all[:, experts:], 0.0), axis=1)
    output, input_grad = expert_dense(
        cent_all, grad_all, gate_weight[0], up_weight[0], down_weight[0]
    )
    parts = jnp.concatenate(
        [
            (mine[:, None] * output.astype(jnp.float32)).astype(jnp.bfloat16),
            (mine[:, None] * input_grad.astype(jnp.float32)).astype(jnp.bfloat16),
        ],
        axis=1,
    )
    summed = topo_reduce_scatter(parts, experts)
    combined = summed[:, :model_width]
    centroid_grad = summed[:, model_width:] - grad_sum
    layer_out = tokens.astype(jnp.float32) + jnp.take(combined - centroid, cluster_ids, axis=0)
    token_grad = out_grad.astype(jnp.float32) + jnp.take(
        centroid_grad / counts[:, None], cluster_ids, axis=0
    )
    return (layer_out, token_grad)


def per_device(*args):
    routes = args[3]
    cent_rows, fanout = routes.shape
    experts = lax.axis_size("expert")
    capacity = min(cent_rows, 2 * cent_rows * fanout // experts)
    if capacity == cent_rows and experts % 4 == 0:
        return per_device_dense(*args)
    return per_device_slots(*args)


def solution(mesh):
    placed = (
        P(("groups", "expert"), None),
        P(("groups", "expert"), None),
        P(("groups", "expert")),
        P(("groups", "expert"), None),
        P(("groups", "expert"), None),
        P("expert", None, None),
        P("expert", None, None),
        P("expert", None, None),
    )
    return jax.shard_map(
        per_device,
        mesh=mesh,
        in_specs=placed,
        out_specs=(P(("groups", "expert"), None), P(("groups", "expert"), None)),
        check_vma=False,
    )
```

```python
import jax
import jax.numpy as jnp
from jax import lax
from jax.sharding import PartitionSpec as P


def expert_forward(inputs, gate_mat, up_mat, down_mat):
    gate_act = jnp.dot(inputs, gate_mat, preferred_element_type=jnp.float32)
    up_act = jnp.dot(inputs, up_mat, preferred_element_type=jnp.float32)
    sigmoid_gate = jax.nn.sigmoid(gate_act)
    hidden = (gate_act * sigmoid_gate * up_act).astype(jnp.bfloat16)
    output = jnp.dot(hidden, down_mat, preferred_element_type=jnp.float32).astype(jnp.bfloat16)
    return (output, gate_act, up_act)


def expert_backward(incoming, gate_act, up_act, gate_mat, up_mat, down_mat):
    against = (((1,), (1,)), ((), ()))
    hidden_grad = lax.dot_general(incoming, down_mat, against, preferred_element_type=jnp.float32)
    sigmoid_gate = jax.nn.sigmoid(gate_act)
    gate_grad = (
        hidden_grad * up_act * sigmoid_gate * (1.0 + gate_act * (1.0 - sigmoid_gate))
    ).astype(jnp.bfloat16)
    up_grad = (hidden_grad * gate_act * sigmoid_gate).astype(jnp.bfloat16)
    summed = lax.dot_general(gate_grad, gate_mat, against, preferred_element_type=jnp.float32)
    summed = summed + lax.dot_general(up_grad, up_mat, against, preferred_element_type=jnp.float32)
    return summed.astype(jnp.bfloat16)


def per_device_slots(
    tokens, out_grad, cluster_ids, routes, route_weights, gate_weight, up_weight, down_weight
):
    model_width = tokens.shape[1]
    cent_rows = routes.shape[0]
    fanout = routes.shape[1]
    experts = lax.axis_size("expert")
    capacity = min(cent_rows, 2 * cent_rows * fanout // experts)
    member = (cluster_ids[:, None] == jnp.arange(cent_rows, dtype=jnp.int32)[None, :]).astype(
        jnp.bfloat16
    )
    counts = jnp.sum(member.astype(jnp.float32), axis=0)
    contract = (((0,), (0,)), ((), ()))
    centroid = (
        lax.dot_general(member, tokens, contract, preferred_element_type=jnp.float32)
        / counts[:, None]
    )
    grad_sum = lax.dot_general(member, out_grad, contract, preferred_element_type=jnp.float32)
    pair_ids = routes.reshape(-1)
    matches = (pair_ids[:, None] == jnp.arange(experts, dtype=jnp.int32)[None, :]).astype(jnp.int32)
    earlier = jnp.cumsum(matches, axis=0) - matches
    position = jnp.sum(earlier * matches, axis=1)
    slot_of = (pair_ids * capacity + position).reshape(cent_rows, fanout)
    slot_range = jnp.arange(experts * capacity, dtype=jnp.int32)
    placing = jnp.any(slot_of[None, :, :] == slot_range[:, None, None], axis=2).astype(jnp.bfloat16)
    send_cent = jnp.dot(placing, centroid.astype(jnp.bfloat16), preferred_element_type=jnp.float32)
    send_cent = send_cent.astype(jnp.bfloat16).reshape(experts, capacity, model_width)
    send_grad = jnp.dot(placing, grad_sum.astype(jnp.bfloat16), preferred_element_type=jnp.float32)
    send_grad = send_grad.astype(jnp.bfloat16).reshape(experts, capacity, model_width)
    gate_mat = gate_weight[0]
    up_mat = up_weight[0]
    down_mat = down_weight[0]
    arrived = lax.all_to_all(send_cent, "expert", split_axis=0, concat_axis=0, tiled=True)
    output, gate_act, up_act = expert_forward(
        arrived.reshape(-1, model_width), gate_mat, up_mat, down_mat
    )
    results = lax.all_to_all(
        output.reshape(experts, capacity, model_width),
        "expert",
        split_axis=0,
        concat_axis=0,
        tiled=True,
    )
    arrived_grad = lax.all_to_all(send_grad, "expert", split_axis=0, concat_axis=0, tiled=True)
    input_grad = expert_backward(
        arrived_grad.reshape(-1, model_width), gate_act, up_act, gate_mat, up_mat, down_mat
    )
    results_grad = lax.all_to_all(
        input_grad.reshape(experts, capacity, model_width),
        "expert",
        split_axis=0,
        concat_axis=0,
        tiled=True,
    )
    returned = results.reshape(-1, model_width)[slot_of]
    returned_grad = results_grad.reshape(-1, model_width)[slot_of]
    combined = jnp.sum(route_weights[:, :, None] * returned.astype(jnp.float32), axis=1)
    centroid_grad = (
        jnp.sum(route_weights[:, :, None] * returned_grad.astype(jnp.float32), axis=1) - grad_sum
    )
    layer_out = tokens.astype(jnp.float32) + jnp.take(combined - centroid, cluster_ids, axis=0)
    token_grad = out_grad.astype(jnp.float32) + jnp.take(
        centroid_grad / counts[:, None], cluster_ids, axis=0
    )
    return (layer_out, token_grad)


def pick(index, options):
    chosen = options[-1]
    for position in range(len(options) - 2, -1, -1):
        chosen = jnp.where(index == position, options[position], chosen)
    return chosen


def place(pieces, lines, like):
    slot = lax.broadcasted_iota(jnp.int32, (lines,) + (1,) * like.ndim, 0)
    stacked = jnp.zeros((lines,) + like.shape, like.dtype)
    for piece, origin in pieces:
        stacked = jnp.where(slot == origin, piece[None], stacked)
    return stacked


def topo_all_gather(shard, experts):
    lines = experts // 4
    me = lax.axis_index("expert")
    line = me // 4
    swap_row = [(j, j ^ 2) for j in range(experts)]
    here = [(shard, line)]
    there = [(lax.ppermute(shard, "expert", swap_row), line)]
    ahead, behind = shard, shard
    for step in range(1, lines):
        ahead = lax.ppermute(
            ahead,
            "expert",
            [(j, j + 4) for j in range(experts) if step - 1 <= j // 4 < lines - 1],
        )
        behind = lax.ppermute(
            behind,
            "expert",
            [(j, j - 4) for j in range(experts) if 1 <= j // 4 <= lines - step],
        )
        here.append((ahead, line - step))
        here.append((behind, line + step))
        ahead_row = [(j, j ^ 2) for j in range(experts) if j // 4 >= step]
        behind_row = [(j, j ^ 2) for j in range(experts) if j // 4 <= lines - 1 - step]
        there.append((lax.ppermute(ahead, "expert", ahead_row), line - step))
        there.append((lax.ppermute(behind, "expert", behind_row), line + step))
    column = place(here, lines, shard)
    across = place(there, lines, shard)
    in_row = (me // 2) % 2
    mine = jnp.stack([pick(in_row, [column, across]), pick(in_row, [across, column])], axis=1)
    return mine.reshape((lines * 2 * shard.shape[0],) + shard.shape[1:])


def topo_reduce_scatter(blocks, experts):
    lines = experts // 4
    me = lax.axis_index("expert")
    rows = blocks.shape[0] // (2 * lines)
    plane = blocks.reshape((lines, 2, rows) + blocks.shape[1:])
    in_row = (me // 2) % 2
    keep = pick(in_row, [plane[:, 0], plane[:, 1]])
    give = pick(in_row, [plane[:, 1], plane[:, 0]])
    line = me // 4

    def row_sum(target, senders):
        mine = lax.dynamic_index_in_dim(keep, target, 0, keepdims=False)
        theirs = lax.dynamic_index_in_dim(give, target, 0, keepdims=False)
        pairs = [(j, j ^ 2) for j in range(experts) if senders(j // 4)]
        got = lax.ppermute(theirs.astype(jnp.bfloat16), "expert", pairs)
        return mine + got.astype(jnp.float32)

    ahead = jnp.zeros(keep.shape[1:], jnp.float32)
    behind = jnp.zeros(keep.shape[1:], jnp.float32)
    for step in range(1, lines):
        target = jnp.clip(line + lines - step, 0, lines - 1)
        ahead = ahead + row_sum(target, lambda z, s=step: z <= s - 1)
        ahead = lax.ppermute(
            ahead.astype(jnp.bfloat16),
            "expert",
            [(j, j + 4) for j in range(experts) if j // 4 <= step - 1],
        ).astype(jnp.float32)
        target = jnp.clip(line - lines + step, 0, lines - 1)
        behind = behind + row_sum(target, lambda z, s=step: z >= lines - s)
        behind = lax.ppermute(
            behind.astype(jnp.bfloat16),
            "expert",
            [(j, j - 4) for j in range(experts) if j // 4 >= lines - step],
        ).astype(jnp.float32)
    return row_sum(line, lambda z: True) + ahead + behind


def expert_dense(cent_in, grad_in, gate_mat, up_mat, down_mat):
    against = (((1,), (1,)), ((), ()))
    gate_act = jnp.dot(cent_in, gate_mat, preferred_element_type=jnp.float32)
    up_act = jnp.dot(cent_in, up_mat, preferred_element_type=jnp.float32)
    sigmoid_gate = jax.nn.sigmoid(gate_act)
    hidden = (gate_act * sigmoid_gate * up_act).astype(jnp.bfloat16)
    output = jnp.dot(hidden, down_mat, preferred_element_type=jnp.float32).astype(jnp.bfloat16)
    hidden_grad = lax.dot_general(grad_in, down_mat, against, preferred_element_type=jnp.float32)
    gate_grad = (
        hidden_grad * up_act * sigmoid_gate * (1.0 + gate_act * (1.0 - sigmoid_gate))
    ).astype(jnp.bfloat16)
    up_grad = (hidden_grad * gate_act * sigmoid_gate).astype(jnp.bfloat16)
    summed = lax.dot_general(gate_grad, gate_mat, against, preferred_element_type=jnp.float32)
    summed = summed + lax.dot_general(up_grad, up_mat, against, preferred_element_type=jnp.float32)
    return output, summed.astype(jnp.bfloat16)


def per_device_dense(
    tokens, out_grad, cluster_ids, routes, route_weights, gate_weight, up_weight, down_weight
):
    cent_rows = routes.shape[0]
    me = lax.axis_index("expert")
    member = (cluster_ids[:, None] == jnp.arange(cent_rows, dtype=jnp.int32)[None, :]).astype(
        jnp.bfloat16
    )
    counts = jnp.sum(member.astype(jnp.float32), axis=0)
    contract = (((0,), (0,)), ((), ()))
    centroid = (
        lax.dot_general(member, tokens, contract, preferred_element_type=jnp.float32)
        / counts[:, None]
    )
    grad_sum = lax.dot_general(member, out_grad, contract, preferred_element_type=jnp.float32)
    experts = lax.axis_size("expert")
    model_width = tokens.shape[1]
    picked = routes[:, :, None] == jnp.arange(experts, dtype=jnp.int32)[None, None, :]
    per_expert = jnp.sum(jnp.where(picked, route_weights[:, :, None], 0.0), axis=1)
    weight_hi = per_expert.astype(jnp.bfloat16)
    weight_lo = (per_expert - weight_hi.astype(jnp.float32)).astype(jnp.bfloat16)
    side = jnp.concatenate([weight_hi, weight_lo], axis=1)
    side_width = -(-side.shape[1] // 128) * 128
    side = jnp.pad(side, ((0, 0), (0, side_width - side.shape[1])))
    payload = jnp.concatenate(
        [centroid.astype(jnp.bfloat16), grad_sum.astype(jnp.bfloat16), side], axis=1
    )
    gathered = topo_all_gather(payload, experts)
    cent_all = gathered[:, :model_width]
    grad_all = gathered[:, model_width : 2 * model_width]
    side_all = gathered[:, 2 * model_width : 2 * model_width + 2 * experts].astype(jnp.float32)
    column = jnp.arange(experts, dtype=jnp.int32)[None, :]
    summed_side = side_all[:, :experts] + side_all[:, experts:]
    mine = jnp.sum(jnp.where(column == me, summed_side, 0.0), axis=1)
    other = jnp.sum(jnp.where(column == (me ^ 1), summed_side, 0.0), axis=1)
    swap_core = [(j, j ^ 1) for j in range(experts)]
    gate_mat, up_mat, down_mat = gate_weight[0], up_weight[0], down_weight[0]
    gate_pair = lax.ppermute(gate_mat, "expert", swap_core)
    up_pair = lax.ppermute(up_mat, "expert", swap_core)
    down_pair = lax.ppermute(down_mat, "expert", swap_core)
    output, input_grad = expert_dense(cent_all, grad_all, gate_mat, up_mat, down_mat)
    output_pair, input_grad_pair = expert_dense(cent_all, grad_all, gate_pair, up_pair, down_pair)
    weighted_out = mine[:, None] * output.astype(jnp.float32) + other[:, None] * output_pair.astype(
        jnp.float32
    )
    weighted_grad = mine[:, None] * input_grad.astype(jnp.float32) + other[
        :, None
    ] * input_grad_pair.astype(jnp.float32)
    summed = topo_reduce_scatter(jnp.concatenate([weighted_out, weighted_grad], axis=1), experts)
    combined = summed[:, :model_width]
    centroid_grad = summed[:, model_width:] - grad_sum
    layer_out = tokens.astype(jnp.float32) + jnp.take(combined - centroid, cluster_ids, axis=0)
    token_grad = out_grad.astype(jnp.float32) + jnp.take(
        centroid_grad / counts[:, None], cluster_ids, axis=0
    )
    return (layer_out, token_grad)


def per_device(*args):
    routes = args[3]
    cent_rows, fanout = routes.shape
    experts = lax.axis_size("expert")
    capacity = min(cent_rows, 2 * cent_rows * fanout // experts)
    if capacity == cent_rows and experts % 4 == 0:
        return per_device_dense(*args)
    return per_device_slots(*args)


def solution(mesh):
    placed = (
        P(("groups", "expert"), None),
        P(("groups", "expert"), None),
        P(("groups", "expert")),
        P(("groups", "expert"), None),
        P(("groups", "expert"), None),
        P("expert", None, None),
        P("expert", None, None),
        P("expert", None, None),
    )
    return jax.shard_map(
        per_device,
        mesh=mesh,
        in_specs=placed,
        out_specs=(P(("groups", "expert"), None), P(("groups", "expert"), None)),
        check_vma=False,
    )
```

```python
import jax
import jax.numpy as jnp
from jax import lax
from jax.sharding import PartitionSpec as P


def expert_forward(inputs, gate_mat, up_mat, down_mat):
    gate_act = jnp.dot(inputs, gate_mat, preferred_element_type=jnp.float32)
    up_act = jnp.dot(inputs, up_mat, preferred_element_type=jnp.float32)
    sigmoid_gate = jax.nn.sigmoid(gate_act)
    hidden = (gate_act * sigmoid_gate * up_act).astype(jnp.bfloat16)
    output = jnp.dot(hidden, down_mat, preferred_element_type=jnp.float32).astype(jnp.bfloat16)
    return (output, gate_act, up_act)


def expert_backward(incoming, gate_act, up_act, gate_mat, up_mat, down_mat):
    against = (((1,), (1,)), ((), ()))
    hidden_grad = lax.dot_general(incoming, down_mat, against, preferred_element_type=jnp.float32)
    sigmoid_gate = jax.nn.sigmoid(gate_act)
    gate_grad = (
        hidden_grad * up_act * sigmoid_gate * (1.0 + gate_act * (1.0 - sigmoid_gate))
    ).astype(jnp.bfloat16)
    up_grad = (hidden_grad * gate_act * sigmoid_gate).astype(jnp.bfloat16)
    summed = lax.dot_general(gate_grad, gate_mat, against, preferred_element_type=jnp.float32)
    summed = summed + lax.dot_general(up_grad, up_mat, against, preferred_element_type=jnp.float32)
    return summed.astype(jnp.bfloat16)


def per_device_slots(
    tokens, out_grad, cluster_ids, routes, route_weights, gate_weight, up_weight, down_weight
):
    model_width = tokens.shape[1]
    cent_rows = routes.shape[0]
    fanout = routes.shape[1]
    experts = lax.axis_size("expert")
    capacity = min(cent_rows, 2 * cent_rows * fanout // experts)
    member = (cluster_ids[:, None] == jnp.arange(cent_rows, dtype=jnp.int32)[None, :]).astype(
        jnp.bfloat16
    )
    counts = jnp.sum(member.astype(jnp.float32), axis=0)
    contract = (((0,), (0,)), ((), ()))
    centroid = (
        lax.dot_general(member, tokens, contract, preferred_element_type=jnp.float32)
        / counts[:, None]
    )
    grad_sum = lax.dot_general(member, out_grad, contract, preferred_element_type=jnp.float32)
    pair_ids = routes.reshape(-1)
    matches = (pair_ids[:, None] == jnp.arange(experts, dtype=jnp.int32)[None, :]).astype(jnp.int32)
    earlier = jnp.cumsum(matches, axis=0) - matches
    position = jnp.sum(earlier * matches, axis=1)
    slot_of = (pair_ids * capacity + position).reshape(cent_rows, fanout)
    slot_range = jnp.arange(experts * capacity, dtype=jnp.int32)
    placing = jnp.any(slot_of[None, :, :] == slot_range[:, None, None], axis=2).astype(jnp.bfloat16)
    send_cent = jnp.dot(placing, centroid.astype(jnp.bfloat16), preferred_element_type=jnp.float32)
    send_cent = send_cent.astype(jnp.bfloat16).reshape(experts, capacity, model_width)
    send_grad = jnp.dot(placing, grad_sum.astype(jnp.bfloat16), preferred_element_type=jnp.float32)
    send_grad = send_grad.astype(jnp.bfloat16).reshape(experts, capacity, model_width)
    gate_mat = gate_weight[0]
    up_mat = up_weight[0]
    down_mat = down_weight[0]
    arrived = lax.all_to_all(send_cent, "expert", split_axis=0, concat_axis=0, tiled=True)
    output, gate_act, up_act = expert_forward(
        arrived.reshape(-1, model_width), gate_mat, up_mat, down_mat
    )
    results = lax.all_to_all(
        output.reshape(experts, capacity, model_width),
        "expert",
        split_axis=0,
        concat_axis=0,
        tiled=True,
    )
    arrived_grad = lax.all_to_all(send_grad, "expert", split_axis=0, concat_axis=0, tiled=True)
    input_grad = expert_backward(
        arrived_grad.reshape(-1, model_width), gate_act, up_act, gate_mat, up_mat, down_mat
    )
    results_grad = lax.all_to_all(
        input_grad.reshape(experts, capacity, model_width),
        "expert",
        split_axis=0,
        concat_axis=0,
        tiled=True,
    )
    returned = results.reshape(-1, model_width)[slot_of]
    returned_grad = results_grad.reshape(-1, model_width)[slot_of]
    combined = jnp.sum(route_weights[:, :, None] * returned.astype(jnp.float32), axis=1)
    centroid_grad = (
        jnp.sum(route_weights[:, :, None] * returned_grad.astype(jnp.float32), axis=1) - grad_sum
    )
    layer_out = tokens.astype(jnp.float32) + jnp.take(combined - centroid, cluster_ids, axis=0)
    token_grad = out_grad.astype(jnp.float32) + jnp.take(
        centroid_grad / counts[:, None], cluster_ids, axis=0
    )
    return (layer_out, token_grad)


def pick(index, options):
    chosen = options[-1]
    for position in range(len(options) - 2, -1, -1):
        chosen = jnp.where(index == position, options[position], chosen)
    return chosen


def place(pieces, lines, like):
    slot = lax.broadcasted_iota(jnp.int32, (lines,) + (1,) * like.ndim, 0)
    stacked = jnp.zeros((lines,) + like.shape, like.dtype)
    for piece, origin in pieces:
        stacked = jnp.where(slot == origin, piece[None], stacked)
    return stacked


def topo_all_gather(shard, experts):
    lines = experts // 4
    me = lax.axis_index("expert")
    line = me // 4
    swap_row = [(j, j ^ 2) for j in range(experts)]
    here = [(shard, line)]
    there = [(lax.ppermute(shard, "expert", swap_row), line)]
    ahead, behind = shard, shard
    for step in range(1, lines):
        ahead = lax.ppermute(
            ahead,
            "expert",
            [(j, j + 4) for j in range(experts) if step - 1 <= j // 4 < lines - 1],
        )
        behind = lax.ppermute(
            behind,
            "expert",
            [(j, j - 4) for j in range(experts) if 1 <= j // 4 <= lines - step],
        )
        here.append((ahead, line - step))
        here.append((behind, line + step))
        both = lax.ppermute(jnp.stack([ahead, behind]), "expert", swap_row)
        there.append((both[0], line - step))
        there.append((both[1], line + step))
    column = place(here, lines, shard)
    across = place(there, lines, shard)
    in_row = (me // 2) % 2
    mine = jnp.stack([pick(in_row, [column, across]), pick(in_row, [across, column])], axis=1)
    return mine.reshape((lines * 2 * shard.shape[0],) + shard.shape[1:])


def topo_reduce_scatter(blocks, experts):
    lines = experts // 4
    me = lax.axis_index("expert")
    rows = blocks.shape[0] // (2 * lines)
    plane = blocks.reshape((lines, 2, rows) + blocks.shape[1:])
    in_row = (me // 2) % 2
    keep = pick(in_row, [plane[:, 0], plane[:, 1]])
    give = pick(in_row, [plane[:, 1], plane[:, 0]])
    line = me // 4

    def row_sums(targets):
        mine = [lax.dynamic_index_in_dim(keep, t, 0, keepdims=False) for t in targets]
        theirs = jnp.stack([lax.dynamic_index_in_dim(give, t, 0, keepdims=False) for t in targets])
        pairs = [(j, j ^ 2) for j in range(experts)]
        got = lax.ppermute(theirs.astype(jnp.bfloat16), "expert", pairs).astype(jnp.float32)
        return [m + got[i] for i, m in enumerate(mine)]

    ahead = jnp.zeros(keep.shape[1:], jnp.float32)
    behind = jnp.zeros(keep.shape[1:], jnp.float32)
    for step in range(1, lines):
        ahead_target = jnp.clip(line + lines - step, 0, lines - 1)
        behind_target = jnp.clip(line - lines + step, 0, lines - 1)
        ahead_part, behind_part = row_sums([ahead_target, behind_target])
        ahead = lax.ppermute(
            (ahead + ahead_part).astype(jnp.bfloat16),
            "expert",
            [(j, j + 4) for j in range(experts) if j // 4 <= step - 1],
        ).astype(jnp.float32)
        behind = lax.ppermute(
            (behind + behind_part).astype(jnp.bfloat16),
            "expert",
            [(j, j - 4) for j in range(experts) if j // 4 >= lines - step],
        ).astype(jnp.float32)
    return row_sums([line])[0] + ahead + behind


def expert_dense(cent_in, grad_in, gate_mat, up_mat, down_mat):
    against = (((1,), (1,)), ((), ()))
    gate_act = jnp.dot(cent_in, gate_mat, preferred_element_type=jnp.float32)
    up_act = jnp.dot(cent_in, up_mat, preferred_element_type=jnp.float32)
    sigmoid_gate = jax.nn.sigmoid(gate_act)
    hidden = (gate_act * sigmoid_gate * up_act).astype(jnp.bfloat16)
    output = jnp.dot(hidden, down_mat, preferred_element_type=jnp.float32).astype(jnp.bfloat16)
    hidden_grad = lax.dot_general(grad_in, down_mat, against, preferred_element_type=jnp.float32)
    gate_grad = (
        hidden_grad * up_act * sigmoid_gate * (1.0 + gate_act * (1.0 - sigmoid_gate))
    ).astype(jnp.bfloat16)
    up_grad = (hidden_grad * gate_act * sigmoid_gate).astype(jnp.bfloat16)
    summed = lax.dot_general(gate_grad, gate_mat, against, preferred_element_type=jnp.float32)
    summed = summed + lax.dot_general(up_grad, up_mat, against, preferred_element_type=jnp.float32)
    return output, summed.astype(jnp.bfloat16)


def per_device_dense(
    tokens, out_grad, cluster_ids, routes, route_weights, gate_weight, up_weight, down_weight
):
    cent_rows = routes.shape[0]
    me = lax.axis_index("expert")
    member = (cluster_ids[:, None] == jnp.arange(cent_rows, dtype=jnp.int32)[None, :]).astype(
        jnp.bfloat16
    )
    counts = jnp.sum(member.astype(jnp.float32), axis=0)
    contract = (((0,), (0,)), ((), ()))
    centroid = (
        lax.dot_general(member, tokens, contract, preferred_element_type=jnp.float32)
        / counts[:, None]
    )
    grad_sum = lax.dot_general(member, out_grad, contract, preferred_element_type=jnp.float32)
    experts = lax.axis_size("expert")
    model_width = tokens.shape[1]
    picked = routes[:, :, None] == jnp.arange(experts, dtype=jnp.int32)[None, None, :]
    per_expert = jnp.sum(jnp.where(picked, route_weights[:, :, None], 0.0), axis=1)
    weight_hi = per_expert.astype(jnp.bfloat16)
    weight_lo = (per_expert - weight_hi.astype(jnp.float32)).astype(jnp.bfloat16)
    side = jnp.concatenate([weight_hi, weight_lo], axis=1)
    side_width = -(-side.shape[1] // 128) * 128
    side = jnp.pad(side, ((0, 0), (0, side_width - side.shape[1])))
    payload = jnp.concatenate(
        [centroid.astype(jnp.bfloat16), grad_sum.astype(jnp.bfloat16), side], axis=1
    )
    gathered = topo_all_gather(payload, experts)
    cent_all = gathered[:, :model_width]
    grad_all = gathered[:, model_width : 2 * model_width]
    side_all = gathered[:, 2 * model_width : 2 * model_width + 2 * experts].astype(jnp.float32)
    column = jnp.arange(experts, dtype=jnp.int32)[None, :]
    summed_side = side_all[:, :experts] + side_all[:, experts:]
    mine = jnp.sum(jnp.where(column == me, summed_side, 0.0), axis=1)
    other = jnp.sum(jnp.where(column == (me ^ 1), summed_side, 0.0), axis=1)
    swap_core = [(j, j ^ 1) for j in range(experts)]
    gate_mat, up_mat, down_mat = gate_weight[0], up_weight[0], down_weight[0]
    gate_pair = lax.ppermute(gate_mat, "expert", swap_core)
    up_pair = lax.ppermute(up_mat, "expert", swap_core)
    down_pair = lax.ppermute(down_mat, "expert", swap_core)
    output, input_grad = expert_dense(cent_all, grad_all, gate_mat, up_mat, down_mat)
    output_pair, input_grad_pair = expert_dense(cent_all, grad_all, gate_pair, up_pair, down_pair)
    weighted_out = mine[:, None] * output.astype(jnp.float32) + other[:, None] * output_pair.astype(
        jnp.float32
    )
    weighted_grad = mine[:, None] * input_grad.astype(jnp.float32) + other[
        :, None
    ] * input_grad_pair.astype(jnp.float32)
    summed = topo_reduce_scatter(jnp.concatenate([weighted_out, weighted_grad], axis=1), experts)
    combined = summed[:, :model_width]
    centroid_grad = summed[:, model_width:] - grad_sum
    layer_out = tokens.astype(jnp.float32) + jnp.take(combined - centroid, cluster_ids, axis=0)
    token_grad = out_grad.astype(jnp.float32) + jnp.take(
        centroid_grad / counts[:, None], cluster_ids, axis=0
    )
    return (layer_out, token_grad)


def per_device(*args):
    routes = args[3]
    cent_rows, fanout = routes.shape
    experts = lax.axis_size("expert")
    capacity = min(cent_rows, 2 * cent_rows * fanout // experts)
    if capacity == cent_rows and experts % 4 == 0:
        return per_device_dense(*args)
    return per_device_slots(*args)


def solution(mesh):
    placed = (
        P(("groups", "expert"), None),
        P(("groups", "expert"), None),
        P(("groups", "expert")),
        P(("groups", "expert"), None),
        P(("groups", "expert"), None),
        P("expert", None, None),
        P("expert", None, None),
        P("expert", None, None),
    )
    return jax.shard_map(
        per_device,
        mesh=mesh,
        in_specs=placed,
        out_specs=(P(("groups", "expert"), None), P(("groups", "expert"), None)),
        check_vma=False,
    )
```

```python
import jax
import jax.numpy as jnp
from jax import lax
from jax.sharding import PartitionSpec as P


def expert_forward(inputs, gate_mat, up_mat, down_mat):
    gate_act = jnp.dot(inputs, gate_mat, preferred_element_type=jnp.float32)
    up_act = jnp.dot(inputs, up_mat, preferred_element_type=jnp.float32)
    sigmoid_gate = jax.nn.sigmoid(gate_act)
    hidden = (gate_act * sigmoid_gate * up_act).astype(jnp.bfloat16)
    output = jnp.dot(hidden, down_mat, preferred_element_type=jnp.float32).astype(jnp.bfloat16)
    return (output, gate_act, up_act)


def expert_backward(incoming, gate_act, up_act, gate_mat, up_mat, down_mat):
    against = (((1,), (1,)), ((), ()))
    hidden_grad = lax.dot_general(incoming, down_mat, against, preferred_element_type=jnp.float32)
    sigmoid_gate = jax.nn.sigmoid(gate_act)
    gate_grad = (
        hidden_grad * up_act * sigmoid_gate * (1.0 + gate_act * (1.0 - sigmoid_gate))
    ).astype(jnp.bfloat16)
    up_grad = (hidden_grad * gate_act * sigmoid_gate).astype(jnp.bfloat16)
    summed = lax.dot_general(gate_grad, gate_mat, against, preferred_element_type=jnp.float32)
    summed = summed + lax.dot_general(up_grad, up_mat, against, preferred_element_type=jnp.float32)
    return summed.astype(jnp.bfloat16)


def per_device_slots(
    tokens, out_grad, cluster_ids, routes, route_weights, gate_weight, up_weight, down_weight
):
    model_width = tokens.shape[1]
    cent_rows = routes.shape[0]
    fanout = routes.shape[1]
    experts = lax.axis_size("expert")
    capacity = min(cent_rows, 2 * cent_rows * fanout // experts)
    member = (cluster_ids[:, None] == jnp.arange(cent_rows, dtype=jnp.int32)[None, :]).astype(
        jnp.bfloat16
    )
    counts = jnp.sum(member.astype(jnp.float32), axis=0)
    contract = (((0,), (0,)), ((), ()))
    centroid = (
        lax.dot_general(member, tokens, contract, preferred_element_type=jnp.float32)
        / counts[:, None]
    )
    grad_sum = lax.dot_general(member, out_grad, contract, preferred_element_type=jnp.float32)
    pair_ids = routes.reshape(-1)
    matches = (pair_ids[:, None] == jnp.arange(experts, dtype=jnp.int32)[None, :]).astype(jnp.int32)
    earlier = jnp.cumsum(matches, axis=0) - matches
    position = jnp.sum(earlier * matches, axis=1)
    slot_of = (pair_ids * capacity + position).reshape(cent_rows, fanout)
    slot_range = jnp.arange(experts * capacity, dtype=jnp.int32)
    placing = jnp.any(slot_of[None, :, :] == slot_range[:, None, None], axis=2).astype(jnp.bfloat16)
    send_cent = jnp.dot(placing, centroid.astype(jnp.bfloat16), preferred_element_type=jnp.float32)
    send_cent = send_cent.astype(jnp.bfloat16).reshape(experts, capacity, model_width)
    send_grad = jnp.dot(placing, grad_sum.astype(jnp.bfloat16), preferred_element_type=jnp.float32)
    send_grad = send_grad.astype(jnp.bfloat16).reshape(experts, capacity, model_width)
    gate_mat = gate_weight[0]
    up_mat = up_weight[0]
    down_mat = down_weight[0]
    arrived = lax.all_to_all(send_cent, "expert", split_axis=0, concat_axis=0, tiled=True)
    output, gate_act, up_act = expert_forward(
        arrived.reshape(-1, model_width), gate_mat, up_mat, down_mat
    )
    results = lax.all_to_all(
        output.reshape(experts, capacity, model_width),
        "expert",
        split_axis=0,
        concat_axis=0,
        tiled=True,
    )
    arrived_grad = lax.all_to_all(send_grad, "expert", split_axis=0, concat_axis=0, tiled=True)
    input_grad = expert_backward(
        arrived_grad.reshape(-1, model_width), gate_act, up_act, gate_mat, up_mat, down_mat
    )
    results_grad = lax.all_to_all(
        input_grad.reshape(experts, capacity, model_width),
        "expert",
        split_axis=0,
        concat_axis=0,
        tiled=True,
    )
    returned = results.reshape(-1, model_width)[slot_of]
    returned_grad = results_grad.reshape(-1, model_width)[slot_of]
    combined = jnp.sum(route_weights[:, :, None] * returned.astype(jnp.float32), axis=1)
    centroid_grad = (
        jnp.sum(route_weights[:, :, None] * returned_grad.astype(jnp.float32), axis=1) - grad_sum
    )
    layer_out = tokens.astype(jnp.float32) + jnp.take(combined - centroid, cluster_ids, axis=0)
    token_grad = out_grad.astype(jnp.float32) + jnp.take(
        centroid_grad / counts[:, None], cluster_ids, axis=0
    )
    return (layer_out, token_grad)


def pick(index, options):
    chosen = options[-1]
    for position in range(len(options) - 2, -1, -1):
        chosen = jnp.where(index == position, options[position], chosen)
    return chosen


def place(pieces, lines, like):
    slot = lax.broadcasted_iota(jnp.int32, (lines,) + (1,) * like.ndim, 0)
    stacked = jnp.zeros((lines,) + like.shape, like.dtype)
    for piece, origin in pieces:
        stacked = jnp.where(slot == origin, piece[None], stacked)
    return stacked


def topo_all_gather(shard, experts):
    lines = experts // 4
    me = lax.axis_index("expert")
    line = me // 4
    swap_row = [(j, j ^ 2) for j in range(experts)]
    here = [(shard, line)]
    there = [(lax.ppermute(shard, "expert", swap_row), line)]
    ahead, behind = shard, shard
    for step in range(1, lines):
        ahead = lax.ppermute(
            ahead,
            "expert",
            [(j, j + 4) for j in range(experts) if step - 1 <= j // 4 < lines - 1],
        )
        behind = lax.ppermute(
            behind,
            "expert",
            [(j, j - 4) for j in range(experts) if 1 <= j // 4 <= lines - step],
        )
        here.append((ahead, line - step))
        here.append((behind, line + step))
        ahead_row = [(j, j ^ 2) for j in range(experts) if j // 4 >= step]
        behind_row = [(j, j ^ 2) for j in range(experts) if j // 4 <= lines - 1 - step]
        there.append((lax.ppermute(ahead, "expert", ahead_row), line - step))
        there.append((lax.ppermute(behind, "expert", behind_row), line + step))
    flat = (lines * shard.shape[0],) + shard.shape[1:]
    return place(here, lines, shard).reshape(flat), place(there, lines, shard).reshape(flat)


def topo_reduce_scatter(own_row, other_row, experts):
    lines = experts // 4
    me = lax.axis_index("expert")
    rows = own_row.shape[0] // lines
    keep = own_row.reshape((lines, rows) + own_row.shape[1:])
    give = other_row.reshape((lines, rows) + other_row.shape[1:])
    line = me // 4

    def row_sum(target, senders):
        mine = lax.dynamic_index_in_dim(keep, target, 0, keepdims=False)
        theirs = lax.dynamic_index_in_dim(give, target, 0, keepdims=False)
        pairs = [(j, j ^ 2) for j in range(experts) if senders(j // 4)]
        got = lax.ppermute(theirs.astype(jnp.bfloat16), "expert", pairs)
        return mine + got.astype(jnp.float32)

    ahead = jnp.zeros(keep.shape[1:], jnp.float32)
    behind = jnp.zeros(keep.shape[1:], jnp.float32)
    for step in range(1, lines):
        target = jnp.clip(line + lines - step, 0, lines - 1)
        ahead = ahead + row_sum(target, lambda z, s=step: z <= s - 1)
        ahead = lax.ppermute(
            ahead.astype(jnp.bfloat16),
            "expert",
            [(j, j + 4) for j in range(experts) if j // 4 <= step - 1],
        ).astype(jnp.float32)
        target = jnp.clip(line - lines + step, 0, lines - 1)
        behind = behind + row_sum(target, lambda z, s=step: z >= lines - s)
        behind = lax.ppermute(
            behind.astype(jnp.bfloat16),
            "expert",
            [(j, j - 4) for j in range(experts) if j // 4 >= lines - step],
        ).astype(jnp.float32)
    return row_sum(line, lambda z: True) + ahead + behind


def expert_dense(cent_in, grad_in, gate_mat, up_mat, down_mat):
    against = (((1,), (1,)), ((), ()))
    gate_act = jnp.dot(cent_in, gate_mat, preferred_element_type=jnp.float32)
    up_act = jnp.dot(cent_in, up_mat, preferred_element_type=jnp.float32)
    sigmoid_gate = jax.nn.sigmoid(gate_act)
    hidden = (gate_act * sigmoid_gate * up_act).astype(jnp.bfloat16)
    output = jnp.dot(hidden, down_mat, preferred_element_type=jnp.float32).astype(jnp.bfloat16)
    hidden_grad = lax.dot_general(grad_in, down_mat, against, preferred_element_type=jnp.float32)
    gate_grad = (
        hidden_grad * up_act * sigmoid_gate * (1.0 + gate_act * (1.0 - sigmoid_gate))
    ).astype(jnp.bfloat16)
    up_grad = (hidden_grad * gate_act * sigmoid_gate).astype(jnp.bfloat16)
    summed = lax.dot_general(gate_grad, gate_mat, against, preferred_element_type=jnp.float32)
    summed = summed + lax.dot_general(up_grad, up_mat, against, preferred_element_type=jnp.float32)
    return output, summed.astype(jnp.bfloat16)


def per_device_dense(
    tokens, out_grad, cluster_ids, routes, route_weights, gate_weight, up_weight, down_weight
):
    cent_rows = routes.shape[0]
    me = lax.axis_index("expert")
    member = (cluster_ids[:, None] == jnp.arange(cent_rows, dtype=jnp.int32)[None, :]).astype(
        jnp.bfloat16
    )
    counts = jnp.sum(member.astype(jnp.float32), axis=0)
    contract = (((0,), (0,)), ((), ()))
    centroid = (
        lax.dot_general(member, tokens, contract, preferred_element_type=jnp.float32)
        / counts[:, None]
    )
    grad_sum = lax.dot_general(member, out_grad, contract, preferred_element_type=jnp.float32)
    experts = lax.axis_size("expert")
    model_width = tokens.shape[1]
    picked = routes[:, :, None] == jnp.arange(experts, dtype=jnp.int32)[None, None, :]
    per_expert = jnp.sum(jnp.where(picked, route_weights[:, :, None], 0.0), axis=1)
    weight_hi = per_expert.astype(jnp.bfloat16)
    weight_lo = (per_expert - weight_hi.astype(jnp.float32)).astype(jnp.bfloat16)
    side = jnp.concatenate([weight_hi, weight_lo], axis=1)
    side_width = -(-side.shape[1] // 128) * 128
    side = jnp.pad(side, ((0, 0), (0, side_width - side.shape[1])))
    payload = jnp.concatenate(
        [centroid.astype(jnp.bfloat16), grad_sum.astype(jnp.bfloat16), side], axis=1
    )
    column_rows, across_rows = topo_all_gather(payload, experts)
    expert_ids = jnp.arange(experts, dtype=jnp.int32)[None, :]
    swap_core = [(j, j ^ 1) for j in range(experts)]
    gate_mat, up_mat, down_mat = gate_weight[0], up_weight[0], down_weight[0]
    gate_pair = lax.ppermute(gate_mat, "expert", swap_core)
    up_pair = lax.ppermute(up_mat, "expert", swap_core)
    down_pair = lax.ppermute(down_mat, "expert", swap_core)

    def contributions(gathered):
        cent_rows_in = gathered[:, :model_width]
        grad_rows_in = gathered[:, model_width : 2 * model_width]
        side_rows = gathered[:, 2 * model_width : 2 * model_width + 2 * experts]
        side_rows = side_rows.astype(jnp.float32)
        summed_side = side_rows[:, :experts] + side_rows[:, experts:]
        mine = jnp.sum(jnp.where(expert_ids == me, summed_side, 0.0), axis=1)[:, None]
        other = jnp.sum(jnp.where(expert_ids == (me ^ 1), summed_side, 0.0), axis=1)[:, None]
        output, input_grad = expert_dense(cent_rows_in, grad_rows_in, gate_mat, up_mat, down_mat)
        output_pair, input_grad_pair = expert_dense(
            cent_rows_in, grad_rows_in, gate_pair, up_pair, down_pair
        )
        weighted_out = mine * output.astype(jnp.float32) + other * output_pair.astype(jnp.float32)
        weighted_grad = mine * input_grad.astype(jnp.float32) + other * input_grad_pair.astype(
            jnp.float32
        )
        return jnp.concatenate([weighted_out, weighted_grad], axis=1)

    own_row = contributions(column_rows)
    other_row = contributions(across_rows)
    summed = topo_reduce_scatter(own_row, other_row, experts)
    combined = summed[:, :model_width]
    centroid_grad = summed[:, model_width:] - grad_sum
    layer_out = tokens.astype(jnp.float32) + jnp.take(combined - centroid, cluster_ids, axis=0)
    token_grad = out_grad.astype(jnp.float32) + jnp.take(
        centroid_grad / counts[:, None], cluster_ids, axis=0
    )
    return (layer_out, token_grad)


def per_device(*args):
    routes = args[3]
    cent_rows, fanout = routes.shape
    experts = lax.axis_size("expert")
    capacity = min(cent_rows, 2 * cent_rows * fanout // experts)
    if capacity == cent_rows and experts % 4 == 0:
        return per_device_dense(*args)
    return per_device_slots(*args)


def solution(mesh):
    placed = (
        P(("groups", "expert"), None),
        P(("groups", "expert"), None),
        P(("groups", "expert")),
        P(("groups", "expert"), None),
        P(("groups", "expert"), None),
        P("expert", None, None),
        P("expert", None, None),
        P("expert", None, None),
    )
    return jax.shard_map(
        per_device,
        mesh=mesh,
        in_specs=placed,
        out_specs=(P(("groups", "expert"), None), P(("groups", "expert"), None)),
        check_vma=False,
    )
```

```python
import jax
import jax.numpy as jnp
from jax import lax
from jax.sharding import PartitionSpec as P


def expert_forward(inputs, gate_mat, up_mat, down_mat):
    gate_act = jnp.dot(inputs, gate_mat, preferred_element_type=jnp.float32)
    up_act = jnp.dot(inputs, up_mat, preferred_element_type=jnp.float32)
    sigmoid_gate = jax.nn.sigmoid(gate_act)
    hidden = (gate_act * sigmoid_gate * up_act).astype(jnp.bfloat16)
    output = jnp.dot(hidden, down_mat, preferred_element_type=jnp.float32).astype(jnp.bfloat16)
    return (output, gate_act, up_act)


def expert_backward(incoming, gate_act, up_act, gate_mat, up_mat, down_mat):
    against = (((1,), (1,)), ((), ()))
    hidden_grad = lax.dot_general(incoming, down_mat, against, preferred_element_type=jnp.float32)
    sigmoid_gate = jax.nn.sigmoid(gate_act)
    gate_grad = (
        hidden_grad * up_act * sigmoid_gate * (1.0 + gate_act * (1.0 - sigmoid_gate))
    ).astype(jnp.bfloat16)
    up_grad = (hidden_grad * gate_act * sigmoid_gate).astype(jnp.bfloat16)
    summed = lax.dot_general(gate_grad, gate_mat, against, preferred_element_type=jnp.float32)
    summed = summed + lax.dot_general(up_grad, up_mat, against, preferred_element_type=jnp.float32)
    return summed.astype(jnp.bfloat16)


def per_device_slots(
    tokens, out_grad, cluster_ids, routes, route_weights, gate_weight, up_weight, down_weight
):
    model_width = tokens.shape[1]
    cent_rows = routes.shape[0]
    fanout = routes.shape[1]
    experts = lax.axis_size("expert")
    capacity = min(cent_rows, 2 * cent_rows * fanout // experts)
    member = (cluster_ids[:, None] == jnp.arange(cent_rows, dtype=jnp.int32)[None, :]).astype(
        jnp.bfloat16
    )
    counts = jnp.sum(member.astype(jnp.float32), axis=0)
    contract = (((0,), (0,)), ((), ()))
    centroid = (
        lax.dot_general(member, tokens, contract, preferred_element_type=jnp.float32)
        / counts[:, None]
    )
    grad_sum = lax.dot_general(member, out_grad, contract, preferred_element_type=jnp.float32)
    pair_ids = routes.reshape(-1)
    matches = (pair_ids[:, None] == jnp.arange(experts, dtype=jnp.int32)[None, :]).astype(jnp.int32)
    earlier = jnp.cumsum(matches, axis=0) - matches
    position = jnp.sum(earlier * matches, axis=1)
    slot_of = (pair_ids * capacity + position).reshape(cent_rows, fanout)
    slot_range = jnp.arange(experts * capacity, dtype=jnp.int32)
    placing = jnp.any(slot_of[None, :, :] == slot_range[:, None, None], axis=2).astype(jnp.bfloat16)
    send_cent = jnp.dot(placing, centroid.astype(jnp.bfloat16), preferred_element_type=jnp.float32)
    send_cent = send_cent.astype(jnp.bfloat16).reshape(experts, capacity, model_width)
    send_grad = jnp.dot(placing, grad_sum.astype(jnp.bfloat16), preferred_element_type=jnp.float32)
    send_grad = send_grad.astype(jnp.bfloat16).reshape(experts, capacity, model_width)
    gate_mat = gate_weight[0]
    up_mat = up_weight[0]
    down_mat = down_weight[0]
    arrived = lax.all_to_all(send_cent, "expert", split_axis=0, concat_axis=0, tiled=True)
    output, gate_act, up_act = expert_forward(
        arrived.reshape(-1, model_width), gate_mat, up_mat, down_mat
    )
    results = lax.all_to_all(
        output.reshape(experts, capacity, model_width),
        "expert",
        split_axis=0,
        concat_axis=0,
        tiled=True,
    )
    arrived_grad = lax.all_to_all(send_grad, "expert", split_axis=0, concat_axis=0, tiled=True)
    input_grad = expert_backward(
        arrived_grad.reshape(-1, model_width), gate_act, up_act, gate_mat, up_mat, down_mat
    )
    results_grad = lax.all_to_all(
        input_grad.reshape(experts, capacity, model_width),
        "expert",
        split_axis=0,
        concat_axis=0,
        tiled=True,
    )
    returned = results.reshape(-1, model_width)[slot_of]
    returned_grad = results_grad.reshape(-1, model_width)[slot_of]
    combined = jnp.sum(route_weights[:, :, None] * returned.astype(jnp.float32), axis=1)
    centroid_grad = (
        jnp.sum(route_weights[:, :, None] * returned_grad.astype(jnp.float32), axis=1) - grad_sum
    )
    layer_out = tokens.astype(jnp.float32) + jnp.take(combined - centroid, cluster_ids, axis=0)
    token_grad = out_grad.astype(jnp.float32) + jnp.take(
        centroid_grad / counts[:, None], cluster_ids, axis=0
    )
    return (layer_out, token_grad)


def pick(index, options):
    chosen = options[-1]
    for position in range(len(options) - 2, -1, -1):
        chosen = jnp.where(index == position, options[position], chosen)
    return chosen


def place(pieces, lines, like):
    slot = lax.broadcasted_iota(jnp.int32, (lines,) + (1,) * like.ndim, 0)
    stacked = jnp.zeros((lines,) + like.shape, like.dtype)
    for piece, origin in pieces:
        stacked = jnp.where(slot == origin, piece[None], stacked)
    return stacked


def topo_all_gather(shard, experts):
    lines = experts // 4
    me = lax.axis_index("expert")
    line = me // 4
    here = [(shard, line)]
    there = [(lax.ppermute(shard, "expert", [(j, j ^ 2) for j in range(experts)]), line)]
    for reach in range(1, lines):
        for shift in (reach, -reach):
            pairs = [(j, j + 4 * shift) for j in range(experts) if 0 <= j // 4 + shift < lines]
            got = lax.ppermute(shard, "expert", pairs)
            here.append((got, line - shift))
            row = [(j, j ^ 2) for j in range(experts) if 0 <= j // 4 - shift < lines]
            there.append((lax.ppermute(got, "expert", row), line - shift))
    flat = (lines * shard.shape[0],) + shard.shape[1:]
    return place(here, lines, shard).reshape(flat), place(there, lines, shard).reshape(flat)


def topo_reduce_scatter(own_row, other_row, experts):
    lines = experts // 4
    me = lax.axis_index("expert")
    rows = own_row.shape[0] // lines
    keep = own_row.reshape((lines, rows) + own_row.shape[1:])
    give = other_row.reshape((lines, rows) + other_row.shape[1:])
    line = me // 4

    def row_sum(target, senders):
        mine = lax.dynamic_index_in_dim(keep, target, 0, keepdims=False)
        theirs = lax.dynamic_index_in_dim(give, target, 0, keepdims=False)
        pairs = [(j, j ^ 2) for j in range(experts) if senders(j // 4)]
        got = lax.ppermute(theirs.astype(jnp.bfloat16), "expert", pairs)
        return mine + got.astype(jnp.float32)

    total = row_sum(line, lambda z: True)
    for reach in range(lines - 1, 0, -1):
        for shift in (reach, -reach):
            target = jnp.clip(line + shift, 0, lines - 1)
            part = row_sum(target, lambda z, s=shift: 0 <= z + s < lines)
            pairs = [(j, j + 4 * shift) for j in range(experts) if 0 <= j // 4 + shift < lines]
            total = total + lax.ppermute(part.astype(jnp.bfloat16), "expert", pairs).astype(
                jnp.float32
            )
    return total


def expert_dense(cent_in, grad_in, gate_mat, up_mat, down_mat):
    against = (((1,), (1,)), ((), ()))
    gate_act = jnp.dot(cent_in, gate_mat, preferred_element_type=jnp.float32)
    up_act = jnp.dot(cent_in, up_mat, preferred_element_type=jnp.float32)
    sigmoid_gate = jax.nn.sigmoid(gate_act)
    hidden = (gate_act * sigmoid_gate * up_act).astype(jnp.bfloat16)
    output = jnp.dot(hidden, down_mat, preferred_element_type=jnp.float32).astype(jnp.bfloat16)
    hidden_grad = lax.dot_general(grad_in, down_mat, against, preferred_element_type=jnp.float32)
    gate_grad = (
        hidden_grad * up_act * sigmoid_gate * (1.0 + gate_act * (1.0 - sigmoid_gate))
    ).astype(jnp.bfloat16)
    up_grad = (hidden_grad * gate_act * sigmoid_gate).astype(jnp.bfloat16)
    summed = lax.dot_general(gate_grad, gate_mat, against, preferred_element_type=jnp.float32)
    summed = summed + lax.dot_general(up_grad, up_mat, against, preferred_element_type=jnp.float32)
    return output, summed.astype(jnp.bfloat16)


def per_device_dense(
    tokens, out_grad, cluster_ids, routes, route_weights, gate_weight, up_weight, down_weight
):
    cent_rows = routes.shape[0]
    me = lax.axis_index("expert")
    member = (cluster_ids[:, None] == jnp.arange(cent_rows, dtype=jnp.int32)[None, :]).astype(
        jnp.bfloat16
    )
    counts = jnp.sum(member.astype(jnp.float32), axis=0)
    contract = (((0,), (0,)), ((), ()))
    centroid = (
        lax.dot_general(member, tokens, contract, preferred_element_type=jnp.float32)
        / counts[:, None]
    )
    grad_sum = lax.dot_general(member, out_grad, contract, preferred_element_type=jnp.float32)
    experts = lax.axis_size("expert")
    model_width = tokens.shape[1]
    picked = routes[:, :, None] == jnp.arange(experts, dtype=jnp.int32)[None, None, :]
    per_expert = jnp.sum(jnp.where(picked, route_weights[:, :, None], 0.0), axis=1)
    weight_hi = per_expert.astype(jnp.bfloat16)
    weight_lo = (per_expert - weight_hi.astype(jnp.float32)).astype(jnp.bfloat16)
    side = jnp.concatenate([weight_hi, weight_lo], axis=1)
    side_width = -(-side.shape[1] // 128) * 128
    side = jnp.pad(side, ((0, 0), (0, side_width - side.shape[1])))
    payload = jnp.concatenate(
        [centroid.astype(jnp.bfloat16), grad_sum.astype(jnp.bfloat16), side], axis=1
    )
    column_rows, across_rows = topo_all_gather(payload, experts)
    expert_ids = jnp.arange(experts, dtype=jnp.int32)[None, :]
    swap_core = [(j, j ^ 1) for j in range(experts)]
    gate_mat, up_mat, down_mat = gate_weight[0], up_weight[0], down_weight[0]
    gate_pair = lax.ppermute(gate_mat, "expert", swap_core)
    up_pair = lax.ppermute(up_mat, "expert", swap_core)
    down_pair = lax.ppermute(down_mat, "expert", swap_core)

    def contributions(gathered):
        cent_rows_in = gathered[:, :model_width]
        grad_rows_in = gathered[:, model_width : 2 * model_width]
        side_rows = gathered[:, 2 * model_width : 2 * model_width + 2 * experts]
        side_rows = side_rows.astype(jnp.float32)
        summed_side = side_rows[:, :experts] + side_rows[:, experts:]
        mine = jnp.sum(jnp.where(expert_ids == me, summed_side, 0.0), axis=1)[:, None]
        other = jnp.sum(jnp.where(expert_ids == (me ^ 1), summed_side, 0.0), axis=1)[:, None]
        output, input_grad = expert_dense(cent_rows_in, grad_rows_in, gate_mat, up_mat, down_mat)
        output_pair, input_grad_pair = expert_dense(
            cent_rows_in, grad_rows_in, gate_pair, up_pair, down_pair
        )
        weighted_out = mine * output.astype(jnp.float32) + other * output_pair.astype(jnp.float32)
        weighted_grad = mine * input_grad.astype(jnp.float32) + other * input_grad_pair.astype(
            jnp.float32
        )
        return jnp.concatenate([weighted_out, weighted_grad], axis=1)

    own_row = contributions(column_rows)
    other_row = contributions(across_rows)
    summed = topo_reduce_scatter(own_row, other_row, experts)
    combined = summed[:, :model_width]
    centroid_grad = summed[:, model_width:] - grad_sum
    layer_out = tokens.astype(jnp.float32) + jnp.take(combined - centroid, cluster_ids, axis=0)
    token_grad = out_grad.astype(jnp.float32) + jnp.take(
        centroid_grad / counts[:, None], cluster_ids, axis=0
    )
    return (layer_out, token_grad)


def per_device(*args):
    routes = args[3]
    cent_rows, fanout = routes.shape
    experts = lax.axis_size("expert")
    capacity = min(cent_rows, 2 * cent_rows * fanout // experts)
    if capacity == cent_rows and experts % 4 == 0:
        return per_device_dense(*args)
    return per_device_slots(*args)


def solution(mesh):
    placed = (
        P(("groups", "expert"), None),
        P(("groups", "expert"), None),
        P(("groups", "expert")),
        P(("groups", "expert"), None),
        P(("groups", "expert"), None),
        P("expert", None, None),
        P("expert", None, None),
        P("expert", None, None),
    )
    return jax.shard_map(
        per_device,
        mesh=mesh,
        in_specs=placed,
        out_specs=(P(("groups", "expert"), None), P(("groups", "expert"), None)),
        check_vma=False,
    )
```

```python
import jax
import jax.numpy as jnp
from jax import lax
from jax.sharding import PartitionSpec as P


def expert_forward(inputs, gate_mat, up_mat, down_mat):
    gate_act = jnp.dot(inputs, gate_mat, preferred_element_type=jnp.float32)
    up_act = jnp.dot(inputs, up_mat, preferred_element_type=jnp.float32)
    sigmoid_gate = jax.nn.sigmoid(gate_act)
    hidden = (gate_act * sigmoid_gate * up_act).astype(jnp.bfloat16)
    output = jnp.dot(hidden, down_mat, preferred_element_type=jnp.float32).astype(jnp.bfloat16)
    return (output, gate_act, up_act)


def expert_backward(incoming, gate_act, up_act, gate_mat, up_mat, down_mat):
    against = (((1,), (1,)), ((), ()))
    hidden_grad = lax.dot_general(incoming, down_mat, against, preferred_element_type=jnp.float32)
    sigmoid_gate = jax.nn.sigmoid(gate_act)
    gate_grad = (
        hidden_grad * up_act * sigmoid_gate * (1.0 + gate_act * (1.0 - sigmoid_gate))
    ).astype(jnp.bfloat16)
    up_grad = (hidden_grad * gate_act * sigmoid_gate).astype(jnp.bfloat16)
    summed = lax.dot_general(gate_grad, gate_mat, against, preferred_element_type=jnp.float32)
    summed = summed + lax.dot_general(up_grad, up_mat, against, preferred_element_type=jnp.float32)
    return summed.astype(jnp.bfloat16)


def per_device_slots(
    tokens, out_grad, cluster_ids, routes, route_weights, gate_weight, up_weight, down_weight
):
    model_width = tokens.shape[1]
    cent_rows = routes.shape[0]
    fanout = routes.shape[1]
    experts = lax.axis_size("expert")
    capacity = min(cent_rows, 2 * cent_rows * fanout // experts)
    member = (cluster_ids[:, None] == jnp.arange(cent_rows, dtype=jnp.int32)[None, :]).astype(
        jnp.bfloat16
    )
    counts = jnp.sum(member.astype(jnp.float32), axis=0)
    contract = (((0,), (0,)), ((), ()))
    centroid = (
        lax.dot_general(member, tokens, contract, preferred_element_type=jnp.float32)
        / counts[:, None]
    )
    grad_sum = lax.dot_general(member, out_grad, contract, preferred_element_type=jnp.float32)
    pair_ids = routes.reshape(-1)
    matches = (pair_ids[:, None] == jnp.arange(experts, dtype=jnp.int32)[None, :]).astype(jnp.int32)
    earlier = jnp.cumsum(matches, axis=0) - matches
    position = jnp.sum(earlier * matches, axis=1)
    slot_of = (pair_ids * capacity + position).reshape(cent_rows, fanout)
    slot_range = jnp.arange(experts * capacity, dtype=jnp.int32)
    placing = jnp.any(slot_of[None, :, :] == slot_range[:, None, None], axis=2).astype(jnp.bfloat16)
    send_cent = jnp.dot(placing, centroid.astype(jnp.bfloat16), preferred_element_type=jnp.float32)
    send_cent = send_cent.astype(jnp.bfloat16).reshape(experts, capacity, model_width)
    send_grad = jnp.dot(placing, grad_sum.astype(jnp.bfloat16), preferred_element_type=jnp.float32)
    send_grad = send_grad.astype(jnp.bfloat16).reshape(experts, capacity, model_width)
    gate_mat = gate_weight[0]
    up_mat = up_weight[0]
    down_mat = down_weight[0]
    arrived = lax.all_to_all(send_cent, "expert", split_axis=0, concat_axis=0, tiled=True)
    output, gate_act, up_act = expert_forward(
        arrived.reshape(-1, model_width), gate_mat, up_mat, down_mat
    )
    results = lax.all_to_all(
        output.reshape(experts, capacity, model_width),
        "expert",
        split_axis=0,
        concat_axis=0,
        tiled=True,
    )
    arrived_grad = lax.all_to_all(send_grad, "expert", split_axis=0, concat_axis=0, tiled=True)
    input_grad = expert_backward(
        arrived_grad.reshape(-1, model_width), gate_act, up_act, gate_mat, up_mat, down_mat
    )
    results_grad = lax.all_to_all(
        input_grad.reshape(experts, capacity, model_width),
        "expert",
        split_axis=0,
        concat_axis=0,
        tiled=True,
    )
    returned = results.reshape(-1, model_width)[slot_of]
    returned_grad = results_grad.reshape(-1, model_width)[slot_of]
    combined = jnp.sum(route_weights[:, :, None] * returned.astype(jnp.float32), axis=1)
    centroid_grad = (
        jnp.sum(route_weights[:, :, None] * returned_grad.astype(jnp.float32), axis=1) - grad_sum
    )
    layer_out = tokens.astype(jnp.float32) + jnp.take(combined - centroid, cluster_ids, axis=0)
    token_grad = out_grad.astype(jnp.float32) + jnp.take(
        centroid_grad / counts[:, None], cluster_ids, axis=0
    )
    return (layer_out, token_grad)


def pick(index, options):
    chosen = options[-1]
    for position in range(len(options) - 2, -1, -1):
        chosen = jnp.where(index == position, options[position], chosen)
    return chosen


def place(pieces, lines, like):
    slot = lax.broadcasted_iota(jnp.int32, (lines,) + (1,) * like.ndim, 0)
    stacked = jnp.zeros((lines,) + like.shape, like.dtype)
    for piece, origin in pieces:
        stacked = jnp.where(slot == origin, piece[None], stacked)
    return stacked


def topo_all_gather(shard, experts):
    lines = experts // 4
    me = lax.axis_index("expert")
    line = me // 4
    swap_row = [(j, j ^ 2) for j in range(experts)]
    here = [(shard, line)]
    there = [(lax.ppermute(shard, "expert", swap_row), line)]
    ahead, behind = shard, shard
    for step in range(1, lines):
        ahead = lax.ppermute(
            ahead,
            "expert",
            [(j, j + 4) for j in range(experts) if step - 1 <= j // 4 < lines - 1],
        )
        behind = lax.ppermute(
            behind,
            "expert",
            [(j, j - 4) for j in range(experts) if 1 <= j // 4 <= lines - step],
        )
        here.append((ahead, line - step))
        here.append((behind, line + step))
        ahead_row = [(j, j ^ 2) for j in range(experts) if j // 4 >= step]
        behind_row = [(j, j ^ 2) for j in range(experts) if j // 4 <= lines - 1 - step]
        there.append((lax.ppermute(ahead, "expert", ahead_row), line - step))
        there.append((lax.ppermute(behind, "expert", behind_row), line + step))
    column = place(here, lines, shard)
    across = place(there, lines, shard)
    in_row = (me // 2) % 2
    mine = jnp.stack([pick(in_row, [column, across]), pick(in_row, [across, column])], axis=1)
    return mine.reshape((lines * 2 * shard.shape[0],) + shard.shape[1:])


def topo_reduce_scatter(blocks, experts):
    lines = experts // 4
    me = lax.axis_index("expert")
    rows = blocks.shape[0] // (2 * lines)
    plane = blocks.reshape((lines, 2, rows) + blocks.shape[1:])
    in_row = (me // 2) % 2
    keep = pick(in_row, [plane[:, 0], plane[:, 1]])
    give = pick(in_row, [plane[:, 1], plane[:, 0]])
    line = me // 4

    def row_sum(target, senders):
        mine = lax.dynamic_index_in_dim(keep, target, 0, keepdims=False)
        theirs = lax.dynamic_index_in_dim(give, target, 0, keepdims=False)
        pairs = [(j, j ^ 2) for j in range(experts) if senders(j // 4)]
        got = lax.ppermute(theirs.astype(jnp.bfloat16), "expert", pairs)
        return mine + got.astype(jnp.float32)

    ahead = jnp.zeros(keep.shape[1:], jnp.float32)
    behind = jnp.zeros(keep.shape[1:], jnp.float32)
    for step in range(1, lines):
        target = jnp.clip(line + lines - step, 0, lines - 1)
        ahead = ahead + row_sum(target, lambda z, s=step: z <= s - 1)
        ahead = lax.ppermute(
            ahead.astype(jnp.bfloat16),
            "expert",
            [(j, j + 4) for j in range(experts) if j // 4 <= step - 1],
        ).astype(jnp.float32)
        target = jnp.clip(line - lines + step, 0, lines - 1)
        behind = behind + row_sum(target, lambda z, s=step: z >= lines - s)
        behind = lax.ppermute(
            behind.astype(jnp.bfloat16),
            "expert",
            [(j, j - 4) for j in range(experts) if j // 4 >= lines - step],
        ).astype(jnp.float32)
    return row_sum(line, lambda z: True) + ahead + behind


def expert_dense(cent_in, grad_in, gate_mat, up_mat, down_mat):
    against = (((1,), (1,)), ((), ()))
    gate_act = jnp.dot(cent_in, gate_mat, preferred_element_type=jnp.float32)
    up_act = jnp.dot(cent_in, up_mat, preferred_element_type=jnp.float32)
    sigmoid_gate = jax.nn.sigmoid(gate_act)
    hidden = (gate_act * sigmoid_gate * up_act).astype(jnp.bfloat16)
    output = jnp.dot(hidden, down_mat, preferred_element_type=jnp.float32).astype(jnp.bfloat16)
    hidden_grad = lax.dot_general(grad_in, down_mat, against, preferred_element_type=jnp.float32)
    gate_grad = (
        hidden_grad * up_act * sigmoid_gate * (1.0 + gate_act * (1.0 - sigmoid_gate))
    ).astype(jnp.bfloat16)
    up_grad = (hidden_grad * gate_act * sigmoid_gate).astype(jnp.bfloat16)
    summed = lax.dot_general(gate_grad, gate_mat, against, preferred_element_type=jnp.float32)
    summed = summed + lax.dot_general(up_grad, up_mat, against, preferred_element_type=jnp.float32)
    return output, summed.astype(jnp.bfloat16)


def per_device_dense(
    tokens, out_grad, cluster_ids, routes, route_weights, gate_weight, up_weight, down_weight
):
    cent_rows = routes.shape[0]
    me = lax.axis_index("expert")
    member = (cluster_ids[:, None] == jnp.arange(cent_rows, dtype=jnp.int32)[None, :]).astype(
        jnp.bfloat16
    )
    counts = jnp.sum(member.astype(jnp.float32), axis=0)
    contract = (((0,), (0,)), ((), ()))
    model_width = tokens.shape[1]
    sums = lax.dot_general(
        member,
        jnp.concatenate([tokens, out_grad], axis=1),
        contract,
        preferred_element_type=jnp.float32,
    )
    centroid = sums[:, :model_width] / counts[:, None]
    grad_sum = sums[:, model_width:]
    experts = lax.axis_size("expert")
    model_width = tokens.shape[1]
    picked = routes[:, :, None] == jnp.arange(experts, dtype=jnp.int32)[None, None, :]
    per_expert = jnp.sum(jnp.where(picked, route_weights[:, :, None], 0.0), axis=1)
    weight_hi = per_expert.astype(jnp.bfloat16)
    weight_lo = (per_expert - weight_hi.astype(jnp.float32)).astype(jnp.bfloat16)
    side = jnp.concatenate([weight_hi, weight_lo], axis=1)
    side_width = -(-side.shape[1] // 128) * 128
    side = jnp.pad(side, ((0, 0), (0, side_width - side.shape[1])))
    payload = jnp.concatenate(
        [centroid.astype(jnp.bfloat16), grad_sum.astype(jnp.bfloat16), side], axis=1
    )
    gathered = topo_all_gather(payload, experts)
    cent_all = gathered[:, :model_width]
    grad_all = gathered[:, model_width : 2 * model_width]
    side_all = gathered[:, 2 * model_width : 2 * model_width + 2 * experts].astype(jnp.float32)
    column = jnp.arange(experts, dtype=jnp.int32)[None, :]
    summed_side = side_all[:, :experts] + side_all[:, experts:]
    mine = jnp.sum(jnp.where(column == me, summed_side, 0.0), axis=1)
    other = jnp.sum(jnp.where(column == (me ^ 1), summed_side, 0.0), axis=1)
    swap_core = [(j, j ^ 1) for j in range(experts)]
    gate_mat, up_mat, down_mat = gate_weight[0], up_weight[0], down_weight[0]
    gate_pair = lax.ppermute(gate_mat, "expert", swap_core)
    up_pair = lax.ppermute(up_mat, "expert", swap_core)
    down_pair = lax.ppermute(down_mat, "expert", swap_core)
    output, input_grad = expert_dense(cent_all, grad_all, gate_mat, up_mat, down_mat)
    output_pair, input_grad_pair = expert_dense(cent_all, grad_all, gate_pair, up_pair, down_pair)
    weighted_out = mine[:, None] * output.astype(jnp.float32) + other[:, None] * output_pair.astype(
        jnp.float32
    )
    weighted_grad = mine[:, None] * input_grad.astype(jnp.float32) + other[
        :, None
    ] * input_grad_pair.astype(jnp.float32)
    summed = topo_reduce_scatter(jnp.concatenate([weighted_out, weighted_grad], axis=1), experts)
    combined = summed[:, :model_width]
    centroid_grad = summed[:, model_width:] - grad_sum
    layer_out = tokens.astype(jnp.float32) + jnp.take(combined - centroid, cluster_ids, axis=0)
    token_grad = out_grad.astype(jnp.float32) + jnp.take(
        centroid_grad / counts[:, None], cluster_ids, axis=0
    )
    return (layer_out, token_grad)


def per_device(*args):
    routes = args[3]
    cent_rows, fanout = routes.shape
    experts = lax.axis_size("expert")
    capacity = min(cent_rows, 2 * cent_rows * fanout // experts)
    if capacity == cent_rows and experts % 4 == 0:
        return per_device_dense(*args)
    return per_device_slots(*args)


def solution(mesh):
    placed = (
        P(("groups", "expert"), None),
        P(("groups", "expert"), None),
        P(("groups", "expert")),
        P(("groups", "expert"), None),
        P(("groups", "expert"), None),
        P("expert", None, None),
        P("expert", None, None),
        P("expert", None, None),
    )
    return jax.shard_map(
        per_device,
        mesh=mesh,
        in_specs=placed,
        out_specs=(P(("groups", "expert"), None), P(("groups", "expert"), None)),
        check_vma=False,
    )
```

```python
import jax
import jax.numpy as jnp
from jax import lax
from jax.sharding import PartitionSpec as P


def expert_forward(inputs, gate_mat, up_mat, down_mat):
    gate_act = jnp.dot(inputs, gate_mat, preferred_element_type=jnp.float32)
    up_act = jnp.dot(inputs, up_mat, preferred_element_type=jnp.float32)
    sigmoid_gate = jax.nn.sigmoid(gate_act)
    hidden = (gate_act * sigmoid_gate * up_act).astype(jnp.bfloat16)
    output = jnp.dot(hidden, down_mat, preferred_element_type=jnp.float32).astype(jnp.bfloat16)
    return (output, gate_act, up_act)


def expert_backward(incoming, gate_act, up_act, gate_mat, up_mat, down_mat):
    against = (((1,), (1,)), ((), ()))
    hidden_grad = lax.dot_general(incoming, down_mat, against, preferred_element_type=jnp.float32)
    sigmoid_gate = jax.nn.sigmoid(gate_act)
    gate_grad = (
        hidden_grad * up_act * sigmoid_gate * (1.0 + gate_act * (1.0 - sigmoid_gate))
    ).astype(jnp.bfloat16)
    up_grad = (hidden_grad * gate_act * sigmoid_gate).astype(jnp.bfloat16)
    summed = lax.dot_general(gate_grad, gate_mat, against, preferred_element_type=jnp.float32)
    summed = summed + lax.dot_general(up_grad, up_mat, against, preferred_element_type=jnp.float32)
    return summed.astype(jnp.bfloat16)


def per_device_slots(
    tokens, out_grad, cluster_ids, routes, route_weights, gate_weight, up_weight, down_weight
):
    model_width = tokens.shape[1]
    cent_rows = routes.shape[0]
    fanout = routes.shape[1]
    experts = lax.axis_size("expert")
    capacity = min(cent_rows, 2 * cent_rows * fanout // experts)
    member = (cluster_ids[:, None] == jnp.arange(cent_rows, dtype=jnp.int32)[None, :]).astype(
        jnp.bfloat16
    )
    counts = jnp.sum(member.astype(jnp.float32), axis=0)
    contract = (((0,), (0,)), ((), ()))
    centroid = (
        lax.dot_general(member, tokens, contract, preferred_element_type=jnp.float32)
        / counts[:, None]
    )
    grad_sum = lax.dot_general(member, out_grad, contract, preferred_element_type=jnp.float32)
    pair_ids = routes.reshape(-1)
    matches = (pair_ids[:, None] == jnp.arange(experts, dtype=jnp.int32)[None, :]).astype(jnp.int32)
    earlier = jnp.cumsum(matches, axis=0) - matches
    position = jnp.sum(earlier * matches, axis=1)
    slot_of = (pair_ids * capacity + position).reshape(cent_rows, fanout)
    slot_range = jnp.arange(experts * capacity, dtype=jnp.int32)
    placing = jnp.any(slot_of[None, :, :] == slot_range[:, None, None], axis=2).astype(jnp.bfloat16)
    send_cent = jnp.dot(placing, centroid.astype(jnp.bfloat16), preferred_element_type=jnp.float32)
    send_cent = send_cent.astype(jnp.bfloat16).reshape(experts, capacity, model_width)
    send_grad = jnp.dot(placing, grad_sum.astype(jnp.bfloat16), preferred_element_type=jnp.float32)
    send_grad = send_grad.astype(jnp.bfloat16).reshape(experts, capacity, model_width)
    gate_mat = gate_weight[0]
    up_mat = up_weight[0]
    down_mat = down_weight[0]
    arrived = lax.all_to_all(send_cent, "expert", split_axis=0, concat_axis=0, tiled=True)
    output, gate_act, up_act = expert_forward(
        arrived.reshape(-1, model_width), gate_mat, up_mat, down_mat
    )
    results = lax.all_to_all(
        output.reshape(experts, capacity, model_width),
        "expert",
        split_axis=0,
        concat_axis=0,
        tiled=True,
    )
    arrived_grad = lax.all_to_all(send_grad, "expert", split_axis=0, concat_axis=0, tiled=True)
    input_grad = expert_backward(
        arrived_grad.reshape(-1, model_width), gate_act, up_act, gate_mat, up_mat, down_mat
    )
    results_grad = lax.all_to_all(
        input_grad.reshape(experts, capacity, model_width),
        "expert",
        split_axis=0,
        concat_axis=0,
        tiled=True,
    )
    returned = results.reshape(-1, model_width)[slot_of]
    returned_grad = results_grad.reshape(-1, model_width)[slot_of]
    combined = jnp.sum(route_weights[:, :, None] * returned.astype(jnp.float32), axis=1)
    centroid_grad = (
        jnp.sum(route_weights[:, :, None] * returned_grad.astype(jnp.float32), axis=1) - grad_sum
    )
    layer_out = tokens.astype(jnp.float32) + jnp.take(combined - centroid, cluster_ids, axis=0)
    token_grad = out_grad.astype(jnp.float32) + jnp.take(
        centroid_grad / counts[:, None], cluster_ids, axis=0
    )
    return (layer_out, token_grad)


def pick(index, options):
    chosen = options[-1]
    for position in range(len(options) - 2, -1, -1):
        chosen = jnp.where(index == position, options[position], chosen)
    return chosen


def place(pieces, lines, like):
    slot = lax.broadcasted_iota(jnp.int32, (lines,) + (1,) * like.ndim, 0)
    stacked = jnp.zeros((lines,) + like.shape, like.dtype)
    for piece, origin in pieces:
        stacked = jnp.where(slot == origin, piece[None], stacked)
    return stacked


def topo_all_gather(shard, experts):
    lines = experts // 4
    me = lax.axis_index("expert")
    line = me // 4
    swap_row = [(j, j ^ 2) for j in range(experts)]
    here = [(shard, line)]
    there = [(lax.ppermute(shard, "expert", swap_row), line)]
    ahead, behind = shard, shard
    for step in range(1, lines):
        ahead = lax.ppermute(
            ahead,
            "expert",
            [(j, j + 4) for j in range(experts) if step - 1 <= j // 4 < lines - 1],
        )
        behind = lax.ppermute(
            behind,
            "expert",
            [(j, j - 4) for j in range(experts) if 1 <= j // 4 <= lines - step],
        )
        here.append((ahead, line - step))
        here.append((behind, line + step))
        ahead_row = [(j, j ^ 2) for j in range(experts) if j // 4 >= step]
        behind_row = [(j, j ^ 2) for j in range(experts) if j // 4 <= lines - 1 - step]
        if 2 * step > lines - 1:
            in_ahead = line >= step
            got = lax.ppermute(
                jnp.where(in_ahead, ahead, behind), "expert", sorted(ahead_row + behind_row)
            )
            origin = jnp.where(in_ahead, line - step, jnp.where(line <= lines - 1 - step, line + step, -1))
            there.append((got, origin))
        else:
            there.append((lax.ppermute(ahead, "expert", ahead_row), line - step))
            there.append((lax.ppermute(behind, "expert", behind_row), line + step))
    column = place(here, lines, shard)
    across = place(there, lines, shard)
    in_row = (me // 2) % 2
    mine = jnp.stack([pick(in_row, [column, across]), pick(in_row, [across, column])], axis=1)
    return mine.reshape((lines * 2 * shard.shape[0],) + shard.shape[1:])


def topo_reduce_scatter(blocks, experts):
    lines = experts // 4
    me = lax.axis_index("expert")
    rows = blocks.shape[0] // (2 * lines)
    plane = blocks.reshape((lines, 2, rows) + blocks.shape[1:])
    in_row = (me // 2) % 2
    keep = pick(in_row, [plane[:, 0], plane[:, 1]])
    give = pick(in_row, [plane[:, 1], plane[:, 0]])
    line = me // 4

    def row_sum(target, senders):
        mine = lax.dynamic_index_in_dim(keep, target, 0, keepdims=False)
        theirs = lax.dynamic_index_in_dim(give, target, 0, keepdims=False)
        pairs = [(j, j ^ 2) for j in range(experts) if senders(j // 4)]
        got = lax.ppermute(theirs.astype(jnp.bfloat16), "expert", pairs)
        return mine + got.astype(jnp.float32)

    ahead = jnp.zeros(keep.shape[1:], jnp.float32)
    behind = jnp.zeros(keep.shape[1:], jnp.float32)
    for step in range(1, lines):
        ahead_target = jnp.clip(line + lines - step, 0, lines - 1)
        behind_target = jnp.clip(line - lines + step, 0, lines - 1)
        if 2 * step <= lines:
            in_ahead = line <= step - 1
            target = jnp.where(in_ahead, ahead_target, behind_target)
            ahead_part = row_sum(target, lambda z, s=step: z <= s - 1 or z >= lines - s)
            behind_part = ahead_part
        else:
            ahead_part = row_sum(ahead_target, lambda z, s=step: z <= s - 1)
            behind_part = row_sum(behind_target, lambda z, s=step: z >= lines - s)
        ahead = lax.ppermute(
            (ahead + ahead_part).astype(jnp.bfloat16),
            "expert",
            [(j, j + 4) for j in range(experts) if j // 4 <= step - 1],
        ).astype(jnp.float32)
        behind = lax.ppermute(
            (behind + behind_part).astype(jnp.bfloat16),
            "expert",
            [(j, j - 4) for j in range(experts) if j // 4 >= lines - step],
        ).astype(jnp.float32)
    return row_sum(line, lambda z: True) + ahead + behind


def expert_dense(cent_in, grad_in, gate_mat, up_mat, down_mat):
    against = (((1,), (1,)), ((), ()))
    gate_act = jnp.dot(cent_in, gate_mat, preferred_element_type=jnp.float32)
    up_act = jnp.dot(cent_in, up_mat, preferred_element_type=jnp.float32)
    sigmoid_gate = jax.nn.sigmoid(gate_act)
    hidden = (gate_act * sigmoid_gate * up_act).astype(jnp.bfloat16)
    output = jnp.dot(hidden, down_mat, preferred_element_type=jnp.float32).astype(jnp.bfloat16)
    hidden_grad = lax.dot_general(grad_in, down_mat, against, preferred_element_type=jnp.float32)
    gate_grad = (
        hidden_grad * up_act * sigmoid_gate * (1.0 + gate_act * (1.0 - sigmoid_gate))
    ).astype(jnp.bfloat16)
    up_grad = (hidden_grad * gate_act * sigmoid_gate).astype(jnp.bfloat16)
    summed = lax.dot_general(gate_grad, gate_mat, against, preferred_element_type=jnp.float32)
    summed = summed + lax.dot_general(up_grad, up_mat, against, preferred_element_type=jnp.float32)
    return output, summed.astype(jnp.bfloat16)


def per_device_dense(
    tokens, out_grad, cluster_ids, routes, route_weights, gate_weight, up_weight, down_weight
):
    cent_rows = routes.shape[0]
    me = lax.axis_index("expert")
    member = (cluster_ids[:, None] == jnp.arange(cent_rows, dtype=jnp.int32)[None, :]).astype(
        jnp.bfloat16
    )
    counts = jnp.sum(member.astype(jnp.float32), axis=0)
    contract = (((0,), (0,)), ((), ()))
    model_width = tokens.shape[1]
    sums = lax.dot_general(
        member,
        jnp.concatenate([tokens, out_grad], axis=1),
        contract,
        preferred_element_type=jnp.float32,
    )
    centroid = sums[:, :model_width] / counts[:, None]
    grad_sum = sums[:, model_width:]
    experts = lax.axis_size("expert")
    model_width = tokens.shape[1]
    picked = routes[:, :, None] == jnp.arange(experts, dtype=jnp.int32)[None, None, :]
    per_expert = jnp.sum(jnp.where(picked, route_weights[:, :, None], 0.0), axis=1)
    weight_hi = per_expert.astype(jnp.bfloat16)
    weight_lo = (per_expert - weight_hi.astype(jnp.float32)).astype(jnp.bfloat16)
    side = jnp.concatenate([weight_hi, weight_lo], axis=1)
    side_width = -(-side.shape[1] // 128) * 128
    side = jnp.pad(side, ((0, 0), (0, side_width - side.shape[1])))
    payload = jnp.concatenate(
        [centroid.astype(jnp.bfloat16), grad_sum.astype(jnp.bfloat16), side], axis=1
    )
    gathered = topo_all_gather(payload, experts)
    cent_all = gathered[:, :model_width]
    grad_all = gathered[:, model_width : 2 * model_width]
    side_all = gathered[:, 2 * model_width : 2 * model_width + 2 * experts].astype(jnp.float32)
    column = jnp.arange(experts, dtype=jnp.int32)[None, :]
    summed_side = side_all[:, :experts] + side_all[:, experts:]
    mine = jnp.sum(jnp.where(column == me, summed_side, 0.0), axis=1)
    other = jnp.sum(jnp.where(column == (me ^ 1), summed_side, 0.0), axis=1)
    swap_core = [(j, j ^ 1) for j in range(experts)]
    gate_mat, up_mat, down_mat = gate_weight[0], up_weight[0], down_weight[0]
    gate_pair = lax.ppermute(gate_mat, "expert", swap_core)
    up_pair = lax.ppermute(up_mat, "expert", swap_core)
    down_pair = lax.ppermute(down_mat, "expert", swap_core)
    output, input_grad = expert_dense(cent_all, grad_all, gate_mat, up_mat, down_mat)
    output_pair, input_grad_pair = expert_dense(cent_all, grad_all, gate_pair, up_pair, down_pair)
    weighted_out = mine[:, None] * output.astype(jnp.float32) + other[:, None] * output_pair.astype(
        jnp.float32
    )
    weighted_grad = mine[:, None] * input_grad.astype(jnp.float32) + other[
        :, None
    ] * input_grad_pair.astype(jnp.float32)
    summed = topo_reduce_scatter(jnp.concatenate([weighted_out, weighted_grad], axis=1), experts)
    combined = summed[:, :model_width]
    centroid_grad = summed[:, model_width:] - grad_sum
    layer_out = tokens.astype(jnp.float32) + jnp.take(combined - centroid, cluster_ids, axis=0)
    token_grad = out_grad.astype(jnp.float32) + jnp.take(
        centroid_grad / counts[:, None], cluster_ids, axis=0
    )
    return (layer_out, token_grad)


def per_device(*args):
    routes = args[3]
    cent_rows, fanout = routes.shape
    experts = lax.axis_size("expert")
    capacity = min(cent_rows, 2 * cent_rows * fanout // experts)
    if capacity == cent_rows and experts % 4 == 0:
        return per_device_dense(*args)
    return per_device_slots(*args)


def solution(mesh):
    placed = (
        P(("groups", "expert"), None),
        P(("groups", "expert"), None),
        P(("groups", "expert")),
        P(("groups", "expert"), None),
        P(("groups", "expert"), None),
        P("expert", None, None),
        P("expert", None, None),
        P("expert", None, None),
    )
    return jax.shard_map(
        per_device,
        mesh=mesh,
        in_specs=placed,
        out_specs=(P(("groups", "expert"), None), P(("groups", "expert"), None)),
        check_vma=False,
    )
```

```python
import jax
import jax.numpy as jnp
from jax import lax
from jax.sharding import PartitionSpec as P


def expert_forward(inputs, gate_mat, up_mat, down_mat):
    gate_act = jnp.dot(inputs, gate_mat, preferred_element_type=jnp.float32)
    up_act = jnp.dot(inputs, up_mat, preferred_element_type=jnp.float32)
    sigmoid_gate = jax.nn.sigmoid(gate_act)
    hidden = (gate_act * sigmoid_gate * up_act).astype(jnp.bfloat16)
    output = jnp.dot(hidden, down_mat, preferred_element_type=jnp.float32).astype(jnp.bfloat16)
    return (output, gate_act, up_act)


def expert_backward(incoming, gate_act, up_act, gate_mat, up_mat, down_mat):
    against = (((1,), (1,)), ((), ()))
    hidden_grad = lax.dot_general(incoming, down_mat, against, preferred_element_type=jnp.float32)
    sigmoid_gate = jax.nn.sigmoid(gate_act)
    gate_grad = (
        hidden_grad * up_act * sigmoid_gate * (1.0 + gate_act * (1.0 - sigmoid_gate))
    ).astype(jnp.bfloat16)
    up_grad = (hidden_grad * gate_act * sigmoid_gate).astype(jnp.bfloat16)
    summed = lax.dot_general(gate_grad, gate_mat, against, preferred_element_type=jnp.float32)
    summed = summed + lax.dot_general(up_grad, up_mat, against, preferred_element_type=jnp.float32)
    return summed.astype(jnp.bfloat16)


def per_device_slots(
    tokens, out_grad, cluster_ids, routes, route_weights, gate_weight, up_weight, down_weight
):
    model_width = tokens.shape[1]
    cent_rows = routes.shape[0]
    fanout = routes.shape[1]
    experts = lax.axis_size("expert")
    capacity = min(cent_rows, 2 * cent_rows * fanout // experts)
    member = (cluster_ids[:, None] == jnp.arange(cent_rows, dtype=jnp.int32)[None, :]).astype(
        jnp.bfloat16
    )
    counts = jnp.sum(member.astype(jnp.float32), axis=0)
    contract = (((0,), (0,)), ((), ()))
    centroid = (
        lax.dot_general(member, tokens, contract, preferred_element_type=jnp.float32)
        / counts[:, None]
    )
    grad_sum = lax.dot_general(member, out_grad, contract, preferred_element_type=jnp.float32)
    pair_ids = routes.reshape(-1)
    matches = (pair_ids[:, None] == jnp.arange(experts, dtype=jnp.int32)[None, :]).astype(jnp.int32)
    earlier = jnp.cumsum(matches, axis=0) - matches
    position = jnp.sum(earlier * matches, axis=1)
    slot_of = (pair_ids * capacity + position).reshape(cent_rows, fanout)
    slot_range = jnp.arange(experts * capacity, dtype=jnp.int32)
    placing = jnp.any(slot_of[None, :, :] == slot_range[:, None, None], axis=2).astype(jnp.bfloat16)
    send_cent = jnp.dot(placing, centroid.astype(jnp.bfloat16), preferred_element_type=jnp.float32)
    send_cent = send_cent.astype(jnp.bfloat16).reshape(experts, capacity, model_width)
    send_grad = jnp.dot(placing, grad_sum.astype(jnp.bfloat16), preferred_element_type=jnp.float32)
    send_grad = send_grad.astype(jnp.bfloat16).reshape(experts, capacity, model_width)
    gate_mat = gate_weight[0]
    up_mat = up_weight[0]
    down_mat = down_weight[0]
    arrived = lax.all_to_all(send_cent, "expert", split_axis=0, concat_axis=0, tiled=True)
    output, gate_act, up_act = expert_forward(
        arrived.reshape(-1, model_width), gate_mat, up_mat, down_mat
    )
    results = lax.all_to_all(
        output.reshape(experts, capacity, model_width),
        "expert",
        split_axis=0,
        concat_axis=0,
        tiled=True,
    )
    arrived_grad = lax.all_to_all(send_grad, "expert", split_axis=0, concat_axis=0, tiled=True)
    input_grad = expert_backward(
        arrived_grad.reshape(-1, model_width), gate_act, up_act, gate_mat, up_mat, down_mat
    )
    results_grad = lax.all_to_all(
        input_grad.reshape(experts, capacity, model_width),
        "expert",
        split_axis=0,
        concat_axis=0,
        tiled=True,
    )
    returned = results.reshape(-1, model_width)[slot_of]
    returned_grad = results_grad.reshape(-1, model_width)[slot_of]
    combined = jnp.sum(route_weights[:, :, None] * returned.astype(jnp.float32), axis=1)
    centroid_grad = (
        jnp.sum(route_weights[:, :, None] * returned_grad.astype(jnp.float32), axis=1) - grad_sum
    )
    layer_out = tokens.astype(jnp.float32) + jnp.take(combined - centroid, cluster_ids, axis=0)
    token_grad = out_grad.astype(jnp.float32) + jnp.take(
        centroid_grad / counts[:, None], cluster_ids, axis=0
    )
    return (layer_out, token_grad)


def pick(index, options):
    chosen = options[-1]
    for position in range(len(options) - 2, -1, -1):
        chosen = jnp.where(index == position, options[position], chosen)
    return chosen


def place(pieces, lines, like):
    slot = lax.broadcasted_iota(jnp.int32, (lines,) + (1,) * like.ndim, 0)
    stacked = jnp.zeros((lines,) + like.shape, like.dtype)
    for piece, origin in pieces:
        stacked = jnp.where(slot == origin, piece[None], stacked)
    return stacked


def by_line(line, values):
    return pick(line, [jnp.asarray(v, jnp.int32) for v in values])


def topo_all_gather(shard, experts):
    lines = experts // 4
    me = lax.axis_index("expert")
    line = me // 4
    swap_row = [(j, j ^ 2) for j in range(experts)]
    here = [(shard, line)]
    there = [(lax.ppermute(shard, "expert", swap_row), line)]
    pieces = []
    queues = [[] for _ in range(lines)]
    ahead, behind = shard, shard

    def send_row(queue_heads):
        senders = [z for z in range(lines) if queue_heads[z] is not None]
        data = pick(line, [pieces[queue_heads[z] if queue_heads[z] is not None else 0][0] for z in range(lines)])
        origin = by_line(line, [pieces[h][1][z] if h is not None else -1 for z, h in enumerate(queue_heads)])
        pairs = [(j, j ^ 2) for j in range(experts) if j // 4 in senders]
        there.append((lax.ppermute(data, "expert", pairs), origin))

    for step in range(1, lines):
        ahead = lax.ppermute(
            ahead,
            "expert",
            [(j, j + 4) for j in range(experts) if step - 1 <= j // 4 < lines - 1],
        )
        behind = lax.ppermute(
            behind,
            "expert",
            [(j, j - 4) for j in range(experts) if 1 <= j // 4 <= lines - step],
        )
        here.append((ahead, line - step))
        here.append((behind, line + step))
        pieces.append((ahead, [z - step for z in range(lines)]))
        pieces.append((behind, [z + step for z in range(lines)]))
        for z in range(lines):
            if z >= step:
                queues[z].append(len(pieces) - 2)
            if z <= lines - 1 - step:
                queues[z].append(len(pieces) - 1)
        send_row([queues[z].pop(0) if queues[z] else None for z in range(lines)])
    while any(queues):
        send_row([queues[z].pop(0) if queues[z] else None for z in range(lines)])
    column = place(here, lines, shard)
    across = place(there, lines, shard)
    in_row = (me // 2) % 2
    mine = jnp.stack([pick(in_row, [column, across]), pick(in_row, [across, column])], axis=1)
    return mine.reshape((lines * 2 * shard.shape[0],) + shard.shape[1:])


def topo_reduce_scatter(blocks, experts):
    lines = experts // 4
    me = lax.axis_index("expert")
    rows = blocks.shape[0] // (2 * lines)
    plane = blocks.reshape((lines, 2, rows) + blocks.shape[1:])
    in_row = (me // 2) % 2
    keep = pick(in_row, [plane[:, 0], plane[:, 1]])
    give = pick(in_row, [plane[:, 1], plane[:, 0]])
    line = me // 4
    plans = []
    for z in range(lines):
        needs = [(step, 0, z + lines - step) for step in range(z + 1, lines)]
        needs += [(step, 1, z - lines + step) for step in range(lines - z, lines)]
        needs = sorted(needs) + [(lines, 2, z)]
        assert all(need[0] >= slot + 1 for slot, need in enumerate(needs))
        plans.append(needs)
    summed = []
    for slot in range(lines):
        target = by_line(line, [plans[z][slot][2] for z in range(lines)])
        mine = lax.dynamic_index_in_dim(keep, target, 0, keepdims=False)
        theirs = lax.dynamic_index_in_dim(give, target, 0, keepdims=False)
        got = lax.ppermute(theirs.astype(jnp.bfloat16), "expert", [(j, j ^ 2) for j in range(experts)])
        summed.append(mine + got.astype(jnp.float32))

    def ready(step, role):
        slots = []
        for z in range(lines):
            found = [k for k, need in enumerate(plans[z]) if need[:2] == (step, role)]
            slots.append(found[0] if found else 0)
        return pick(line, [summed[k] for k in slots])

    ahead = jnp.zeros(keep.shape[1:], jnp.float32)
    behind = jnp.zeros(keep.shape[1:], jnp.float32)
    for step in range(1, lines):
        ahead = lax.ppermute(
            (ahead + ready(step, 0)).astype(jnp.bfloat16),
            "expert",
            [(j, j + 4) for j in range(experts) if j // 4 <= step - 1],
        ).astype(jnp.float32)
        behind = lax.ppermute(
            (behind + ready(step, 1)).astype(jnp.bfloat16),
            "expert",
            [(j, j - 4) for j in range(experts) if j // 4 >= lines - step],
        ).astype(jnp.float32)
    return ready(lines, 2) + ahead + behind


def expert_dense(cent_in, grad_in, gate_mat, up_mat, down_mat):
    against = (((1,), (1,)), ((), ()))
    gate_act = jnp.dot(cent_in, gate_mat, preferred_element_type=jnp.float32)
    up_act = jnp.dot(cent_in, up_mat, preferred_element_type=jnp.float32)
    sigmoid_gate = jax.nn.sigmoid(gate_act)
    hidden = (gate_act * sigmoid_gate * up_act).astype(jnp.bfloat16)
    output = jnp.dot(hidden, down_mat, preferred_element_type=jnp.float32).astype(jnp.bfloat16)
    hidden_grad = lax.dot_general(grad_in, down_mat, against, preferred_element_type=jnp.float32)
    gate_grad = (
        hidden_grad * up_act * sigmoid_gate * (1.0 + gate_act * (1.0 - sigmoid_gate))
    ).astype(jnp.bfloat16)
    up_grad = (hidden_grad * gate_act * sigmoid_gate).astype(jnp.bfloat16)
    summed = lax.dot_general(gate_grad, gate_mat, against, preferred_element_type=jnp.float32)
    summed = summed + lax.dot_general(up_grad, up_mat, against, preferred_element_type=jnp.float32)
    return output, summed.astype(jnp.bfloat16)


def per_device_dense(
    tokens, out_grad, cluster_ids, routes, route_weights, gate_weight, up_weight, down_weight
):
    cent_rows = routes.shape[0]
    me = lax.axis_index("expert")
    member = (cluster_ids[:, None] == jnp.arange(cent_rows, dtype=jnp.int32)[None, :]).astype(
        jnp.bfloat16
    )
    counts = jnp.sum(member.astype(jnp.float32), axis=0)
    contract = (((0,), (0,)), ((), ()))
    model_width = tokens.shape[1]
    sums = lax.dot_general(
        member,
        jnp.concatenate([tokens, out_grad], axis=1),
        contract,
        preferred_element_type=jnp.float32,
    )
    centroid = sums[:, :model_width] / counts[:, None]
    grad_sum = sums[:, model_width:]
    experts = lax.axis_size("expert")
    model_width = tokens.shape[1]
    picked = routes[:, :, None] == jnp.arange(experts, dtype=jnp.int32)[None, None, :]
    per_expert = jnp.sum(jnp.where(picked, route_weights[:, :, None], 0.0), axis=1)
    weight_hi = per_expert.astype(jnp.bfloat16)
    weight_lo = (per_expert - weight_hi.astype(jnp.float32)).astype(jnp.bfloat16)
    side = jnp.concatenate([weight_hi, weight_lo], axis=1)
    side_width = -(-side.shape[1] // 128) * 128
    side = jnp.pad(side, ((0, 0), (0, side_width - side.shape[1])))
    payload = jnp.concatenate(
        [centroid.astype(jnp.bfloat16), grad_sum.astype(jnp.bfloat16), side], axis=1
    )
    gathered = topo_all_gather(payload, experts)
    cent_all = gathered[:, :model_width]
    grad_all = gathered[:, model_width : 2 * model_width]
    side_all = gathered[:, 2 * model_width : 2 * model_width + 2 * experts].astype(jnp.float32)
    column = jnp.arange(experts, dtype=jnp.int32)[None, :]
    summed_side = side_all[:, :experts] + side_all[:, experts:]
    mine = jnp.sum(jnp.where(column == me, summed_side, 0.0), axis=1)
    other = jnp.sum(jnp.where(column == (me ^ 1), summed_side, 0.0), axis=1)
    swap_core = [(j, j ^ 1) for j in range(experts)]
    gate_mat, up_mat, down_mat = gate_weight[0], up_weight[0], down_weight[0]
    gate_pair = lax.ppermute(gate_mat, "expert", swap_core)
    up_pair = lax.ppermute(up_mat, "expert", swap_core)
    down_pair = lax.ppermute(down_mat, "expert", swap_core)
    output, input_grad = expert_dense(cent_all, grad_all, gate_mat, up_mat, down_mat)
    output_pair, input_grad_pair = expert_dense(cent_all, grad_all, gate_pair, up_pair, down_pair)
    weighted_out = mine[:, None] * output.astype(jnp.float32) + other[:, None] * output_pair.astype(
        jnp.float32
    )
    weighted_grad = mine[:, None] * input_grad.astype(jnp.float32) + other[
        :, None
    ] * input_grad_pair.astype(jnp.float32)
    summed = topo_reduce_scatter(jnp.concatenate([weighted_out, weighted_grad], axis=1), experts)
    combined = summed[:, :model_width]
    centroid_grad = summed[:, model_width:] - grad_sum
    layer_out = tokens.astype(jnp.float32) + jnp.take(combined - centroid, cluster_ids, axis=0)
    token_grad = out_grad.astype(jnp.float32) + jnp.take(
        centroid_grad / counts[:, None], cluster_ids, axis=0
    )
    return (layer_out, token_grad)


def per_device(*args):
    routes = args[3]
    cent_rows, fanout = routes.shape
    experts = lax.axis_size("expert")
    capacity = min(cent_rows, 2 * cent_rows * fanout // experts)
    if capacity == cent_rows and experts % 4 == 0:
        return per_device_dense(*args)
    return per_device_slots(*args)


def solution(mesh):
    placed = (
        P(("groups", "expert"), None),
        P(("groups", "expert"), None),
        P(("groups", "expert")),
        P(("groups", "expert"), None),
        P(("groups", "expert"), None),
        P("expert", None, None),
        P("expert", None, None),
        P("expert", None, None),
    )
    return jax.shard_map(
        per_device,
        mesh=mesh,
        in_specs=placed,
        out_specs=(P(("groups", "expert"), None), P(("groups", "expert"), None)),
        check_vma=False,
    )
```

```python
import jax
import jax.numpy as jnp
from jax import lax
from jax.sharding import PartitionSpec as P


def expert_forward(inputs, gate_mat, up_mat, down_mat):
    gate_act = jnp.dot(inputs, gate_mat, preferred_element_type=jnp.float32)
    up_act = jnp.dot(inputs, up_mat, preferred_element_type=jnp.float32)
    sigmoid_gate = jax.nn.sigmoid(gate_act)
    hidden = (gate_act * sigmoid_gate * up_act).astype(jnp.bfloat16)
    output = jnp.dot(hidden, down_mat, preferred_element_type=jnp.float32).astype(jnp.bfloat16)
    return (output, gate_act, up_act)


def expert_backward(incoming, gate_act, up_act, gate_mat, up_mat, down_mat):
    against = (((1,), (1,)), ((), ()))
    hidden_grad = lax.dot_general(incoming, down_mat, against, preferred_element_type=jnp.float32)
    sigmoid_gate = jax.nn.sigmoid(gate_act)
    gate_grad = (
        hidden_grad * up_act * sigmoid_gate * (1.0 + gate_act * (1.0 - sigmoid_gate))
    ).astype(jnp.bfloat16)
    up_grad = (hidden_grad * gate_act * sigmoid_gate).astype(jnp.bfloat16)
    summed = lax.dot_general(gate_grad, gate_mat, against, preferred_element_type=jnp.float32)
    summed = summed + lax.dot_general(up_grad, up_mat, against, preferred_element_type=jnp.float32)
    return summed.astype(jnp.bfloat16)


def per_device_slots(
    tokens, out_grad, cluster_ids, routes, route_weights, gate_weight, up_weight, down_weight
):
    model_width = tokens.shape[1]
    cent_rows = routes.shape[0]
    fanout = routes.shape[1]
    experts = lax.axis_size("expert")
    capacity = min(cent_rows, 2 * cent_rows * fanout // experts)
    member = (cluster_ids[:, None] == jnp.arange(cent_rows, dtype=jnp.int32)[None, :]).astype(
        jnp.bfloat16
    )
    counts = jnp.sum(member.astype(jnp.float32), axis=0)
    contract = (((0,), (0,)), ((), ()))
    centroid = (
        lax.dot_general(member, tokens, contract, preferred_element_type=jnp.float32)
        / counts[:, None]
    )
    grad_sum = lax.dot_general(member, out_grad, contract, preferred_element_type=jnp.float32)
    pair_ids = routes.reshape(-1)
    matches = (pair_ids[:, None] == jnp.arange(experts, dtype=jnp.int32)[None, :]).astype(jnp.int32)
    earlier = jnp.cumsum(matches, axis=0) - matches
    position = jnp.sum(earlier * matches, axis=1)
    slot_of = (pair_ids * capacity + position).reshape(cent_rows, fanout)
    slot_range = jnp.arange(experts * capacity, dtype=jnp.int32)
    placing = jnp.any(slot_of[None, :, :] == slot_range[:, None, None], axis=2).astype(jnp.bfloat16)
    send_cent = jnp.dot(placing, centroid.astype(jnp.bfloat16), preferred_element_type=jnp.float32)
    send_cent = send_cent.astype(jnp.bfloat16).reshape(experts, capacity, model_width)
    send_grad = jnp.dot(placing, grad_sum.astype(jnp.bfloat16), preferred_element_type=jnp.float32)
    send_grad = send_grad.astype(jnp.bfloat16).reshape(experts, capacity, model_width)
    gate_mat = gate_weight[0]
    up_mat = up_weight[0]
    down_mat = down_weight[0]
    arrived = lax.all_to_all(send_cent, "expert", split_axis=0, concat_axis=0, tiled=True)
    output, gate_act, up_act = expert_forward(
        arrived.reshape(-1, model_width), gate_mat, up_mat, down_mat
    )
    results = lax.all_to_all(
        output.reshape(experts, capacity, model_width),
        "expert",
        split_axis=0,
        concat_axis=0,
        tiled=True,
    )
    arrived_grad = lax.all_to_all(send_grad, "expert", split_axis=0, concat_axis=0, tiled=True)
    input_grad = expert_backward(
        arrived_grad.reshape(-1, model_width), gate_act, up_act, gate_mat, up_mat, down_mat
    )
    results_grad = lax.all_to_all(
        input_grad.reshape(experts, capacity, model_width),
        "expert",
        split_axis=0,
        concat_axis=0,
        tiled=True,
    )
    returned = results.reshape(-1, model_width)[slot_of]
    returned_grad = results_grad.reshape(-1, model_width)[slot_of]
    combined = jnp.sum(route_weights[:, :, None] * returned.astype(jnp.float32), axis=1)
    centroid_grad = (
        jnp.sum(route_weights[:, :, None] * returned_grad.astype(jnp.float32), axis=1) - grad_sum
    )
    layer_out = tokens.astype(jnp.float32) + jnp.take(combined - centroid, cluster_ids, axis=0)
    token_grad = out_grad.astype(jnp.float32) + jnp.take(
        centroid_grad / counts[:, None], cluster_ids, axis=0
    )
    return (layer_out, token_grad)


def pick(index, options):
    chosen = options[-1]
    for position in range(len(options) - 2, -1, -1):
        chosen = jnp.where(index == position, options[position], chosen)
    return chosen


def place(pieces, lines, like):
    slot = lax.broadcasted_iota(jnp.int32, (lines,) + (1,) * like.ndim, 0)
    stacked = jnp.zeros((lines,) + like.shape, like.dtype)
    for piece, origin in pieces:
        stacked = jnp.where(slot == origin, piece[None], stacked)
    return stacked


def by_line(line, values):
    return pick(line, [jnp.asarray(v, jnp.int32) for v in values])


def topo_all_gather(shard, experts):
    lines = experts // 4
    me = lax.axis_index("expert")
    line = me // 4
    swap_row = [(j, j ^ 2) for j in range(experts)]
    here = [(shard, line)]
    there = [(lax.ppermute(shard, "expert", swap_row), line)]
    pieces = []
    queues = [[] for _ in range(lines)]
    ahead, behind = shard, shard

    def send_row(queue_heads):
        senders = [z for z in range(lines) if queue_heads[z] is not None]
        data = pick(line, [pieces[queue_heads[z] if queue_heads[z] is not None else 0][0] for z in range(lines)])
        origin = by_line(line, [pieces[h][1][z] if h is not None else -1 for z, h in enumerate(queue_heads)])
        pairs = [(j, j ^ 2) for j in range(experts) if j // 4 in senders]
        there.append((lax.ppermute(data, "expert", pairs), origin))

    for step in range(1, lines):
        ahead = lax.ppermute(
            ahead,
            "expert",
            [(j, j + 4) for j in range(experts) if step - 1 <= j // 4 < lines - 1],
        )
        behind = lax.ppermute(
            behind,
            "expert",
            [(j, j - 4) for j in range(experts) if 1 <= j // 4 <= lines - step],
        )
        here.append((ahead, line - step))
        here.append((behind, line + step))
        pieces.append((ahead, [z - step for z in range(lines)]))
        pieces.append((behind, [z + step for z in range(lines)]))
        for z in range(lines):
            if z >= step:
                queues[z].append(len(pieces) - 2)
            if z <= lines - 1 - step:
                queues[z].append(len(pieces) - 1)
        send_row([queues[z].pop(0) if queues[z] else None for z in range(lines)])
    while any(queues):
        send_row([queues[z].pop(0) if queues[z] else None for z in range(lines)])
    column = place(here, lines, shard)
    across = place(there, lines, shard)
    in_row = (me // 2) % 2
    mine = jnp.stack([pick(in_row, [column, across]), pick(in_row, [across, column])], axis=1)
    return mine.reshape((lines * 2 * shard.shape[0],) + shard.shape[1:])


def topo_reduce_scatter(blocks, experts):
    lines = experts // 4
    me = lax.axis_index("expert")
    rows = blocks.shape[0] // (2 * lines)
    plane = blocks.reshape((lines, 2, rows) + blocks.shape[1:])
    in_row = (me // 2) % 2
    keep = pick(in_row, [plane[:, 0], plane[:, 1]])
    give = pick(in_row, [plane[:, 1], plane[:, 0]])
    line = me // 4

    def row_sum(target, senders):
        mine = lax.dynamic_index_in_dim(keep, target, 0, keepdims=False)
        theirs = lax.dynamic_index_in_dim(give, target, 0, keepdims=False)
        pairs = [(j, j ^ 2) for j in range(experts) if senders(j // 4)]
        got = lax.ppermute(theirs.astype(jnp.bfloat16), "expert", pairs)
        return mine + got.astype(jnp.float32)

    ahead = jnp.zeros(keep.shape[1:], jnp.float32)
    behind = jnp.zeros(keep.shape[1:], jnp.float32)
    for step in range(1, lines):
        ahead_target = jnp.clip(line + lines - step, 0, lines - 1)
        behind_target = jnp.clip(line - lines + step, 0, lines - 1)
        if 2 * step <= lines:
            in_ahead = line <= step - 1
            target = jnp.where(in_ahead, ahead_target, behind_target)
            ahead_part = row_sum(target, lambda z, s=step: z <= s - 1 or z >= lines - s)
            behind_part = ahead_part
        else:
            ahead_part = row_sum(ahead_target, lambda z, s=step: z <= s - 1)
            behind_part = row_sum(behind_target, lambda z, s=step: z >= lines - s)
        ahead = lax.ppermute(
            (ahead + ahead_part).astype(jnp.bfloat16),
            "expert",
            [(j, j + 4) for j in range(experts) if j // 4 <= step - 1],
        ).astype(jnp.float32)
        behind = lax.ppermute(
            (behind + behind_part).astype(jnp.bfloat16),
            "expert",
            [(j, j - 4) for j in range(experts) if j // 4 >= lines - step],
        ).astype(jnp.float32)
    return row_sum(line, lambda z: True) + ahead + behind


def expert_dense(cent_in, grad_in, gate_mat, up_mat, down_mat):
    against = (((1,), (1,)), ((), ()))
    gate_act = jnp.dot(cent_in, gate_mat, preferred_element_type=jnp.float32)
    up_act = jnp.dot(cent_in, up_mat, preferred_element_type=jnp.float32)
    sigmoid_gate = jax.nn.sigmoid(gate_act)
    hidden = (gate_act * sigmoid_gate * up_act).astype(jnp.bfloat16)
    output = jnp.dot(hidden, down_mat, preferred_element_type=jnp.float32).astype(jnp.bfloat16)
    hidden_grad = lax.dot_general(grad_in, down_mat, against, preferred_element_type=jnp.float32)
    gate_grad = (
        hidden_grad * up_act * sigmoid_gate * (1.0 + gate_act * (1.0 - sigmoid_gate))
    ).astype(jnp.bfloat16)
    up_grad = (hidden_grad * gate_act * sigmoid_gate).astype(jnp.bfloat16)
    summed = lax.dot_general(gate_grad, gate_mat, against, preferred_element_type=jnp.float32)
    summed = summed + lax.dot_general(up_grad, up_mat, against, preferred_element_type=jnp.float32)
    return output, summed.astype(jnp.bfloat16)


def per_device_dense(
    tokens, out_grad, cluster_ids, routes, route_weights, gate_weight, up_weight, down_weight
):
    cent_rows = routes.shape[0]
    me = lax.axis_index("expert")
    member = (cluster_ids[:, None] == jnp.arange(cent_rows, dtype=jnp.int32)[None, :]).astype(
        jnp.bfloat16
    )
    counts = jnp.sum(member.astype(jnp.float32), axis=0)
    contract = (((0,), (0,)), ((), ()))
    model_width = tokens.shape[1]
    sums = lax.dot_general(
        member,
        jnp.concatenate([tokens, out_grad], axis=1),
        contract,
        preferred_element_type=jnp.float32,
    )
    centroid = sums[:, :model_width] / counts[:, None]
    grad_sum = sums[:, model_width:]
    experts = lax.axis_size("expert")
    model_width = tokens.shape[1]
    picked = routes[:, :, None] == jnp.arange(experts, dtype=jnp.int32)[None, None, :]
    per_expert = jnp.sum(jnp.where(picked, route_weights[:, :, None], 0.0), axis=1)
    weight_hi = per_expert.astype(jnp.bfloat16)
    weight_lo = (per_expert - weight_hi.astype(jnp.float32)).astype(jnp.bfloat16)
    side = jnp.concatenate([weight_hi, weight_lo], axis=1)
    side_width = -(-side.shape[1] // 128) * 128
    side = jnp.pad(side, ((0, 0), (0, side_width - side.shape[1])))
    payload = jnp.concatenate(
        [centroid.astype(jnp.bfloat16), grad_sum.astype(jnp.bfloat16), side], axis=1
    )
    gathered = topo_all_gather(payload, experts)
    cent_all = gathered[:, :model_width]
    grad_all = gathered[:, model_width : 2 * model_width]
    side_all = gathered[:, 2 * model_width : 2 * model_width + 2 * experts].astype(jnp.float32)
    column = jnp.arange(experts, dtype=jnp.int32)[None, :]
    summed_side = side_all[:, :experts] + side_all[:, experts:]
    mine = jnp.sum(jnp.where(column == me, summed_side, 0.0), axis=1)
    other = jnp.sum(jnp.where(column == (me ^ 1), summed_side, 0.0), axis=1)
    swap_core = [(j, j ^ 1) for j in range(experts)]
    gate_mat, up_mat, down_mat = gate_weight[0], up_weight[0], down_weight[0]
    gate_pair = lax.ppermute(gate_mat, "expert", swap_core)
    up_pair = lax.ppermute(up_mat, "expert", swap_core)
    down_pair = lax.ppermute(down_mat, "expert", swap_core)
    output, input_grad = expert_dense(cent_all, grad_all, gate_mat, up_mat, down_mat)
    output_pair, input_grad_pair = expert_dense(cent_all, grad_all, gate_pair, up_pair, down_pair)
    weighted_out = mine[:, None] * output.astype(jnp.float32) + other[:, None] * output_pair.astype(
        jnp.float32
    )
    weighted_grad = mine[:, None] * input_grad.astype(jnp.float32) + other[
        :, None
    ] * input_grad_pair.astype(jnp.float32)
    summed = topo_reduce_scatter(jnp.concatenate([weighted_out, weighted_grad], axis=1), experts)
    combined = summed[:, :model_width]
    centroid_grad = summed[:, model_width:] - grad_sum
    layer_out = tokens.astype(jnp.float32) + jnp.take(combined - centroid, cluster_ids, axis=0)
    token_grad = out_grad.astype(jnp.float32) + jnp.take(
        centroid_grad / counts[:, None], cluster_ids, axis=0
    )
    return (layer_out, token_grad)


def per_device(*args):
    routes = args[3]
    cent_rows, fanout = routes.shape
    experts = lax.axis_size("expert")
    capacity = min(cent_rows, 2 * cent_rows * fanout // experts)
    if capacity == cent_rows and experts % 4 == 0:
        return per_device_dense(*args)
    return per_device_slots(*args)


def solution(mesh):
    placed = (
        P(("groups", "expert"), None),
        P(("groups", "expert"), None),
        P(("groups", "expert")),
        P(("groups", "expert"), None),
        P(("groups", "expert"), None),
        P("expert", None, None),
        P("expert", None, None),
        P("expert", None, None),
    )
    return jax.shard_map(
        per_device,
        mesh=mesh,
        in_specs=placed,
        out_specs=(P(("groups", "expert"), None), P(("groups", "expert"), None)),
        check_vma=False,
    )
```

```python
import jax
import jax.numpy as jnp
from jax import lax
from jax.sharding import PartitionSpec as P


def expert_forward(inputs, gate_mat, up_mat, down_mat):
    gate_act = jnp.dot(inputs, gate_mat, preferred_element_type=jnp.float32)
    up_act = jnp.dot(inputs, up_mat, preferred_element_type=jnp.float32)
    sigmoid_gate = jax.nn.sigmoid(gate_act)
    hidden = (gate_act * sigmoid_gate * up_act).astype(jnp.bfloat16)
    output = jnp.dot(hidden, down_mat, preferred_element_type=jnp.float32).astype(jnp.bfloat16)
    return (output, gate_act, up_act)


def expert_backward(incoming, gate_act, up_act, gate_mat, up_mat, down_mat):
    against = (((1,), (1,)), ((), ()))
    hidden_grad = lax.dot_general(incoming, down_mat, against, preferred_element_type=jnp.float32)
    sigmoid_gate = jax.nn.sigmoid(gate_act)
    gate_grad = (
        hidden_grad * up_act * sigmoid_gate * (1.0 + gate_act * (1.0 - sigmoid_gate))
    ).astype(jnp.bfloat16)
    up_grad = (hidden_grad * gate_act * sigmoid_gate).astype(jnp.bfloat16)
    summed = lax.dot_general(gate_grad, gate_mat, against, preferred_element_type=jnp.float32)
    summed = summed + lax.dot_general(up_grad, up_mat, against, preferred_element_type=jnp.float32)
    return summed.astype(jnp.bfloat16)


def per_device_slots(
    tokens, out_grad, cluster_ids, routes, route_weights, gate_weight, up_weight, down_weight
):
    model_width = tokens.shape[1]
    cent_rows = routes.shape[0]
    fanout = routes.shape[1]
    experts = lax.axis_size("expert")
    capacity = min(cent_rows, 2 * cent_rows * fanout // experts)
    member = (cluster_ids[:, None] == jnp.arange(cent_rows, dtype=jnp.int32)[None, :]).astype(
        jnp.bfloat16
    )
    counts = jnp.sum(member.astype(jnp.float32), axis=0)
    contract = (((0,), (0,)), ((), ()))
    centroid = (
        lax.dot_general(member, tokens, contract, preferred_element_type=jnp.float32)
        / counts[:, None]
    )
    grad_sum = lax.dot_general(member, out_grad, contract, preferred_element_type=jnp.float32)
    pair_ids = routes.reshape(-1)
    matches = (pair_ids[:, None] == jnp.arange(experts, dtype=jnp.int32)[None, :]).astype(jnp.int32)
    earlier = jnp.cumsum(matches, axis=0) - matches
    position = jnp.sum(earlier * matches, axis=1)
    slot_of = (pair_ids * capacity + position).reshape(cent_rows, fanout)
    slot_range = jnp.arange(experts * capacity, dtype=jnp.int32)
    placing = jnp.any(slot_of[None, :, :] == slot_range[:, None, None], axis=2).astype(jnp.bfloat16)
    send_cent = jnp.dot(placing, centroid.astype(jnp.bfloat16), preferred_element_type=jnp.float32)
    send_cent = send_cent.astype(jnp.bfloat16).reshape(experts, capacity, model_width)
    send_grad = jnp.dot(placing, grad_sum.astype(jnp.bfloat16), preferred_element_type=jnp.float32)
    send_grad = send_grad.astype(jnp.bfloat16).reshape(experts, capacity, model_width)
    gate_mat = gate_weight[0]
    up_mat = up_weight[0]
    down_mat = down_weight[0]
    arrived = lax.all_to_all(send_cent, "expert", split_axis=0, concat_axis=0, tiled=True)
    output, gate_act, up_act = expert_forward(
        arrived.reshape(-1, model_width), gate_mat, up_mat, down_mat
    )
    results = lax.all_to_all(
        output.reshape(experts, capacity, model_width),
        "expert",
        split_axis=0,
        concat_axis=0,
        tiled=True,
    )
    arrived_grad = lax.all_to_all(send_grad, "expert", split_axis=0, concat_axis=0, tiled=True)
    input_grad = expert_backward(
        arrived_grad.reshape(-1, model_width), gate_act, up_act, gate_mat, up_mat, down_mat
    )
    results_grad = lax.all_to_all(
        input_grad.reshape(experts, capacity, model_width),
        "expert",
        split_axis=0,
        concat_axis=0,
        tiled=True,
    )
    returned = results.reshape(-1, model_width)[slot_of]
    returned_grad = results_grad.reshape(-1, model_width)[slot_of]
    combined = jnp.sum(route_weights[:, :, None] * returned.astype(jnp.float32), axis=1)
    centroid_grad = (
        jnp.sum(route_weights[:, :, None] * returned_grad.astype(jnp.float32), axis=1) - grad_sum
    )
    layer_out = tokens.astype(jnp.float32) + jnp.take(combined - centroid, cluster_ids, axis=0)
    token_grad = out_grad.astype(jnp.float32) + jnp.take(
        centroid_grad / counts[:, None], cluster_ids, axis=0
    )
    return (layer_out, token_grad)


def pick(index, options):
    chosen = options[-1]
    for position in range(len(options) - 2, -1, -1):
        chosen = jnp.where(index == position, options[position], chosen)
    return chosen


def place(pieces, lines, like):
    slot = lax.broadcasted_iota(jnp.int32, (lines,) + (1,) * like.ndim, 0)
    stacked = jnp.zeros((lines,) + like.shape, like.dtype)
    for piece, origin in pieces:
        stacked = jnp.where(slot == origin, piece[None], stacked)
    return stacked


def topo_all_gather(shard, experts):
    lines = experts // 4
    me = lax.axis_index("expert")
    line = me // 4
    swap_row = [(j, j ^ 2) for j in range(experts)]
    here = [(shard, line)]
    there = [(lax.ppermute(shard, "expert", swap_row), line)]
    ahead, behind = shard, shard
    for step in range(1, lines):
        ahead = lax.ppermute(
            ahead,
            "expert",
            [(j, j + 4) for j in range(experts) if step - 1 <= j // 4 < lines - 1],
        )
        behind = lax.ppermute(
            behind,
            "expert",
            [(j, j - 4) for j in range(experts) if 1 <= j // 4 <= lines - step],
        )
        here.append((ahead, line - step))
        here.append((behind, line + step))
        ahead_row = [(j, j ^ 2) for j in range(experts) if j // 4 >= step]
        behind_row = [(j, j ^ 2) for j in range(experts) if j // 4 <= lines - 1 - step]
        if 2 * step > lines - 1:
            in_ahead = line >= step
            got = lax.ppermute(
                jnp.where(in_ahead, ahead, behind), "expert", sorted(ahead_row + behind_row)
            )
            origin = jnp.where(in_ahead, line - step, jnp.where(line <= lines - 1 - step, line + step, -1))
            there.append((got, origin))
        else:
            there.append((lax.ppermute(ahead, "expert", ahead_row), line - step))
            there.append((lax.ppermute(behind, "expert", behind_row), line + step))
    column = place(here, lines, shard)
    across = place(there, lines, shard)
    in_row = (me // 2) % 2
    mine = jnp.stack([pick(in_row, [column, across]), pick(in_row, [across, column])], axis=1)
    return mine.reshape((lines * 2 * shard.shape[0],) + shard.shape[1:])


def topo_reduce_scatter(blocks, experts):
    lines = experts // 4
    me = lax.axis_index("expert")
    rows = blocks.shape[0] // (2 * lines)
    plane = blocks.reshape((lines, 2, rows) + blocks.shape[1:])
    in_row = (me // 2) % 2
    keep = pick(in_row, [plane[:, 0], plane[:, 1]])
    give = pick(in_row, [plane[:, 1], plane[:, 0]])
    line = me // 4

    def row_sum(target, senders):
        mine = lax.dynamic_index_in_dim(keep, target, 0, keepdims=False)
        theirs = lax.dynamic_index_in_dim(give, target, 0, keepdims=False)
        pairs = [(j, j ^ 2) for j in range(experts) if senders(j // 4)]
        got = lax.ppermute(theirs.astype(jnp.bfloat16), "expert", pairs)
        return mine + got.astype(jnp.float32)

    if lines == 4:
        return four_line_sum(keep, give, line, row_sum)
    ahead = jnp.zeros(keep.shape[1:], jnp.float32)
    behind = jnp.zeros(keep.shape[1:], jnp.float32)
    for step in range(1, lines):
        ahead_target = jnp.clip(line + lines - step, 0, lines - 1)
        behind_target = jnp.clip(line - lines + step, 0, lines - 1)
        if 2 * step <= lines:
            in_ahead = line <= step - 1
            target = jnp.where(in_ahead, ahead_target, behind_target)
            ahead_part = row_sum(target, lambda z, s=step: z <= s - 1 or z >= lines - s)
            behind_part = ahead_part
        else:
            ahead_part = row_sum(ahead_target, lambda z, s=step: z <= s - 1)
            behind_part = row_sum(behind_target, lambda z, s=step: z >= lines - s)
        ahead = lax.ppermute(
            (ahead + ahead_part).astype(jnp.bfloat16),
            "expert",
            [(j, j + 4) for j in range(experts) if j // 4 <= step - 1],
        ).astype(jnp.float32)
        behind = lax.ppermute(
            (behind + behind_part).astype(jnp.bfloat16),
            "expert",
            [(j, j - 4) for j in range(experts) if j // 4 >= lines - step],
        ).astype(jnp.float32)
    return row_sum(line, lambda z: True) + ahead + behind


def four_line_sum(keep, give, line, row_sum):
    experts = 16
    end = (line == 0) | (line == 3)
    first = row_sum(jnp.where(end, 3 - line, line), lambda z: True)
    ahead = lax.ppermute(first.astype(jnp.bfloat16), "expert", [(j, j + 4) for j in range(4)])
    behind = lax.ppermute(first.astype(jnp.bfloat16), "expert", [(j, j - 4) for j in range(12, 16)])
    ahead, behind = ahead.astype(jnp.float32), behind.astype(jnp.float32)
    second = row_sum(jnp.where(line <= 1, line + 2, line - 2), lambda z: True)
    ahead = lax.ppermute(
        (ahead + second).astype(jnp.bfloat16), "expert", [(j, j + 4) for j in range(8)]
    ).astype(jnp.float32)
    behind = lax.ppermute(
        (behind + second).astype(jnp.bfloat16), "expert", [(j, j - 4) for j in range(8, 16)]
    ).astype(jnp.float32)
    third = row_sum(jnp.where(line <= 2, line + 1, line - 1), lambda z: True)
    fourth = row_sum(jnp.where(end, line, line - 1), lambda z: True)
    behind_part = jnp.where(line == 3, third, fourth)
    ahead = lax.ppermute(
        (ahead + third).astype(jnp.bfloat16), "expert", [(j, j + 4) for j in range(12)]
    ).astype(jnp.float32)
    behind = lax.ppermute(
        (behind + behind_part).astype(jnp.bfloat16), "expert", [(j, j - 4) for j in range(4, 16)]
    ).astype(jnp.float32)
    return jnp.where(end, fourth, first) + ahead + behind


def expert_dense(cent_in, grad_in, gate_mat, up_mat, down_mat):
    against = (((1,), (1,)), ((), ()))
    gate_act = jnp.dot(cent_in, gate_mat, preferred_element_type=jnp.float32)
    up_act = jnp.dot(cent_in, up_mat, preferred_element_type=jnp.float32)
    sigmoid_gate = jax.nn.sigmoid(gate_act)
    hidden = (gate_act * sigmoid_gate * up_act).astype(jnp.bfloat16)
    output = jnp.dot(hidden, down_mat, preferred_element_type=jnp.float32).astype(jnp.bfloat16)
    hidden_grad = lax.dot_general(grad_in, down_mat, against, preferred_element_type=jnp.float32)
    gate_grad = (
        hidden_grad * up_act * sigmoid_gate * (1.0 + gate_act * (1.0 - sigmoid_gate))
    ).astype(jnp.bfloat16)
    up_grad = (hidden_grad * gate_act * sigmoid_gate).astype(jnp.bfloat16)
    summed = lax.dot_general(gate_grad, gate_mat, against, preferred_element_type=jnp.float32)
    summed = summed + lax.dot_general(up_grad, up_mat, against, preferred_element_type=jnp.float32)
    return output, summed.astype(jnp.bfloat16)


def per_device_dense(
    tokens, out_grad, cluster_ids, routes, route_weights, gate_weight, up_weight, down_weight
):
    cent_rows = routes.shape[0]
    me = lax.axis_index("expert")
    member = (cluster_ids[:, None] == jnp.arange(cent_rows, dtype=jnp.int32)[None, :]).astype(
        jnp.bfloat16
    )
    counts = jnp.sum(member.astype(jnp.float32), axis=0)
    contract = (((0,), (0,)), ((), ()))
    model_width = tokens.shape[1]
    sums = lax.dot_general(
        member,
        jnp.concatenate([tokens, out_grad], axis=1),
        contract,
        preferred_element_type=jnp.float32,
    )
    centroid = sums[:, :model_width] / counts[:, None]
    grad_sum = sums[:, model_width:]
    experts = lax.axis_size("expert")
    model_width = tokens.shape[1]
    picked = routes[:, :, None] == jnp.arange(experts, dtype=jnp.int32)[None, None, :]
    per_expert = jnp.sum(jnp.where(picked, route_weights[:, :, None], 0.0), axis=1)
    weight_hi = per_expert.astype(jnp.bfloat16)
    weight_lo = (per_expert - weight_hi.astype(jnp.float32)).astype(jnp.bfloat16)
    side = jnp.concatenate([weight_hi, weight_lo], axis=1)
    side_width = -(-side.shape[1] // 128) * 128
    side = jnp.pad(side, ((0, 0), (0, side_width - side.shape[1])))
    payload = jnp.concatenate(
        [centroid.astype(jnp.bfloat16), grad_sum.astype(jnp.bfloat16), side], axis=1
    )
    gathered = topo_all_gather(payload, experts)
    cent_all = gathered[:, :model_width]
    grad_all = gathered[:, model_width : 2 * model_width]
    side_all = gathered[:, 2 * model_width : 2 * model_width + 2 * experts].astype(jnp.float32)
    column = jnp.arange(experts, dtype=jnp.int32)[None, :]
    summed_side = side_all[:, :experts] + side_all[:, experts:]
    mine = jnp.sum(jnp.where(column == me, summed_side, 0.0), axis=1)
    other = jnp.sum(jnp.where(column == (me ^ 1), summed_side, 0.0), axis=1)
    swap_core = [(j, j ^ 1) for j in range(experts)]
    gate_mat, up_mat, down_mat = gate_weight[0], up_weight[0], down_weight[0]
    gate_pair = lax.ppermute(gate_mat, "expert", swap_core)
    up_pair = lax.ppermute(up_mat, "expert", swap_core)
    down_pair = lax.ppermute(down_mat, "expert", swap_core)
    output, input_grad = expert_dense(cent_all, grad_all, gate_mat, up_mat, down_mat)
    output_pair, input_grad_pair = expert_dense(cent_all, grad_all, gate_pair, up_pair, down_pair)
    weighted_out = mine[:, None] * output.astype(jnp.float32) + other[:, None] * output_pair.astype(
        jnp.float32
    )
    weighted_grad = mine[:, None] * input_grad.astype(jnp.float32) + other[
        :, None
    ] * input_grad_pair.astype(jnp.float32)
    summed = topo_reduce_scatter(jnp.concatenate([weighted_out, weighted_grad], axis=1), experts)
    combined = summed[:, :model_width]
    centroid_grad = summed[:, model_width:] - grad_sum
    layer_out = tokens.astype(jnp.float32) + jnp.take(combined - centroid, cluster_ids, axis=0)
    token_grad = out_grad.astype(jnp.float32) + jnp.take(
        centroid_grad / counts[:, None], cluster_ids, axis=0
    )
    return (layer_out, token_grad)


def per_device(*args):
    routes = args[3]
    cent_rows, fanout = routes.shape
    experts = lax.axis_size("expert")
    capacity = min(cent_rows, 2 * cent_rows * fanout // experts)
    if capacity == cent_rows and experts % 4 == 0:
        return per_device_dense(*args)
    return per_device_slots(*args)


def solution(mesh):
    placed = (
        P(("groups", "expert"), None),
        P(("groups", "expert"), None),
        P(("groups", "expert")),
        P(("groups", "expert"), None),
        P(("groups", "expert"), None),
        P("expert", None, None),
        P("expert", None, None),
        P("expert", None, None),
    )
    return jax.shard_map(
        per_device,
        mesh=mesh,
        in_specs=placed,
        out_specs=(P(("groups", "expert"), None), P(("groups", "expert"), None)),
        check_vma=False,
    )
```

```python
import jax
import jax.numpy as jnp
from jax import lax
from jax.sharding import PartitionSpec as P


def expert_forward(inputs, gate_mat, up_mat, down_mat):
    gate_act = jnp.dot(inputs, gate_mat, preferred_element_type=jnp.float32)
    up_act = jnp.dot(inputs, up_mat, preferred_element_type=jnp.float32)
    sigmoid_gate = jax.nn.sigmoid(gate_act)
    hidden = (gate_act * sigmoid_gate * up_act).astype(jnp.bfloat16)
    output = jnp.dot(hidden, down_mat, preferred_element_type=jnp.float32).astype(jnp.bfloat16)
    return (output, gate_act, up_act)


def expert_backward(incoming, gate_act, up_act, gate_mat, up_mat, down_mat):
    against = (((1,), (1,)), ((), ()))
    hidden_grad = lax.dot_general(incoming, down_mat, against, preferred_element_type=jnp.float32)
    sigmoid_gate = jax.nn.sigmoid(gate_act)
    gate_grad = (
        hidden_grad * up_act * sigmoid_gate * (1.0 + gate_act * (1.0 - sigmoid_gate))
    ).astype(jnp.bfloat16)
    up_grad = (hidden_grad * gate_act * sigmoid_gate).astype(jnp.bfloat16)
    summed = lax.dot_general(gate_grad, gate_mat, against, preferred_element_type=jnp.float32)
    summed = summed + lax.dot_general(up_grad, up_mat, against, preferred_element_type=jnp.float32)
    return summed.astype(jnp.bfloat16)


def per_device_slots(
    tokens, out_grad, cluster_ids, routes, route_weights, gate_weight, up_weight, down_weight
):
    model_width = tokens.shape[1]
    cent_rows = routes.shape[0]
    fanout = routes.shape[1]
    experts = lax.axis_size("expert")
    capacity = min(cent_rows, 2 * cent_rows * fanout // experts)
    member = (cluster_ids[:, None] == jnp.arange(cent_rows, dtype=jnp.int32)[None, :]).astype(
        jnp.bfloat16
    )
    counts = jnp.sum(member.astype(jnp.float32), axis=0)
    contract = (((0,), (0,)), ((), ()))
    centroid = (
        lax.dot_general(member, tokens, contract, preferred_element_type=jnp.float32)
        / counts[:, None]
    )
    grad_sum = lax.dot_general(member, out_grad, contract, preferred_element_type=jnp.float32)
    pair_ids = routes.reshape(-1)
    matches = (pair_ids[:, None] == jnp.arange(experts, dtype=jnp.int32)[None, :]).astype(jnp.int32)
    earlier = jnp.cumsum(matches, axis=0) - matches
    position = jnp.sum(earlier * matches, axis=1)
    slot_of = (pair_ids * capacity + position).reshape(cent_rows, fanout)
    slot_range = jnp.arange(experts * capacity, dtype=jnp.int32)
    placing = jnp.any(slot_of[None, :, :] == slot_range[:, None, None], axis=2).astype(jnp.bfloat16)
    send_cent = jnp.dot(placing, centroid.astype(jnp.bfloat16), preferred_element_type=jnp.float32)
    send_cent = send_cent.astype(jnp.bfloat16).reshape(experts, capacity, model_width)
    send_grad = jnp.dot(placing, grad_sum.astype(jnp.bfloat16), preferred_element_type=jnp.float32)
    send_grad = send_grad.astype(jnp.bfloat16).reshape(experts, capacity, model_width)
    gate_mat = gate_weight[0]
    up_mat = up_weight[0]
    down_mat = down_weight[0]
    arrived = lax.all_to_all(send_cent, "expert", split_axis=0, concat_axis=0, tiled=True)
    output, gate_act, up_act = expert_forward(
        arrived.reshape(-1, model_width), gate_mat, up_mat, down_mat
    )
    results = lax.all_to_all(
        output.reshape(experts, capacity, model_width),
        "expert",
        split_axis=0,
        concat_axis=0,
        tiled=True,
    )
    arrived_grad = lax.all_to_all(send_grad, "expert", split_axis=0, concat_axis=0, tiled=True)
    input_grad = expert_backward(
        arrived_grad.reshape(-1, model_width), gate_act, up_act, gate_mat, up_mat, down_mat
    )
    results_grad = lax.all_to_all(
        input_grad.reshape(experts, capacity, model_width),
        "expert",
        split_axis=0,
        concat_axis=0,
        tiled=True,
    )
    returned = results.reshape(-1, model_width)[slot_of]
    returned_grad = results_grad.reshape(-1, model_width)[slot_of]
    combined = jnp.sum(route_weights[:, :, None] * returned.astype(jnp.float32), axis=1)
    centroid_grad = (
        jnp.sum(route_weights[:, :, None] * returned_grad.astype(jnp.float32), axis=1) - grad_sum
    )
    layer_out = tokens.astype(jnp.float32) + jnp.take(combined - centroid, cluster_ids, axis=0)
    token_grad = out_grad.astype(jnp.float32) + jnp.take(
        centroid_grad / counts[:, None], cluster_ids, axis=0
    )
    return (layer_out, token_grad)


def pick(index, options):
    chosen = options[-1]
    for position in range(len(options) - 2, -1, -1):
        chosen = jnp.where(index == position, options[position], chosen)
    return chosen


def place(pieces, lines, like):
    slot = lax.broadcasted_iota(jnp.int32, (lines,) + (1,) * like.ndim, 0)
    stacked = jnp.zeros((lines,) + like.shape, like.dtype)
    for piece, origin in pieces:
        stacked = jnp.where(slot == origin, piece[None], stacked)
    return stacked


def topo_all_gather(shard, experts):
    lines = experts // 4
    me = lax.axis_index("expert")
    line = me // 4
    swap_row = [(j, j ^ 2) for j in range(experts)]
    here = [(shard, line)]
    if lines == 4:
        here, there = four_line_gather(shard, line, here, swap_row)
        column = place(here, lines, shard)
        across = place(there, lines, shard)
        in_row = (me // 2) % 2
        mine = jnp.stack([pick(in_row, [column, across]), pick(in_row, [across, column])], axis=1)
        return mine.reshape((lines * 2 * shard.shape[0],) + shard.shape[1:])
    there = [(lax.ppermute(shard, "expert", swap_row), line)]
    ahead, behind = shard, shard
    for step in range(1, lines):
        ahead = lax.ppermute(
            ahead,
            "expert",
            [(j, j + 4) for j in range(experts) if step - 1 <= j // 4 < lines - 1],
        )
        behind = lax.ppermute(
            behind,
            "expert",
            [(j, j - 4) for j in range(experts) if 1 <= j // 4 <= lines - step],
        )
        here.append((ahead, line - step))
        here.append((behind, line + step))
        ahead_row = [(j, j ^ 2) for j in range(experts) if j // 4 >= step]
        behind_row = [(j, j ^ 2) for j in range(experts) if j // 4 <= lines - 1 - step]
        if 2 * step > lines - 1:
            in_ahead = line >= step
            got = lax.ppermute(
                jnp.where(in_ahead, ahead, behind), "expert", sorted(ahead_row + behind_row)
            )
            origin = jnp.where(in_ahead, line - step, jnp.where(line <= lines - 1 - step, line + step, -1))
            there.append((got, origin))
        else:
            there.append((lax.ppermute(ahead, "expert", ahead_row), line - step))
            there.append((lax.ppermute(behind, "expert", behind_row), line + step))
    column = place(here, lines, shard)
    across = place(there, lines, shard)
    in_row = (me // 2) % 2
    mine = jnp.stack([pick(in_row, [column, across]), pick(in_row, [across, column])], axis=1)
    return mine.reshape((lines * 2 * shard.shape[0],) + shard.shape[1:])


def topo_reduce_scatter(blocks, experts):
    lines = experts // 4
    me = lax.axis_index("expert")
    rows = blocks.shape[0] // (2 * lines)
    plane = blocks.reshape((lines, 2, rows) + blocks.shape[1:])
    in_row = (me // 2) % 2
    keep = pick(in_row, [plane[:, 0], plane[:, 1]])
    give = pick(in_row, [plane[:, 1], plane[:, 0]])
    line = me // 4

    def row_sum(target, senders):
        mine = lax.dynamic_index_in_dim(keep, target, 0, keepdims=False)
        theirs = lax.dynamic_index_in_dim(give, target, 0, keepdims=False)
        pairs = [(j, j ^ 2) for j in range(experts) if senders(j // 4)]
        got = lax.ppermute(theirs.astype(jnp.bfloat16), "expert", pairs)
        return mine + got.astype(jnp.float32)

    if lines == 4:
        return four_line_sum(keep, give, line, row_sum)
    ahead = jnp.zeros(keep.shape[1:], jnp.float32)
    behind = jnp.zeros(keep.shape[1:], jnp.float32)
    for step in range(1, lines):
        ahead_target = jnp.clip(line + lines - step, 0, lines - 1)
        behind_target = jnp.clip(line - lines + step, 0, lines - 1)
        if 2 * step <= lines:
            in_ahead = line <= step - 1
            target = jnp.where(in_ahead, ahead_target, behind_target)
            ahead_part = row_sum(target, lambda z, s=step: z <= s - 1 or z >= lines - s)
            behind_part = ahead_part
        else:
            ahead_part = row_sum(ahead_target, lambda z, s=step: z <= s - 1)
            behind_part = row_sum(behind_target, lambda z, s=step: z >= lines - s)
        ahead = lax.ppermute(
            (ahead + ahead_part).astype(jnp.bfloat16),
            "expert",
            [(j, j + 4) for j in range(experts) if j // 4 <= step - 1],
        ).astype(jnp.float32)
        behind = lax.ppermute(
            (behind + behind_part).astype(jnp.bfloat16),
            "expert",
            [(j, j - 4) for j in range(experts) if j // 4 >= lines - step],
        ).astype(jnp.float32)
    return row_sum(line, lambda z: True) + ahead + behind


def four_line_gather(shard, line, here, swap_row):
    there = [(lax.ppermute(shard, "expert", swap_row), line)]
    ahead = lax.ppermute(shard, "expert", [(j, j + 4) for j in range(12)])
    behind = lax.ppermute(shard, "expert", [(j, j - 4) for j in range(4, 16)])
    here = here + [(ahead, line - 1), (behind, line + 1)]
    first_behind = behind
    got = lax.ppermute(jnp.where(line == 0, behind, ahead), "expert", swap_row)
    there.append((got, jnp.where(line == 0, line + 1, line - 1)))
    ahead = lax.ppermute(ahead, "expert", [(j, j + 4) for j in range(4, 12)])
    behind = lax.ppermute(behind, "expert", [(j, j - 4) for j in range(4, 12)])
    here = here + [(ahead, line - 2), (behind, line + 2)]
    got = lax.ppermute(jnp.where(line >= 2, ahead, behind), "expert", swap_row)
    there.append((got, jnp.where(line >= 2, line - 2, line + 2)))
    ahead = lax.ppermute(ahead, "expert", [(j, j + 4) for j in range(8, 12)])
    behind = lax.ppermute(behind, "expert", [(j, j - 4) for j in range(4, 8)])
    here = here + [(ahead, line - 3), (behind, line + 3)]
    last = jnp.where(line == 3, ahead, jnp.where(line == 0, behind, first_behind))
    got = lax.ppermute(last, "expert", swap_row)
    there.append((got, jnp.where(line == 3, 0, jnp.where(line == 0, 3, line + 1))))
    return here, there


def four_line_sum(keep, give, line, row_sum):
    experts = 16
    end = (line == 0) | (line == 3)
    first = row_sum(jnp.where(end, 3 - line, line), lambda z: True)
    ahead = lax.ppermute(first.astype(jnp.bfloat16), "expert", [(j, j + 4) for j in range(4)])
    behind = lax.ppermute(first.astype(jnp.bfloat16), "expert", [(j, j - 4) for j in range(12, 16)])
    ahead, behind = ahead.astype(jnp.float32), behind.astype(jnp.float32)
    second = row_sum(jnp.where(line <= 1, line + 2, line - 2), lambda z: True)
    ahead = lax.ppermute(
        (ahead + second).astype(jnp.bfloat16), "expert", [(j, j + 4) for j in range(8)]
    ).astype(jnp.float32)
    behind = lax.ppermute(
        (behind + second).astype(jnp.bfloat16), "expert", [(j, j - 4) for j in range(8, 16)]
    ).astype(jnp.float32)
    third = row_sum(jnp.where(line <= 2, line + 1, line - 1), lambda z: True)
    fourth = row_sum(jnp.where(end, line, line - 1), lambda z: True)
    behind_part = jnp.where(line == 3, third, fourth)
    ahead = lax.ppermute(
        (ahead + third).astype(jnp.bfloat16), "expert", [(j, j + 4) for j in range(12)]
    ).astype(jnp.float32)
    behind = lax.ppermute(
        (behind + behind_part).astype(jnp.bfloat16), "expert", [(j, j - 4) for j in range(4, 16)]
    ).astype(jnp.float32)
    return jnp.where(end, fourth, first) + ahead + behind


def expert_dense(cent_in, grad_in, gate_mat, up_mat, down_mat):
    against = (((1,), (1,)), ((), ()))
    gate_act = jnp.dot(cent_in, gate_mat, preferred_element_type=jnp.float32)
    up_act = jnp.dot(cent_in, up_mat, preferred_element_type=jnp.float32)
    sigmoid_gate = jax.nn.sigmoid(gate_act)
    hidden = (gate_act * sigmoid_gate * up_act).astype(jnp.bfloat16)
    output = jnp.dot(hidden, down_mat, preferred_element_type=jnp.float32).astype(jnp.bfloat16)
    hidden_grad = lax.dot_general(grad_in, down_mat, against, preferred_element_type=jnp.float32)
    gate_grad = (
        hidden_grad * up_act * sigmoid_gate * (1.0 + gate_act * (1.0 - sigmoid_gate))
    ).astype(jnp.bfloat16)
    up_grad = (hidden_grad * gate_act * sigmoid_gate).astype(jnp.bfloat16)
    summed = lax.dot_general(gate_grad, gate_mat, against, preferred_element_type=jnp.float32)
    summed = summed + lax.dot_general(up_grad, up_mat, against, preferred_element_type=jnp.float32)
    return output, summed.astype(jnp.bfloat16)


def per_device_dense(
    tokens, out_grad, cluster_ids, routes, route_weights, gate_weight, up_weight, down_weight
):
    cent_rows = routes.shape[0]
    me = lax.axis_index("expert")
    member = (cluster_ids[:, None] == jnp.arange(cent_rows, dtype=jnp.int32)[None, :]).astype(
        jnp.bfloat16
    )
    counts = jnp.sum(member.astype(jnp.float32), axis=0)
    contract = (((0,), (0,)), ((), ()))
    model_width = tokens.shape[1]
    sums = lax.dot_general(
        member,
        jnp.concatenate([tokens, out_grad], axis=1),
        contract,
        preferred_element_type=jnp.float32,
    )
    centroid = sums[:, :model_width] / counts[:, None]
    grad_sum = sums[:, model_width:]
    experts = lax.axis_size("expert")
    model_width = tokens.shape[1]
    picked = routes[:, :, None] == jnp.arange(experts, dtype=jnp.int32)[None, None, :]
    per_expert = jnp.sum(jnp.where(picked, route_weights[:, :, None], 0.0), axis=1)
    weight_hi = per_expert.astype(jnp.bfloat16)
    weight_lo = (per_expert - weight_hi.astype(jnp.float32)).astype(jnp.bfloat16)
    side = jnp.concatenate([weight_hi, weight_lo], axis=1)
    side_width = -(-side.shape[1] // 128) * 128
    side = jnp.pad(side, ((0, 0), (0, side_width - side.shape[1])))
    payload = jnp.concatenate(
        [centroid.astype(jnp.bfloat16), grad_sum.astype(jnp.bfloat16), side], axis=1
    )
    gathered = topo_all_gather(payload, experts)
    cent_all = gathered[:, :model_width]
    grad_all = gathered[:, model_width : 2 * model_width]
    side_all = gathered[:, 2 * model_width : 2 * model_width + 2 * experts].astype(jnp.float32)
    column = jnp.arange(experts, dtype=jnp.int32)[None, :]
    summed_side = side_all[:, :experts] + side_all[:, experts:]
    mine = jnp.sum(jnp.where(column == me, summed_side, 0.0), axis=1)
    other = jnp.sum(jnp.where(column == (me ^ 1), summed_side, 0.0), axis=1)
    swap_core = [(j, j ^ 1) for j in range(experts)]
    gate_mat, up_mat, down_mat = gate_weight[0], up_weight[0], down_weight[0]
    gate_pair = lax.ppermute(gate_mat, "expert", swap_core)
    up_pair = lax.ppermute(up_mat, "expert", swap_core)
    down_pair = lax.ppermute(down_mat, "expert", swap_core)
    output, input_grad = expert_dense(cent_all, grad_all, gate_mat, up_mat, down_mat)
    output_pair, input_grad_pair = expert_dense(cent_all, grad_all, gate_pair, up_pair, down_pair)
    weighted_out = mine[:, None] * output.astype(jnp.float32) + other[:, None] * output_pair.astype(
        jnp.float32
    )
    weighted_grad = mine[:, None] * input_grad.astype(jnp.float32) + other[
        :, None
    ] * input_grad_pair.astype(jnp.float32)
    summed = topo_reduce_scatter(jnp.concatenate([weighted_out, weighted_grad], axis=1), experts)
    combined = summed[:, :model_width]
    centroid_grad = summed[:, model_width:] - grad_sum
    layer_out = tokens.astype(jnp.float32) + jnp.take(combined - centroid, cluster_ids, axis=0)
    token_grad = out_grad.astype(jnp.float32) + jnp.take(
        centroid_grad / counts[:, None], cluster_ids, axis=0
    )
    return (layer_out, token_grad)


def per_device(*args):
    routes = args[3]
    cent_rows, fanout = routes.shape
    experts = lax.axis_size("expert")
    capacity = min(cent_rows, 2 * cent_rows * fanout // experts)
    if capacity == cent_rows and experts % 4 == 0:
        return per_device_dense(*args)
    return per_device_slots(*args)


def solution(mesh):
    placed = (
        P(("groups", "expert"), None),
        P(("groups", "expert"), None),
        P(("groups", "expert")),
        P(("groups", "expert"), None),
        P(("groups", "expert"), None),
        P("expert", None, None),
        P("expert", None, None),
        P("expert", None, None),
    )
    return jax.shard_map(
        per_device,
        mesh=mesh,
        in_specs=placed,
        out_specs=(P(("groups", "expert"), None), P(("groups", "expert"), None)),
        check_vma=False,
    )
```

```python
import jax
import jax.numpy as jnp
from jax import lax
from jax.sharding import PartitionSpec as P


def expert_forward(inputs, gate_mat, up_mat, down_mat):
    gate_act = jnp.dot(inputs, gate_mat, preferred_element_type=jnp.float32)
    up_act = jnp.dot(inputs, up_mat, preferred_element_type=jnp.float32)
    sigmoid_gate = jax.nn.sigmoid(gate_act)
    hidden = (gate_act * sigmoid_gate * up_act).astype(jnp.bfloat16)
    output = jnp.dot(hidden, down_mat, preferred_element_type=jnp.float32).astype(jnp.bfloat16)
    return (output, gate_act, up_act)


def expert_backward(incoming, gate_act, up_act, gate_mat, up_mat, down_mat):
    against = (((1,), (1,)), ((), ()))
    hidden_grad = lax.dot_general(incoming, down_mat, against, preferred_element_type=jnp.float32)
    sigmoid_gate = jax.nn.sigmoid(gate_act)
    gate_grad = (
        hidden_grad * up_act * sigmoid_gate * (1.0 + gate_act * (1.0 - sigmoid_gate))
    ).astype(jnp.bfloat16)
    up_grad = (hidden_grad * gate_act * sigmoid_gate).astype(jnp.bfloat16)
    summed = lax.dot_general(gate_grad, gate_mat, against, preferred_element_type=jnp.float32)
    summed = summed + lax.dot_general(up_grad, up_mat, against, preferred_element_type=jnp.float32)
    return summed.astype(jnp.bfloat16)


def per_device_slots(
    tokens, out_grad, cluster_ids, routes, route_weights, gate_weight, up_weight, down_weight
):
    model_width = tokens.shape[1]
    cent_rows = routes.shape[0]
    fanout = routes.shape[1]
    experts = lax.axis_size("expert")
    capacity = min(cent_rows, 2 * cent_rows * fanout // experts)
    member = (cluster_ids[:, None] == jnp.arange(cent_rows, dtype=jnp.int32)[None, :]).astype(
        jnp.bfloat16
    )
    counts = jnp.sum(member.astype(jnp.float32), axis=0)
    contract = (((0,), (0,)), ((), ()))
    centroid = (
        lax.dot_general(member, tokens, contract, preferred_element_type=jnp.float32)
        / counts[:, None]
    )
    grad_sum = lax.dot_general(member, out_grad, contract, preferred_element_type=jnp.float32)
    pair_ids = routes.reshape(-1)
    matches = (pair_ids[:, None] == jnp.arange(experts, dtype=jnp.int32)[None, :]).astype(jnp.int32)
    earlier = jnp.cumsum(matches, axis=0) - matches
    position = jnp.sum(earlier * matches, axis=1)
    slot_of = (pair_ids * capacity + position).reshape(cent_rows, fanout)
    slot_range = jnp.arange(experts * capacity, dtype=jnp.int32)
    placing = jnp.any(slot_of[None, :, :] == slot_range[:, None, None], axis=2).astype(jnp.bfloat16)
    send_cent = jnp.dot(placing, centroid.astype(jnp.bfloat16), preferred_element_type=jnp.float32)
    send_cent = send_cent.astype(jnp.bfloat16).reshape(experts, capacity, model_width)
    send_grad = jnp.dot(placing, grad_sum.astype(jnp.bfloat16), preferred_element_type=jnp.float32)
    send_grad = send_grad.astype(jnp.bfloat16).reshape(experts, capacity, model_width)
    gate_mat = gate_weight[0]
    up_mat = up_weight[0]
    down_mat = down_weight[0]
    arrived = lax.all_to_all(send_cent, "expert", split_axis=0, concat_axis=0, tiled=True)
    output, gate_act, up_act = expert_forward(
        arrived.reshape(-1, model_width), gate_mat, up_mat, down_mat
    )
    results = lax.all_to_all(
        output.reshape(experts, capacity, model_width),
        "expert",
        split_axis=0,
        concat_axis=0,
        tiled=True,
    )
    arrived_grad = lax.all_to_all(send_grad, "expert", split_axis=0, concat_axis=0, tiled=True)
    input_grad = expert_backward(
        arrived_grad.reshape(-1, model_width), gate_act, up_act, gate_mat, up_mat, down_mat
    )
    results_grad = lax.all_to_all(
        input_grad.reshape(experts, capacity, model_width),
        "expert",
        split_axis=0,
        concat_axis=0,
        tiled=True,
    )
    returned = results.reshape(-1, model_width)[slot_of]
    returned_grad = results_grad.reshape(-1, model_width)[slot_of]
    combined = jnp.sum(route_weights[:, :, None] * returned.astype(jnp.float32), axis=1)
    centroid_grad = (
        jnp.sum(route_weights[:, :, None] * returned_grad.astype(jnp.float32), axis=1) - grad_sum
    )
    layer_out = tokens.astype(jnp.float32) + jnp.take(combined - centroid, cluster_ids, axis=0)
    token_grad = out_grad.astype(jnp.float32) + jnp.take(
        centroid_grad / counts[:, None], cluster_ids, axis=0
    )
    return (layer_out, token_grad)


def pick(index, options):
    chosen = options[-1]
    for position in range(len(options) - 2, -1, -1):
        chosen = jnp.where(index == position, options[position], chosen)
    return chosen


def place(pieces, lines, like):
    slot = lax.broadcasted_iota(jnp.int32, (lines,) + (1,) * like.ndim, 0)
    stacked = jnp.zeros((lines,) + like.shape, like.dtype)
    for piece, origin in pieces:
        stacked = jnp.where(slot == origin, piece[None], stacked)
    return stacked


def topo_all_gather(shard, experts):
    lines = experts // 4
    me = lax.axis_index("expert")
    line = me // 4
    swap_row = [(j, j ^ 2) for j in range(experts)]
    here = [(shard, line)]
    there = [(lax.ppermute(shard, "expert", swap_row), line)]
    ahead, behind = shard, shard
    for step in range(1, lines):
        ahead = lax.ppermute(
            ahead,
            "expert",
            [(j, j + 4) for j in range(experts) if step - 1 <= j // 4 < lines - 1],
        )
        behind = lax.ppermute(
            behind,
            "expert",
            [(j, j - 4) for j in range(experts) if 1 <= j // 4 <= lines - step],
        )
        here.append((ahead, line - step))
        here.append((behind, line + step))
        ahead_row = [(j, j ^ 2) for j in range(experts) if j // 4 >= step]
        behind_row = [(j, j ^ 2) for j in range(experts) if j // 4 <= lines - 1 - step]
        if 2 * step > lines - 1:
            in_ahead = line >= step
            got = lax.ppermute(
                jnp.where(in_ahead, ahead, behind), "expert", sorted(ahead_row + behind_row)
            )
            origin = jnp.where(in_ahead, line - step, jnp.where(line <= lines - 1 - step, line + step, -1))
            there.append((got, origin))
        else:
            there.append((lax.ppermute(ahead, "expert", ahead_row), line - step))
            there.append((lax.ppermute(behind, "expert", behind_row), line + step))
    column = place(here, lines, shard)
    across = place(there, lines, shard)
    in_row = (me // 2) % 2
    mine = jnp.stack([pick(in_row, [column, across]), pick(in_row, [across, column])], axis=1)
    return mine.reshape((lines * 2 * shard.shape[0],) + shard.shape[1:])


def topo_reduce_scatter(blocks, experts):
    lines = experts // 4
    me = lax.axis_index("expert")
    rows = blocks.shape[0] // (2 * lines)
    plane = blocks.reshape((lines, 2, rows) + blocks.shape[1:])
    in_row = (me // 2) % 2
    keep = pick(in_row, [plane[:, 0], plane[:, 1]])
    give = pick(in_row, [plane[:, 1], plane[:, 0]])
    line = me // 4

    def row_sum(target, senders):
        mine = lax.dynamic_index_in_dim(keep, target, 0, keepdims=False)
        theirs = lax.dynamic_index_in_dim(give, target, 0, keepdims=False)
        pairs = [(j, j ^ 2) for j in range(experts) if senders(j // 4)]
        got = lax.ppermute(theirs.astype(jnp.bfloat16), "expert", pairs)
        return mine + got.astype(jnp.float32)

    if lines == 4:
        return four_line_sum(keep, give, line, row_sum)
    ahead = jnp.zeros(keep.shape[1:], jnp.float32)
    behind = jnp.zeros(keep.shape[1:], jnp.float32)
    for step in range(1, lines):
        ahead_target = jnp.clip(line + lines - step, 0, lines - 1)
        behind_target = jnp.clip(line - lines + step, 0, lines - 1)
        if 2 * step <= lines:
            in_ahead = line <= step - 1
            target = jnp.where(in_ahead, ahead_target, behind_target)
            ahead_part = row_sum(target, lambda z, s=step: z <= s - 1 or z >= lines - s)
            behind_part = ahead_part
        else:
            ahead_part = row_sum(ahead_target, lambda z, s=step: z <= s - 1)
            behind_part = row_sum(behind_target, lambda z, s=step: z >= lines - s)
        ahead = lax.ppermute(
            (ahead + ahead_part).astype(jnp.bfloat16),
            "expert",
            [(j, j + 4) for j in range(experts) if j // 4 <= step - 1],
        ).astype(jnp.float32)
        behind = lax.ppermute(
            (behind + behind_part).astype(jnp.bfloat16),
            "expert",
            [(j, j - 4) for j in range(experts) if j // 4 >= lines - step],
        ).astype(jnp.float32)
    return row_sum(line, lambda z: True) + ahead + behind


def four_line_sum(keep, give, line, row_sum):
    experts = 16
    end = (line == 0) | (line == 3)
    first = row_sum(jnp.where(end, 3 - line, line), lambda z: True)
    ahead = lax.ppermute(first.astype(jnp.bfloat16), "expert", [(j, j + 4) for j in range(4)])
    behind = lax.ppermute(first.astype(jnp.bfloat16), "expert", [(j, j - 4) for j in range(12, 16)])
    ahead, behind = ahead.astype(jnp.float32), behind.astype(jnp.float32)
    second = row_sum(jnp.where(line <= 1, line + 2, line - 2), lambda z: True)
    ahead = lax.ppermute(
        (ahead + second).astype(jnp.bfloat16), "expert", [(j, j + 4) for j in range(8)]
    ).astype(jnp.float32)
    behind = lax.ppermute(
        (behind + second).astype(jnp.bfloat16), "expert", [(j, j - 4) for j in range(8, 16)]
    ).astype(jnp.float32)
    third = row_sum(jnp.where(line <= 2, line + 1, line - 1), lambda z: True)
    fourth = row_sum(jnp.where(end, line, line - 1), lambda z: True)
    behind_part = jnp.where(line == 3, third, fourth)
    ahead = lax.ppermute(
        (ahead + third).astype(jnp.bfloat16), "expert", [(j, j + 4) for j in range(12)]
    ).astype(jnp.float32)
    behind = lax.ppermute(
        (behind + behind_part).astype(jnp.bfloat16), "expert", [(j, j - 4) for j in range(4, 16)]
    ).astype(jnp.float32)
    return jnp.where(end, fourth, first) + ahead + behind


def expert_joined(cent_in, grad_in, joined_mat, down_mat):
    hidden_width = down_mat.shape[0]
    against = (((1,), (1,)), ((), ()))
    both_act = jnp.dot(cent_in, joined_mat, preferred_element_type=jnp.float32)
    gate_act = both_act[:, :hidden_width]
    up_act = both_act[:, hidden_width:]
    sigmoid_gate = jax.nn.sigmoid(gate_act)
    hidden = (gate_act * sigmoid_gate * up_act).astype(jnp.bfloat16)
    output = jnp.dot(hidden, down_mat, preferred_element_type=jnp.float32).astype(jnp.bfloat16)
    hidden_grad = lax.dot_general(grad_in, down_mat, against, preferred_element_type=jnp.float32)
    gate_grad = (
        hidden_grad * up_act * sigmoid_gate * (1.0 + gate_act * (1.0 - sigmoid_gate))
    ).astype(jnp.bfloat16)
    up_grad = (hidden_grad * gate_act * sigmoid_gate).astype(jnp.bfloat16)
    joined_grad = jnp.concatenate([gate_grad, up_grad], axis=1)
    summed = lax.dot_general(joined_grad, joined_mat, against, preferred_element_type=jnp.float32)
    return output, summed.astype(jnp.bfloat16)


def expert_dense(cent_in, grad_in, gate_mat, up_mat, down_mat):
    against = (((1,), (1,)), ((), ()))
    gate_act = jnp.dot(cent_in, gate_mat, preferred_element_type=jnp.float32)
    up_act = jnp.dot(cent_in, up_mat, preferred_element_type=jnp.float32)
    sigmoid_gate = jax.nn.sigmoid(gate_act)
    hidden = (gate_act * sigmoid_gate * up_act).astype(jnp.bfloat16)
    output = jnp.dot(hidden, down_mat, preferred_element_type=jnp.float32).astype(jnp.bfloat16)
    hidden_grad = lax.dot_general(grad_in, down_mat, against, preferred_element_type=jnp.float32)
    gate_grad = (
        hidden_grad * up_act * sigmoid_gate * (1.0 + gate_act * (1.0 - sigmoid_gate))
    ).astype(jnp.bfloat16)
    up_grad = (hidden_grad * gate_act * sigmoid_gate).astype(jnp.bfloat16)
    summed = lax.dot_general(gate_grad, gate_mat, against, preferred_element_type=jnp.float32)
    summed = summed + lax.dot_general(up_grad, up_mat, against, preferred_element_type=jnp.float32)
    return output, summed.astype(jnp.bfloat16)


def per_device_dense(
    tokens, out_grad, cluster_ids, routes, route_weights, gate_weight, up_weight, down_weight
):
    cent_rows = routes.shape[0]
    me = lax.axis_index("expert")
    member = (cluster_ids[:, None] == jnp.arange(cent_rows, dtype=jnp.int32)[None, :]).astype(
        jnp.bfloat16
    )
    counts = jnp.sum(member.astype(jnp.float32), axis=0)
    contract = (((0,), (0,)), ((), ()))
    model_width = tokens.shape[1]
    sums = lax.dot_general(
        member,
        jnp.concatenate([tokens, out_grad], axis=1),
        contract,
        preferred_element_type=jnp.float32,
    )
    centroid = sums[:, :model_width] / counts[:, None]
    grad_sum = sums[:, model_width:]
    experts = lax.axis_size("expert")
    model_width = tokens.shape[1]
    picked = routes[:, :, None] == jnp.arange(experts, dtype=jnp.int32)[None, None, :]
    per_expert = jnp.sum(jnp.where(picked, route_weights[:, :, None], 0.0), axis=1)
    weight_hi = per_expert.astype(jnp.bfloat16)
    weight_lo = (per_expert - weight_hi.astype(jnp.float32)).astype(jnp.bfloat16)
    side = jnp.concatenate([weight_hi, weight_lo], axis=1)
    side_width = -(-side.shape[1] // 128) * 128
    side = jnp.pad(side, ((0, 0), (0, side_width - side.shape[1])))
    payload = jnp.concatenate(
        [centroid.astype(jnp.bfloat16), grad_sum.astype(jnp.bfloat16), side], axis=1
    )
    gathered = topo_all_gather(payload, experts)
    cent_all = gathered[:, :model_width]
    grad_all = gathered[:, model_width : 2 * model_width]
    side_all = gathered[:, 2 * model_width : 2 * model_width + 2 * experts].astype(jnp.float32)
    column = jnp.arange(experts, dtype=jnp.int32)[None, :]
    summed_side = side_all[:, :experts] + side_all[:, experts:]
    mine = jnp.sum(jnp.where(column == me, summed_side, 0.0), axis=1)
    other = jnp.sum(jnp.where(column == (me ^ 1), summed_side, 0.0), axis=1)
    swap_core = [(j, j ^ 1) for j in range(experts)]
    gate_mat, up_mat, down_mat = gate_weight[0], up_weight[0], down_weight[0]
    joined_mat = jnp.concatenate([gate_mat, up_mat], axis=1)
    joined_pair = lax.ppermute(joined_mat, "expert", swap_core)
    down_pair = lax.ppermute(down_mat, "expert", swap_core)
    output, input_grad = expert_joined(cent_all, grad_all, joined_mat, down_mat)
    output_pair, input_grad_pair = expert_joined(cent_all, grad_all, joined_pair, down_pair)
    weighted_out = mine[:, None] * output.astype(jnp.float32) + other[:, None] * output_pair.astype(
        jnp.float32
    )
    weighted_grad = mine[:, None] * input_grad.astype(jnp.float32) + other[
        :, None
    ] * input_grad_pair.astype(jnp.float32)
    summed = topo_reduce_scatter(jnp.concatenate([weighted_out, weighted_grad], axis=1), experts)
    combined = summed[:, :model_width]
    centroid_grad = summed[:, model_width:] - grad_sum
    layer_out = tokens.astype(jnp.float32) + jnp.take(combined - centroid, cluster_ids, axis=0)
    token_grad = out_grad.astype(jnp.float32) + jnp.take(
        centroid_grad / counts[:, None], cluster_ids, axis=0
    )
    return (layer_out, token_grad)


def per_device(*args):
    routes = args[3]
    cent_rows, fanout = routes.shape
    experts = lax.axis_size("expert")
    capacity = min(cent_rows, 2 * cent_rows * fanout // experts)
    if capacity == cent_rows and experts % 4 == 0:
        return per_device_dense(*args)
    return per_device_slots(*args)


def solution(mesh):
    placed = (
        P(("groups", "expert"), None),
        P(("groups", "expert"), None),
        P(("groups", "expert")),
        P(("groups", "expert"), None),
        P(("groups", "expert"), None),
        P("expert", None, None),
        P("expert", None, None),
        P("expert", None, None),
    )
    return jax.shard_map(
        per_device,
        mesh=mesh,
        in_specs=placed,
        out_specs=(P(("groups", "expert"), None), P(("groups", "expert"), None)),
        check_vma=False,
    )
```

```python
import jax
import jax.numpy as jnp
from jax import lax
from jax.sharding import PartitionSpec as P


def expert_forward(inputs, gate_mat, up_mat, down_mat):
    gate_act = jnp.dot(inputs, gate_mat, preferred_element_type=jnp.float32)
    up_act = jnp.dot(inputs, up_mat, preferred_element_type=jnp.float32)
    sigmoid_gate = jax.nn.sigmoid(gate_act)
    hidden = (gate_act * sigmoid_gate * up_act).astype(jnp.bfloat16)
    output = jnp.dot(hidden, down_mat, preferred_element_type=jnp.float32).astype(jnp.bfloat16)
    return (output, gate_act, up_act)


def expert_backward(incoming, gate_act, up_act, gate_mat, up_mat, down_mat):
    against = (((1,), (1,)), ((), ()))
    hidden_grad = lax.dot_general(incoming, down_mat, against, preferred_element_type=jnp.float32)
    sigmoid_gate = jax.nn.sigmoid(gate_act)
    gate_grad = (
        hidden_grad * up_act * sigmoid_gate * (1.0 + gate_act * (1.0 - sigmoid_gate))
    ).astype(jnp.bfloat16)
    up_grad = (hidden_grad * gate_act * sigmoid_gate).astype(jnp.bfloat16)
    summed = lax.dot_general(gate_grad, gate_mat, against, preferred_element_type=jnp.float32)
    summed = summed + lax.dot_general(up_grad, up_mat, against, preferred_element_type=jnp.float32)
    return summed.astype(jnp.bfloat16)


def per_device_slots(
    tokens, out_grad, cluster_ids, routes, route_weights, gate_weight, up_weight, down_weight
):
    model_width = tokens.shape[1]
    cent_rows = routes.shape[0]
    fanout = routes.shape[1]
    experts = lax.axis_size("expert")
    capacity = min(cent_rows, 2 * cent_rows * fanout // experts)
    member = (cluster_ids[:, None] == jnp.arange(cent_rows, dtype=jnp.int32)[None, :]).astype(
        jnp.bfloat16
    )
    counts = jnp.sum(member.astype(jnp.float32), axis=0)
    contract = (((0,), (0,)), ((), ()))
    centroid = (
        lax.dot_general(member, tokens, contract, preferred_element_type=jnp.float32)
        / counts[:, None]
    )
    grad_sum = lax.dot_general(member, out_grad, contract, preferred_element_type=jnp.float32)
    pair_ids = routes.reshape(-1)
    matches = (pair_ids[:, None] == jnp.arange(experts, dtype=jnp.int32)[None, :]).astype(jnp.int32)
    earlier = jnp.cumsum(matches, axis=0) - matches
    position = jnp.sum(earlier * matches, axis=1)
    slot_of = (pair_ids * capacity + position).reshape(cent_rows, fanout)
    slot_range = jnp.arange(experts * capacity, dtype=jnp.int32)
    placing = jnp.any(slot_of[None, :, :] == slot_range[:, None, None], axis=2).astype(jnp.bfloat16)
    send_cent = jnp.dot(placing, centroid.astype(jnp.bfloat16), preferred_element_type=jnp.float32)
    send_cent = send_cent.astype(jnp.bfloat16).reshape(experts, capacity, model_width)
    send_grad = jnp.dot(placing, grad_sum.astype(jnp.bfloat16), preferred_element_type=jnp.float32)
    send_grad = send_grad.astype(jnp.bfloat16).reshape(experts, capacity, model_width)
    gate_mat = gate_weight[0]
    up_mat = up_weight[0]
    down_mat = down_weight[0]
    arrived = lax.all_to_all(send_cent, "expert", split_axis=0, concat_axis=0, tiled=True)
    output, gate_act, up_act = expert_forward(
        arrived.reshape(-1, model_width), gate_mat, up_mat, down_mat
    )
    results = lax.all_to_all(
        output.reshape(experts, capacity, model_width),
        "expert",
        split_axis=0,
        concat_axis=0,
        tiled=True,
    )
    arrived_grad = lax.all_to_all(send_grad, "expert", split_axis=0, concat_axis=0, tiled=True)
    input_grad = expert_backward(
        arrived_grad.reshape(-1, model_width), gate_act, up_act, gate_mat, up_mat, down_mat
    )
    results_grad = lax.all_to_all(
        input_grad.reshape(experts, capacity, model_width),
        "expert",
        split_axis=0,
        concat_axis=0,
        tiled=True,
    )
    returned = results.reshape(-1, model_width)[slot_of]
    returned_grad = results_grad.reshape(-1, model_width)[slot_of]
    combined = jnp.sum(route_weights[:, :, None] * returned.astype(jnp.float32), axis=1)
    centroid_grad = (
        jnp.sum(route_weights[:, :, None] * returned_grad.astype(jnp.float32), axis=1) - grad_sum
    )
    layer_out = tokens.astype(jnp.float32) + jnp.take(combined - centroid, cluster_ids, axis=0)
    token_grad = out_grad.astype(jnp.float32) + jnp.take(
        centroid_grad / counts[:, None], cluster_ids, axis=0
    )
    return (layer_out, token_grad)


def pick(index, options):
    chosen = options[-1]
    for position in range(len(options) - 2, -1, -1):
        chosen = jnp.where(index == position, options[position], chosen)
    return chosen


def place(pieces, lines, like):
    slot = lax.broadcasted_iota(jnp.int32, (lines,) + (1,) * like.ndim, 0)
    stacked = jnp.zeros((lines,) + like.shape, like.dtype)
    for piece, origin in pieces:
        stacked = jnp.where(slot == origin, piece[None], stacked)
    return stacked


def topo_all_gather(shard, experts):
    lines = experts // 4
    me = lax.axis_index("expert")
    line = me // 4
    swap_row = [(j, j ^ 2) for j in range(experts)]
    here = [(shard, line)]
    there = [(lax.ppermute(shard, "expert", swap_row), line)]
    ahead, behind = shard, shard
    for step in range(1, lines):
        ahead = lax.ppermute(
            ahead,
            "expert",
            [(j, j + 4) for j in range(experts) if step - 1 <= j // 4 < lines - 1],
        )
        behind = lax.ppermute(
            behind,
            "expert",
            [(j, j - 4) for j in range(experts) if 1 <= j // 4 <= lines - step],
        )
        here.append((ahead, line - step))
        here.append((behind, line + step))
        ahead_row = [(j, j ^ 2) for j in range(experts) if j // 4 >= step]
        behind_row = [(j, j ^ 2) for j in range(experts) if j // 4 <= lines - 1 - step]
        if 2 * step > lines - 1:
            in_ahead = line >= step
            got = lax.ppermute(
                jnp.where(in_ahead, ahead, behind), "expert", sorted(ahead_row + behind_row)
            )
            origin = jnp.where(in_ahead, line - step, jnp.where(line <= lines - 1 - step, line + step, -1))
            there.append((got, origin))
        else:
            there.append((lax.ppermute(ahead, "expert", ahead_row), line - step))
            there.append((lax.ppermute(behind, "expert", behind_row), line + step))
    both = jnp.stack([place(here, lines, shard), place(there, lines, shard)])
    return both.reshape((lines * 2 * shard.shape[0],) + shard.shape[1:])


def topo_reduce_scatter(blocks, experts):
    lines = experts // 4
    me = lax.axis_index("expert")
    rows = blocks.shape[0] // (2 * lines)
    plane = blocks.reshape((2, lines, rows) + blocks.shape[1:])
    keep = plane[0]
    give = plane[1]
    line = me // 4

    def row_sum(target, senders):
        mine = lax.dynamic_index_in_dim(keep, target, 0, keepdims=False)
        theirs = lax.dynamic_index_in_dim(give, target, 0, keepdims=False)
        pairs = [(j, j ^ 2) for j in range(experts) if senders(j // 4)]
        got = lax.ppermute(theirs.astype(jnp.bfloat16), "expert", pairs)
        return mine + got.astype(jnp.float32)

    if lines == 4:
        return four_line_sum(keep, give, line, row_sum)
    ahead = jnp.zeros(keep.shape[1:], jnp.float32)
    behind = jnp.zeros(keep.shape[1:], jnp.float32)
    for step in range(1, lines):
        ahead_target = jnp.clip(line + lines - step, 0, lines - 1)
        behind_target = jnp.clip(line - lines + step, 0, lines - 1)
        if 2 * step <= lines:
            in_ahead = line <= step - 1
            target = jnp.where(in_ahead, ahead_target, behind_target)
            ahead_part = row_sum(target, lambda z, s=step: z <= s - 1 or z >= lines - s)
            behind_part = ahead_part
        else:
            ahead_part = row_sum(ahead_target, lambda z, s=step: z <= s - 1)
            behind_part = row_sum(behind_target, lambda z, s=step: z >= lines - s)
        ahead = lax.ppermute(
            (ahead + ahead_part).astype(jnp.bfloat16),
            "expert",
            [(j, j + 4) for j in range(experts) if j // 4 <= step - 1],
        ).astype(jnp.float32)
        behind = lax.ppermute(
            (behind + behind_part).astype(jnp.bfloat16),
            "expert",
            [(j, j - 4) for j in range(experts) if j // 4 >= lines - step],
        ).astype(jnp.float32)
    return row_sum(line, lambda z: True) + ahead + behind


def four_line_sum(keep, give, line, row_sum):
    experts = 16
    end = (line == 0) | (line == 3)
    first = row_sum(jnp.where(end, 3 - line, line), lambda z: True)
    ahead = lax.ppermute(first.astype(jnp.bfloat16), "expert", [(j, j + 4) for j in range(4)])
    behind = lax.ppermute(first.astype(jnp.bfloat16), "expert", [(j, j - 4) for j in range(12, 16)])
    ahead, behind = ahead.astype(jnp.float32), behind.astype(jnp.float32)
    second = row_sum(jnp.where(line <= 1, line + 2, line - 2), lambda z: True)
    ahead = lax.ppermute(
        (ahead + second).astype(jnp.bfloat16), "expert", [(j, j + 4) for j in range(8)]
    ).astype(jnp.float32)
    behind = lax.ppermute(
        (behind + second).astype(jnp.bfloat16), "expert", [(j, j - 4) for j in range(8, 16)]
    ).astype(jnp.float32)
    third = row_sum(jnp.where(line <= 2, line + 1, line - 1), lambda z: True)
    fourth = row_sum(jnp.where(end, line, line - 1), lambda z: True)
    behind_part = jnp.where(line == 3, third, fourth)
    ahead = lax.ppermute(
        (ahead + third).astype(jnp.bfloat16), "expert", [(j, j + 4) for j in range(12)]
    ).astype(jnp.float32)
    behind = lax.ppermute(
        (behind + behind_part).astype(jnp.bfloat16), "expert", [(j, j - 4) for j in range(4, 16)]
    ).astype(jnp.float32)
    return jnp.where(end, fourth, first) + ahead + behind


def expert_dense(cent_in, grad_in, gate_mat, up_mat, down_mat):
    against = (((1,), (1,)), ((), ()))
    gate_act = jnp.dot(cent_in, gate_mat, preferred_element_type=jnp.float32)
    up_act = jnp.dot(cent_in, up_mat, preferred_element_type=jnp.float32)
    sigmoid_gate = jax.nn.sigmoid(gate_act)
    hidden = (gate_act * sigmoid_gate * up_act).astype(jnp.bfloat16)
    output = jnp.dot(hidden, down_mat, preferred_element_type=jnp.float32).astype(jnp.bfloat16)
    hidden_grad = lax.dot_general(grad_in, down_mat, against, preferred_element_type=jnp.float32)
    gate_grad = (
        hidden_grad * up_act * sigmoid_gate * (1.0 + gate_act * (1.0 - sigmoid_gate))
    ).astype(jnp.bfloat16)
    up_grad = (hidden_grad * gate_act * sigmoid_gate).astype(jnp.bfloat16)
    summed = lax.dot_general(gate_grad, gate_mat, against, preferred_element_type=jnp.float32)
    summed = summed + lax.dot_general(up_grad, up_mat, against, preferred_element_type=jnp.float32)
    return output, summed.astype(jnp.bfloat16)


def per_device_dense(
    tokens, out_grad, cluster_ids, routes, route_weights, gate_weight, up_weight, down_weight
):
    cent_rows = routes.shape[0]
    me = lax.axis_index("expert")
    member = (cluster_ids[:, None] == jnp.arange(cent_rows, dtype=jnp.int32)[None, :]).astype(
        jnp.bfloat16
    )
    counts = jnp.sum(member.astype(jnp.float32), axis=0)
    contract = (((0,), (0,)), ((), ()))
    model_width = tokens.shape[1]
    sums = lax.dot_general(
        member,
        jnp.concatenate([tokens, out_grad], axis=1),
        contract,
        preferred_element_type=jnp.float32,
    )
    centroid = sums[:, :model_width] / counts[:, None]
    grad_sum = sums[:, model_width:]
    experts = lax.axis_size("expert")
    model_width = tokens.shape[1]
    picked = routes[:, :, None] == jnp.arange(experts, dtype=jnp.int32)[None, None, :]
    per_expert = jnp.sum(jnp.where(picked, route_weights[:, :, None], 0.0), axis=1)
    weight_hi = per_expert.astype(jnp.bfloat16)
    weight_lo = (per_expert - weight_hi.astype(jnp.float32)).astype(jnp.bfloat16)
    side = jnp.concatenate([weight_hi, weight_lo], axis=1)
    side_width = -(-side.shape[1] // 128) * 128
    side = jnp.pad(side, ((0, 0), (0, side_width - side.shape[1])))
    payload = jnp.concatenate(
        [centroid.astype(jnp.bfloat16), grad_sum.astype(jnp.bfloat16), side], axis=1
    )
    gathered = topo_all_gather(payload, experts)
    cent_all = gathered[:, :model_width]
    grad_all = gathered[:, model_width : 2 * model_width]
    side_all = gathered[:, 2 * model_width : 2 * model_width + 2 * experts].astype(jnp.float32)
    column = jnp.arange(experts, dtype=jnp.int32)[None, :]
    summed_side = side_all[:, :experts] + side_all[:, experts:]
    mine = jnp.sum(jnp.where(column == me, summed_side, 0.0), axis=1)
    other = jnp.sum(jnp.where(column == (me ^ 1), summed_side, 0.0), axis=1)
    swap_core = [(j, j ^ 1) for j in range(experts)]
    gate_mat, up_mat, down_mat = gate_weight[0], up_weight[0], down_weight[0]
    gate_pair = lax.ppermute(gate_mat, "expert", swap_core)
    up_pair = lax.ppermute(up_mat, "expert", swap_core)
    down_pair = lax.ppermute(down_mat, "expert", swap_core)
    output, input_grad = expert_dense(cent_all, grad_all, gate_mat, up_mat, down_mat)
    output_pair, input_grad_pair = expert_dense(cent_all, grad_all, gate_pair, up_pair, down_pair)
    weighted_out = mine[:, None] * output.astype(jnp.float32) + other[:, None] * output_pair.astype(
        jnp.float32
    )
    weighted_grad = mine[:, None] * input_grad.astype(jnp.float32) + other[
        :, None
    ] * input_grad_pair.astype(jnp.float32)
    summed = topo_reduce_scatter(jnp.concatenate([weighted_out, weighted_grad], axis=1), experts)
    combined = summed[:, :model_width]
    centroid_grad = summed[:, model_width:] - grad_sum
    layer_out = tokens.astype(jnp.float32) + jnp.take(combined - centroid, cluster_ids, axis=0)
    token_grad = out_grad.astype(jnp.float32) + jnp.take(
        centroid_grad / counts[:, None], cluster_ids, axis=0
    )
    return (layer_out, token_grad)


def per_device(*args):
    routes = args[3]
    cent_rows, fanout = routes.shape
    experts = lax.axis_size("expert")
    capacity = min(cent_rows, 2 * cent_rows * fanout // experts)
    if capacity == cent_rows and experts % 4 == 0:
        return per_device_dense(*args)
    return per_device_slots(*args)


def solution(mesh):
    placed = (
        P(("groups", "expert"), None),
        P(("groups", "expert"), None),
        P(("groups", "expert")),
        P(("groups", "expert"), None),
        P(("groups", "expert"), None),
        P("expert", None, None),
        P("expert", None, None),
        P("expert", None, None),
    )
    return jax.shard_map(
        per_device,
        mesh=mesh,
        in_specs=placed,
        out_specs=(P(("groups", "expert"), None), P(("groups", "expert"), None)),
        check_vma=False,
    )
```

```python
import jax
import jax.numpy as jnp
from jax import lax
from jax.sharding import PartitionSpec as P


def expert_forward(inputs, gate_mat, up_mat, down_mat):
    gate_act = jnp.dot(inputs, gate_mat, preferred_element_type=jnp.float32)
    up_act = jnp.dot(inputs, up_mat, preferred_element_type=jnp.float32)
    sigmoid_gate = jax.nn.sigmoid(gate_act)
    hidden = (gate_act * sigmoid_gate * up_act).astype(jnp.bfloat16)
    output = jnp.dot(hidden, down_mat, preferred_element_type=jnp.float32).astype(jnp.bfloat16)
    return (output, gate_act, up_act)


def expert_backward(incoming, gate_act, up_act, gate_mat, up_mat, down_mat):
    against = (((1,), (1,)), ((), ()))
    hidden_grad = lax.dot_general(incoming, down_mat, against, preferred_element_type=jnp.float32)
    sigmoid_gate = jax.nn.sigmoid(gate_act)
    gate_grad = (
        hidden_grad * up_act * sigmoid_gate * (1.0 + gate_act * (1.0 - sigmoid_gate))
    ).astype(jnp.bfloat16)
    up_grad = (hidden_grad * gate_act * sigmoid_gate).astype(jnp.bfloat16)
    summed = lax.dot_general(gate_grad, gate_mat, against, preferred_element_type=jnp.float32)
    summed = summed + lax.dot_general(up_grad, up_mat, against, preferred_element_type=jnp.float32)
    return summed.astype(jnp.bfloat16)


def per_device_slots(
    tokens, out_grad, cluster_ids, routes, route_weights, gate_weight, up_weight, down_weight
):
    model_width = tokens.shape[1]
    cent_rows = routes.shape[0]
    fanout = routes.shape[1]
    experts = lax.axis_size("expert")
    capacity = min(cent_rows, 2 * cent_rows * fanout // experts)
    member = (cluster_ids[:, None] == jnp.arange(cent_rows, dtype=jnp.int32)[None, :]).astype(
        jnp.bfloat16
    )
    counts = jnp.sum(member.astype(jnp.float32), axis=0)
    contract = (((0,), (0,)), ((), ()))
    centroid = (
        lax.dot_general(member, tokens, contract, preferred_element_type=jnp.float32)
        / counts[:, None]
    )
    grad_sum = lax.dot_general(member, out_grad, contract, preferred_element_type=jnp.float32)
    pair_ids = routes.reshape(-1)
    matches = (pair_ids[:, None] == jnp.arange(experts, dtype=jnp.int32)[None, :]).astype(jnp.int32)
    earlier = jnp.cumsum(matches, axis=0) - matches
    position = jnp.sum(earlier * matches, axis=1)
    slot_of = (pair_ids * capacity + position).reshape(cent_rows, fanout)
    slot_range = jnp.arange(experts * capacity, dtype=jnp.int32)
    placing = jnp.any(slot_of[None, :, :] == slot_range[:, None, None], axis=2).astype(jnp.bfloat16)
    send_cent = jnp.dot(placing, centroid.astype(jnp.bfloat16), preferred_element_type=jnp.float32)
    send_cent = send_cent.astype(jnp.bfloat16).reshape(experts, capacity, model_width)
    send_grad = jnp.dot(placing, grad_sum.astype(jnp.bfloat16), preferred_element_type=jnp.float32)
    send_grad = send_grad.astype(jnp.bfloat16).reshape(experts, capacity, model_width)
    gate_mat = gate_weight[0]
    up_mat = up_weight[0]
    down_mat = down_weight[0]
    arrived = lax.all_to_all(send_cent, "expert", split_axis=0, concat_axis=0, tiled=True)
    output, gate_act, up_act = expert_forward(
        arrived.reshape(-1, model_width), gate_mat, up_mat, down_mat
    )
    results = lax.all_to_all(
        output.reshape(experts, capacity, model_width),
        "expert",
        split_axis=0,
        concat_axis=0,
        tiled=True,
    )
    arrived_grad = lax.all_to_all(send_grad, "expert", split_axis=0, concat_axis=0, tiled=True)
    input_grad = expert_backward(
        arrived_grad.reshape(-1, model_width), gate_act, up_act, gate_mat, up_mat, down_mat
    )
    results_grad = lax.all_to_all(
        input_grad.reshape(experts, capacity, model_width),
        "expert",
        split_axis=0,
        concat_axis=0,
        tiled=True,
    )
    returned = results.reshape(-1, model_width)[slot_of]
    returned_grad = results_grad.reshape(-1, model_width)[slot_of]
    combined = jnp.sum(route_weights[:, :, None] * returned.astype(jnp.float32), axis=1)
    centroid_grad = (
        jnp.sum(route_weights[:, :, None] * returned_grad.astype(jnp.float32), axis=1) - grad_sum
    )
    layer_out = tokens.astype(jnp.float32) + jnp.take(combined - centroid, cluster_ids, axis=0)
    token_grad = out_grad.astype(jnp.float32) + jnp.take(
        centroid_grad / counts[:, None], cluster_ids, axis=0
    )
    return (layer_out, token_grad)


def pick(index, options):
    chosen = options[-1]
    for position in range(len(options) - 2, -1, -1):
        chosen = jnp.where(index == position, options[position], chosen)
    return chosen


def place(pieces, lines, like):
    slot = lax.broadcasted_iota(jnp.int32, (lines,) + (1,) * like.ndim, 0)
    stacked = jnp.zeros((lines,) + like.shape, like.dtype)
    for piece, origin in pieces:
        stacked = jnp.where(slot == origin, piece[None], stacked)
    return stacked


def topo_all_gather(shard, experts):
    lines = experts // 4
    me = lax.axis_index("expert")
    line = me // 4
    swap_row = [(j, j ^ 2) for j in range(experts)]
    here = [(shard, line)]
    there = [(lax.ppermute(shard, "expert", swap_row), line)]
    ahead, behind = shard, shard
    for step in range(1, lines):
        ahead = lax.ppermute(
            ahead,
            "expert",
            [(j, j + 4) for j in range(experts) if step - 1 <= j // 4 < lines - 1],
        )
        behind = lax.ppermute(
            behind,
            "expert",
            [(j, j - 4) for j in range(experts) if 1 <= j // 4 <= lines - step],
        )
        here.append((ahead, line - step))
        here.append((behind, line + step))
        ahead_row = [(j, j ^ 2) for j in range(experts) if j // 4 >= step]
        behind_row = [(j, j ^ 2) for j in range(experts) if j // 4 <= lines - 1 - step]
        if 2 * step > lines - 1:
            in_ahead = line >= step
            got = lax.ppermute(
                jnp.where(in_ahead, ahead, behind), "expert", sorted(ahead_row + behind_row)
            )
            origin = jnp.where(in_ahead, line - step, jnp.where(line <= lines - 1 - step, line + step, -1))
            there.append((got, origin))
        else:
            there.append((lax.ppermute(ahead, "expert", ahead_row), line - step))
            there.append((lax.ppermute(behind, "expert", behind_row), line + step))
    both = jnp.stack([place(here, lines, shard), place(there, lines, shard)])
    return both.reshape((lines * 2 * shard.shape[0],) + shard.shape[1:])


def topo_reduce_scatter(blocks, experts):
    lines = experts // 4
    me = lax.axis_index("expert")
    rows = blocks.shape[0] // (2 * lines)
    plane = blocks.reshape((2, lines, rows) + blocks.shape[1:])
    keep = plane[0]
    give = plane[1]
    line = me // 4

    def row_sum(target, senders):
        mine = lax.dynamic_index_in_dim(keep, target, 0, keepdims=False)
        theirs = lax.dynamic_index_in_dim(give, target, 0, keepdims=False)
        pairs = [(j, j ^ 2) for j in range(experts) if senders(j // 4)]
        got = lax.ppermute(theirs.astype(jnp.bfloat16), "expert", pairs)
        return mine + got.astype(jnp.float32)

    if lines == 4:
        return four_line_sum(keep, give, line, row_sum)
    ahead = jnp.zeros(keep.shape[1:], jnp.float32)
    behind = jnp.zeros(keep.shape[1:], jnp.float32)
    for step in range(1, lines):
        ahead_target = jnp.clip(line + lines - step, 0, lines - 1)
        behind_target = jnp.clip(line - lines + step, 0, lines - 1)
        if 2 * step <= lines:
            in_ahead = line <= step - 1
            target = jnp.where(in_ahead, ahead_target, behind_target)
            ahead_part = row_sum(target, lambda z, s=step: z <= s - 1 or z >= lines - s)
            behind_part = ahead_part
        else:
            ahead_part = row_sum(ahead_target, lambda z, s=step: z <= s - 1)
            behind_part = row_sum(behind_target, lambda z, s=step: z >= lines - s)
        ahead = lax.ppermute(
            (ahead + ahead_part).astype(jnp.bfloat16),
            "expert",
            [(j, j + 4) for j in range(experts) if j // 4 <= step - 1],
        ).astype(jnp.float32)
        behind = lax.ppermute(
            (behind + behind_part).astype(jnp.bfloat16),
            "expert",
            [(j, j - 4) for j in range(experts) if j // 4 >= lines - step],
        ).astype(jnp.float32)
    return row_sum(line, lambda z: True) + ahead + behind


def four_line_sum(keep, give, line, row_sum):
    experts = 16
    end = (line == 0) | (line == 3)
    first = row_sum(jnp.where(end, 3 - line, line), lambda z: True)
    ahead = lax.ppermute(first.astype(jnp.bfloat16), "expert", [(j, j + 4) for j in range(4)])
    behind = lax.ppermute(first.astype(jnp.bfloat16), "expert", [(j, j - 4) for j in range(12, 16)])
    ahead, behind = ahead.astype(jnp.float32), behind.astype(jnp.float32)
    second = row_sum(jnp.where(line <= 1, line + 2, line - 2), lambda z: True)
    ahead = lax.ppermute(
        (ahead + second).astype(jnp.bfloat16), "expert", [(j, j + 4) for j in range(8)]
    ).astype(jnp.float32)
    behind = lax.ppermute(
        (behind + second).astype(jnp.bfloat16), "expert", [(j, j - 4) for j in range(8, 16)]
    ).astype(jnp.float32)
    third = row_sum(jnp.where(line <= 2, line + 1, line - 1), lambda z: True)
    fourth = row_sum(jnp.where(end, line, line - 1), lambda z: True)
    behind_part = jnp.where(line == 3, third, fourth)
    ahead = lax.ppermute(
        (ahead + third).astype(jnp.bfloat16), "expert", [(j, j + 4) for j in range(12)]
    ).astype(jnp.float32)
    behind = lax.ppermute(
        (behind + behind_part).astype(jnp.bfloat16), "expert", [(j, j - 4) for j in range(4, 16)]
    ).astype(jnp.float32)
    return jnp.where(end, fourth, first) + ahead + behind


def expert_dense(cent_in, grad_in, gate_mat, up_mat, down_mat):
    against = (((1,), (1,)), ((), ()))
    gate_act = jnp.dot(cent_in, gate_mat, preferred_element_type=jnp.float32)
    up_act = jnp.dot(cent_in, up_mat, preferred_element_type=jnp.float32)
    sigmoid_gate = jax.nn.sigmoid(gate_act)
    hidden = (gate_act * sigmoid_gate * up_act).astype(jnp.bfloat16)
    output = jnp.dot(hidden, down_mat, preferred_element_type=jnp.float32).astype(jnp.bfloat16)
    hidden_grad = lax.dot_general(grad_in, down_mat, against, preferred_element_type=jnp.float32)
    gate_grad = (
        hidden_grad * up_act * sigmoid_gate * (1.0 + gate_act * (1.0 - sigmoid_gate))
    ).astype(jnp.bfloat16)
    up_grad = (hidden_grad * gate_act * sigmoid_gate).astype(jnp.bfloat16)
    summed = lax.dot_general(gate_grad, gate_mat, against, preferred_element_type=jnp.float32)
    summed = summed + lax.dot_general(up_grad, up_mat, against, preferred_element_type=jnp.float32)
    return output, summed.astype(jnp.bfloat16)


def per_device_dense(
    tokens, out_grad, cluster_ids, routes, route_weights, gate_weight, up_weight, down_weight
):
    cent_rows = routes.shape[0]
    me = lax.axis_index("expert")
    member = (cluster_ids[:, None] == jnp.arange(cent_rows, dtype=jnp.int32)[None, :]).astype(
        jnp.bfloat16
    )
    counts = jnp.sum(member.astype(jnp.float32), axis=0)
    contract = (((0,), (0,)), ((), ()))
    model_width = tokens.shape[1]
    sums = lax.dot_general(
        member,
        jnp.concatenate([tokens, out_grad], axis=1),
        contract,
        preferred_element_type=jnp.float32,
    )
    centroid = sums[:, :model_width] / counts[:, None]
    grad_sum = sums[:, model_width:]
    experts = lax.axis_size("expert")
    model_width = tokens.shape[1]
    picked = routes[:, :, None] == jnp.arange(experts, dtype=jnp.int32)[None, None, :]
    per_expert = jnp.sum(jnp.where(picked, route_weights[:, :, None], 0.0), axis=1)
    weight_hi = per_expert.astype(jnp.bfloat16)
    weight_lo = (per_expert - weight_hi.astype(jnp.float32)).astype(jnp.bfloat16)
    side = jnp.concatenate([weight_hi, weight_lo], axis=1)
    side_width = -(-side.shape[1] // 128) * 128
    side = jnp.pad(side, ((0, 0), (0, side_width - side.shape[1])))
    payload = jnp.concatenate(
        [centroid.astype(jnp.bfloat16), grad_sum.astype(jnp.bfloat16), side], axis=1
    )
    gathered = topo_all_gather(payload, experts)
    cent_all = gathered[:, :model_width]
    grad_all = gathered[:, model_width : 2 * model_width]
    side_all = gathered[:, 2 * model_width : 2 * model_width + 2 * experts].astype(jnp.float32)
    column = jnp.arange(experts, dtype=jnp.int32)[None, :]
    summed_side = side_all[:, :experts] + side_all[:, experts:]
    mine = jnp.sum(jnp.where(column == me, summed_side, 0.0), axis=1)
    other = jnp.sum(jnp.where(column == (me ^ 1), summed_side, 0.0), axis=1)
    swap_core = [(j, j ^ 1) for j in range(experts)]
    gate_mat, up_mat, down_mat = gate_weight[0], up_weight[0], down_weight[0]
    gate_pair = lax.ppermute(gate_mat, "expert", swap_core)
    up_pair = lax.ppermute(up_mat, "expert", swap_core)
    down_pair = lax.ppermute(down_mat, "expert", swap_core)
    output, input_grad = expert_dense(cent_all, grad_all, gate_mat, up_mat, down_mat)
    output_pair, input_grad_pair = expert_dense(cent_all, grad_all, gate_pair, up_pair, down_pair)
    weighted_out = mine[:, None] * output.astype(jnp.float32) + other[:, None] * output_pair.astype(
        jnp.float32
    )
    weighted_grad = mine[:, None] * input_grad.astype(jnp.float32) + other[
        :, None
    ] * input_grad_pair.astype(jnp.float32)
    summed = topo_reduce_scatter(jnp.concatenate([weighted_out, weighted_grad], axis=1), experts)
    combined = summed[:, :model_width]
    centroid_grad = summed[:, model_width:] - grad_sum
    table = jnp.concatenate([combined - centroid, centroid_grad / counts[:, None]], axis=1)
    spread = jnp.dot(member.astype(jnp.float32), table, precision=lax.Precision.HIGHEST)
    layer_out = tokens.astype(jnp.float32) + spread[:, :model_width]
    token_grad = out_grad.astype(jnp.float32) + spread[:, model_width:]
    return (layer_out, token_grad)


def per_device(*args):
    routes = args[3]
    cent_rows, fanout = routes.shape
    experts = lax.axis_size("expert")
    capacity = min(cent_rows, 2 * cent_rows * fanout // experts)
    if capacity == cent_rows and experts % 4 == 0:
        return per_device_dense(*args)
    return per_device_slots(*args)


def solution(mesh):
    placed = (
        P(("groups", "expert"), None),
        P(("groups", "expert"), None),
        P(("groups", "expert")),
        P(("groups", "expert"), None),
        P(("groups", "expert"), None),
        P("expert", None, None),
        P("expert", None, None),
        P("expert", None, None),
    )
    return jax.shard_map(
        per_device,
        mesh=mesh,
        in_specs=placed,
        out_specs=(P(("groups", "expert"), None), P(("groups", "expert"), None)),
        check_vma=False,
    )
```

```python
import jax
import jax.numpy as jnp
from jax import lax
from jax.sharding import PartitionSpec as P


def expert_forward(inputs, gate_mat, up_mat, down_mat):
    gate_act = jnp.dot(inputs, gate_mat, preferred_element_type=jnp.float32)
    up_act = jnp.dot(inputs, up_mat, preferred_element_type=jnp.float32)
    sigmoid_gate = jax.nn.sigmoid(gate_act)
    hidden = (gate_act * sigmoid_gate * up_act).astype(jnp.bfloat16)
    output = jnp.dot(hidden, down_mat, preferred_element_type=jnp.float32).astype(jnp.bfloat16)
    return (output, gate_act, up_act)


def expert_backward(incoming, gate_act, up_act, gate_mat, up_mat, down_mat):
    against = (((1,), (1,)), ((), ()))
    hidden_grad = lax.dot_general(incoming, down_mat, against, preferred_element_type=jnp.float32)
    sigmoid_gate = jax.nn.sigmoid(gate_act)
    gate_grad = (
        hidden_grad * up_act * sigmoid_gate * (1.0 + gate_act * (1.0 - sigmoid_gate))
    ).astype(jnp.bfloat16)
    up_grad = (hidden_grad * gate_act * sigmoid_gate).astype(jnp.bfloat16)
    summed = lax.dot_general(gate_grad, gate_mat, against, preferred_element_type=jnp.float32)
    summed = summed + lax.dot_general(up_grad, up_mat, against, preferred_element_type=jnp.float32)
    return summed.astype(jnp.bfloat16)


def per_device_slots(
    tokens, out_grad, cluster_ids, routes, route_weights, gate_weight, up_weight, down_weight
):
    model_width = tokens.shape[1]
    cent_rows = routes.shape[0]
    fanout = routes.shape[1]
    experts = lax.axis_size("expert")
    capacity = min(cent_rows, 2 * cent_rows * fanout // experts)
    member = (cluster_ids[:, None] == jnp.arange(cent_rows, dtype=jnp.int32)[None, :]).astype(
        jnp.bfloat16
    )
    counts = jnp.sum(member.astype(jnp.float32), axis=0)
    contract = (((0,), (0,)), ((), ()))
    centroid = (
        lax.dot_general(member, tokens, contract, preferred_element_type=jnp.float32)
        / counts[:, None]
    )
    grad_sum = lax.dot_general(member, out_grad, contract, preferred_element_type=jnp.float32)
    pair_ids = routes.reshape(-1)
    matches = (pair_ids[:, None] == jnp.arange(experts, dtype=jnp.int32)[None, :]).astype(jnp.int32)
    earlier = jnp.cumsum(matches, axis=0) - matches
    position = jnp.sum(earlier * matches, axis=1)
    slot_of = (pair_ids * capacity + position).reshape(cent_rows, fanout)
    slot_range = jnp.arange(experts * capacity, dtype=jnp.int32)
    placing = jnp.any(slot_of[None, :, :] == slot_range[:, None, None], axis=2).astype(jnp.bfloat16)
    send_cent = jnp.dot(placing, centroid.astype(jnp.bfloat16), preferred_element_type=jnp.float32)
    send_cent = send_cent.astype(jnp.bfloat16).reshape(experts, capacity, model_width)
    send_grad = jnp.dot(placing, grad_sum.astype(jnp.bfloat16), preferred_element_type=jnp.float32)
    send_grad = send_grad.astype(jnp.bfloat16).reshape(experts, capacity, model_width)
    gate_mat = gate_weight[0]
    up_mat = up_weight[0]
    down_mat = down_weight[0]
    arrived = lax.all_to_all(send_cent, "expert", split_axis=0, concat_axis=0, tiled=True)
    output, gate_act, up_act = expert_forward(
        arrived.reshape(-1, model_width), gate_mat, up_mat, down_mat
    )
    results = lax.all_to_all(
        output.reshape(experts, capacity, model_width),
        "expert",
        split_axis=0,
        concat_axis=0,
        tiled=True,
    )
    arrived_grad = lax.all_to_all(send_grad, "expert", split_axis=0, concat_axis=0, tiled=True)
    input_grad = expert_backward(
        arrived_grad.reshape(-1, model_width), gate_act, up_act, gate_mat, up_mat, down_mat
    )
    results_grad = lax.all_to_all(
        input_grad.reshape(experts, capacity, model_width),
        "expert",
        split_axis=0,
        concat_axis=0,
        tiled=True,
    )
    returned = results.reshape(-1, model_width)[slot_of]
    returned_grad = results_grad.reshape(-1, model_width)[slot_of]
    combined = jnp.sum(route_weights[:, :, None] * returned.astype(jnp.float32), axis=1)
    centroid_grad = (
        jnp.sum(route_weights[:, :, None] * returned_grad.astype(jnp.float32), axis=1) - grad_sum
    )
    layer_out = tokens.astype(jnp.float32) + jnp.take(combined - centroid, cluster_ids, axis=0)
    token_grad = out_grad.astype(jnp.float32) + jnp.take(
        centroid_grad / counts[:, None], cluster_ids, axis=0
    )
    return (layer_out, token_grad)


def pick(index, options):
    chosen = options[-1]
    for position in range(len(options) - 2, -1, -1):
        chosen = jnp.where(index == position, options[position], chosen)
    return chosen


def place(pieces, lines, like):
    slot = lax.broadcasted_iota(jnp.int32, (lines,) + (1,) * like.ndim, 0)
    stacked = jnp.zeros((lines,) + like.shape, like.dtype)
    for piece, origin in pieces:
        stacked = jnp.where(slot == origin, piece[None], stacked)
    return stacked


def topo_all_gather(shard, experts):
    lines = experts // 4
    me = lax.axis_index("expert")
    line = me // 4
    swap_row = [(j, j ^ 2) for j in range(experts)]
    here = [(shard, line)]
    if lines == 4:
        here, there = four_line_gather(shard, line, swap_row)
        both = jnp.stack([place(here, lines, shard), place(there, lines, shard)])
        return both.reshape((lines * 2 * shard.shape[0],) + shard.shape[1:])
    there = [(lax.ppermute(shard, "expert", swap_row), line)]
    ahead, behind = shard, shard
    for step in range(1, lines):
        ahead = lax.ppermute(
            ahead,
            "expert",
            [(j, j + 4) for j in range(experts) if step - 1 <= j // 4 < lines - 1],
        )
        behind = lax.ppermute(
            behind,
            "expert",
            [(j, j - 4) for j in range(experts) if 1 <= j // 4 <= lines - step],
        )
        here.append((ahead, line - step))
        here.append((behind, line + step))
        ahead_row = [(j, j ^ 2) for j in range(experts) if j // 4 >= step]
        behind_row = [(j, j ^ 2) for j in range(experts) if j // 4 <= lines - 1 - step]
        if 2 * step > lines - 1:
            in_ahead = line >= step
            got = lax.ppermute(
                jnp.where(in_ahead, ahead, behind), "expert", sorted(ahead_row + behind_row)
            )
            origin = jnp.where(in_ahead, line - step, jnp.where(line <= lines - 1 - step, line + step, -1))
            there.append((got, origin))
        else:
            there.append((lax.ppermute(ahead, "expert", ahead_row), line - step))
            there.append((lax.ppermute(behind, "expert", behind_row), line + step))
    both = jnp.stack([place(here, lines, shard), place(there, lines, shard)])
    return both.reshape((lines * 2 * shard.shape[0],) + shard.shape[1:])


def topo_reduce_scatter(blocks, experts):
    lines = experts // 4
    me = lax.axis_index("expert")
    rows = blocks.shape[0] // (2 * lines)
    plane = blocks.reshape((2, lines, rows) + blocks.shape[1:])
    keep = plane[0]
    give = plane[1]
    line = me // 4

    def row_sum(target, senders):
        mine = lax.dynamic_index_in_dim(keep, target, 0, keepdims=False)
        theirs = lax.dynamic_index_in_dim(give, target, 0, keepdims=False)
        pairs = [(j, j ^ 2) for j in range(experts) if senders(j // 4)]
        got = lax.ppermute(theirs.astype(jnp.bfloat16), "expert", pairs)
        return mine + got.astype(jnp.float32)

    if lines == 4:
        return four_line_sum(keep, give, line, row_sum)
    ahead = jnp.zeros(keep.shape[1:], jnp.float32)
    behind = jnp.zeros(keep.shape[1:], jnp.float32)
    for step in range(1, lines):
        ahead_target = jnp.clip(line + lines - step, 0, lines - 1)
        behind_target = jnp.clip(line - lines + step, 0, lines - 1)
        if 2 * step <= lines:
            in_ahead = line <= step - 1
            target = jnp.where(in_ahead, ahead_target, behind_target)
            ahead_part = row_sum(target, lambda z, s=step: z <= s - 1 or z >= lines - s)
            behind_part = ahead_part
        else:
            ahead_part = row_sum(ahead_target, lambda z, s=step: z <= s - 1)
            behind_part = row_sum(behind_target, lambda z, s=step: z >= lines - s)
        ahead = lax.ppermute(
            (ahead + ahead_part).astype(jnp.bfloat16),
            "expert",
            [(j, j + 4) for j in range(experts) if j // 4 <= step - 1],
        ).astype(jnp.float32)
        behind = lax.ppermute(
            (behind + behind_part).astype(jnp.bfloat16),
            "expert",
            [(j, j - 4) for j in range(experts) if j // 4 >= lines - step],
        ).astype(jnp.float32)
    return row_sum(line, lambda z: True) + ahead + behind


def four_line_gather(shard, line, swap_row):
    own_row = lax.ppermute(shard, "expert", swap_row)
    ahead = lax.ppermute(shard, "expert", [(j, j + 4) for j in range(12)])
    behind = lax.ppermute(shard, "expert", [(j, j - 4) for j in range(4, 16)])
    ahead_row = lax.ppermute(ahead, "expert", [(j, j ^ 2) for j in range(4, 16)])
    behind_row = lax.ppermute(behind, "expert", [(j, j ^ 2) for j in range(12)])
    ahead_two = lax.ppermute(ahead, "expert", [(j, j + 4) for j in range(4, 12)])
    behind_two = lax.ppermute(behind, "expert", [(j, j - 4) for j in range(4, 12)])
    second_row = lax.ppermute(jnp.where(line >= 2, ahead_two, behind_two), "expert", swap_row)
    last_ahead = lax.ppermute(
        jnp.stack([ahead_two, second_row]), "expert", [(j, j + 4) for j in range(8, 12)]
    )
    last_behind = lax.ppermute(
        jnp.stack([behind_two, second_row]), "expert", [(j, j - 4) for j in range(4, 8)]
    )
    here = [
        (shard, line),
        (ahead, line - 1),
        (behind, line + 1),
        (ahead_two, line - 2),
        (behind_two, line + 2),
        (last_ahead[0], line - 3),
        (last_behind[0], line + 3),
    ]
    there = [
        (own_row, line),
        (ahead_row, line - 1),
        (behind_row, line + 1),
        (second_row, jnp.where(line >= 2, line - 2, line + 2)),
        (last_ahead[1], line - 3),
        (last_behind[1], line + 3),
    ]
    return here, there


def four_line_sum(keep, give, line, row_sum):
    experts = 16
    end = (line == 0) | (line == 3)
    first = row_sum(jnp.where(end, 3 - line, line), lambda z: True)
    ahead = lax.ppermute(first.astype(jnp.bfloat16), "expert", [(j, j + 4) for j in range(4)])
    behind = lax.ppermute(first.astype(jnp.bfloat16), "expert", [(j, j - 4) for j in range(12, 16)])
    ahead, behind = ahead.astype(jnp.float32), behind.astype(jnp.float32)
    second = row_sum(jnp.where(line <= 1, line + 2, line - 2), lambda z: True)
    ahead = lax.ppermute(
        (ahead + second).astype(jnp.bfloat16), "expert", [(j, j + 4) for j in range(8)]
    ).astype(jnp.float32)
    behind = lax.ppermute(
        (behind + second).astype(jnp.bfloat16), "expert", [(j, j - 4) for j in range(8, 16)]
    ).astype(jnp.float32)
    third = row_sum(jnp.where(line <= 2, line + 1, line - 1), lambda z: True)
    fourth = row_sum(jnp.where(end, line, line - 1), lambda z: True)
    behind_part = jnp.where(line == 3, third, fourth)
    ahead = lax.ppermute(
        (ahead + third).astype(jnp.bfloat16), "expert", [(j, j + 4) for j in range(12)]
    ).astype(jnp.float32)
    behind = lax.ppermute(
        (behind + behind_part).astype(jnp.bfloat16), "expert", [(j, j - 4) for j in range(4, 16)]
    ).astype(jnp.float32)
    return jnp.where(end, fourth, first) + ahead + behind


def expert_dense(cent_in, grad_in, gate_mat, up_mat, down_mat):
    against = (((1,), (1,)), ((), ()))
    gate_act = jnp.dot(cent_in, gate_mat, preferred_element_type=jnp.float32)
    up_act = jnp.dot(cent_in, up_mat, preferred_element_type=jnp.float32)
    sigmoid_gate = jax.nn.sigmoid(gate_act)
    hidden = (gate_act * sigmoid_gate * up_act).astype(jnp.bfloat16)
    output = jnp.dot(hidden, down_mat, preferred_element_type=jnp.float32).astype(jnp.bfloat16)
    hidden_grad = lax.dot_general(grad_in, down_mat, against, preferred_element_type=jnp.float32)
    gate_grad = (
        hidden_grad * up_act * sigmoid_gate * (1.0 + gate_act * (1.0 - sigmoid_gate))
    ).astype(jnp.bfloat16)
    up_grad = (hidden_grad * gate_act * sigmoid_gate).astype(jnp.bfloat16)
    summed = lax.dot_general(gate_grad, gate_mat, against, preferred_element_type=jnp.float32)
    summed = summed + lax.dot_general(up_grad, up_mat, against, preferred_element_type=jnp.float32)
    return output, summed.astype(jnp.bfloat16)


def per_device_dense(
    tokens, out_grad, cluster_ids, routes, route_weights, gate_weight, up_weight, down_weight
):
    cent_rows = routes.shape[0]
    me = lax.axis_index("expert")
    member = (cluster_ids[:, None] == jnp.arange(cent_rows, dtype=jnp.int32)[None, :]).astype(
        jnp.bfloat16
    )
    counts = jnp.sum(member.astype(jnp.float32), axis=0)
    contract = (((0,), (0,)), ((), ()))
    model_width = tokens.shape[1]
    sums = lax.dot_general(
        member,
        jnp.concatenate([tokens, out_grad], axis=1),
        contract,
        preferred_element_type=jnp.float32,
    )
    centroid = sums[:, :model_width] / counts[:, None]
    grad_sum = sums[:, model_width:]
    experts = lax.axis_size("expert")
    model_width = tokens.shape[1]
    picked = routes[:, :, None] == jnp.arange(experts, dtype=jnp.int32)[None, None, :]
    per_expert = jnp.sum(jnp.where(picked, route_weights[:, :, None], 0.0), axis=1)
    weight_hi = per_expert.astype(jnp.bfloat16)
    weight_lo = (per_expert - weight_hi.astype(jnp.float32)).astype(jnp.bfloat16)
    side = jnp.concatenate([weight_hi, weight_lo], axis=1)
    side_width = -(-side.shape[1] // 128) * 128
    side = jnp.pad(side, ((0, 0), (0, side_width - side.shape[1])))
    payload = jnp.concatenate(
        [centroid.astype(jnp.bfloat16), grad_sum.astype(jnp.bfloat16), side], axis=1
    )
    gathered = topo_all_gather(payload, experts)
    cent_all = gathered[:, :model_width]
    grad_all = gathered[:, model_width : 2 * model_width]
    side_all = gathered[:, 2 * model_width : 2 * model_width + 2 * experts].astype(jnp.float32)
    column = jnp.arange(experts, dtype=jnp.int32)[None, :]
    summed_side = side_all[:, :experts] + side_all[:, experts:]
    mine = jnp.sum(jnp.where(column == me, summed_side, 0.0), axis=1)
    other = jnp.sum(jnp.where(column == (me ^ 1), summed_side, 0.0), axis=1)
    swap_core = [(j, j ^ 1) for j in range(experts)]
    gate_mat, up_mat, down_mat = gate_weight[0], up_weight[0], down_weight[0]
    gate_pair = lax.ppermute(gate_mat, "expert", swap_core)
    up_pair = lax.ppermute(up_mat, "expert", swap_core)
    down_pair = lax.ppermute(down_mat, "expert", swap_core)
    output, input_grad = expert_dense(cent_all, grad_all, gate_mat, up_mat, down_mat)
    output_pair, input_grad_pair = expert_dense(cent_all, grad_all, gate_pair, up_pair, down_pair)
    weighted_out = mine[:, None] * output.astype(jnp.float32) + other[:, None] * output_pair.astype(
        jnp.float32
    )
    weighted_grad = mine[:, None] * input_grad.astype(jnp.float32) + other[
        :, None
    ] * input_grad_pair.astype(jnp.float32)
    summed = topo_reduce_scatter(jnp.concatenate([weighted_out, weighted_grad], axis=1), experts)
    combined = summed[:, :model_width]
    centroid_grad = summed[:, model_width:] - grad_sum
    table = jnp.concatenate([combined - centroid, centroid_grad / counts[:, None]], axis=1)
    spread = jnp.dot(member.astype(jnp.float32), table, precision=lax.Precision.HIGHEST)
    layer_out = tokens.astype(jnp.float32) + spread[:, :model_width]
    token_grad = out_grad.astype(jnp.float32) + spread[:, model_width:]
    return (layer_out, token_grad)


def per_device(*args):
    routes = args[3]
    cent_rows, fanout = routes.shape
    experts = lax.axis_size("expert")
    capacity = min(cent_rows, 2 * cent_rows * fanout // experts)
    if capacity == cent_rows and experts % 4 == 0:
        return per_device_dense(*args)
    return per_device_slots(*args)


def solution(mesh):
    placed = (
        P(("groups", "expert"), None),
        P(("groups", "expert"), None),
        P(("groups", "expert")),
        P(("groups", "expert"), None),
        P(("groups", "expert"), None),
        P("expert", None, None),
        P("expert", None, None),
        P("expert", None, None),
    )
    return jax.shard_map(
        per_device,
        mesh=mesh,
        in_specs=placed,
        out_specs=(P(("groups", "expert"), None), P(("groups", "expert"), None)),
        check_vma=False,
    )
```

```python
import jax
import jax.numpy as jnp
from jax import lax
from jax.sharding import PartitionSpec as P


def expert_forward(inputs, gate_mat, up_mat, down_mat):
    gate_act = jnp.dot(inputs, gate_mat, preferred_element_type=jnp.float32)
    up_act = jnp.dot(inputs, up_mat, preferred_element_type=jnp.float32)
    sigmoid_gate = jax.nn.sigmoid(gate_act)
    hidden = (gate_act * sigmoid_gate * up_act).astype(jnp.bfloat16)
    output = jnp.dot(hidden, down_mat, preferred_element_type=jnp.float32).astype(jnp.bfloat16)
    return (output, gate_act, up_act)


def expert_backward(incoming, gate_act, up_act, gate_mat, up_mat, down_mat):
    against = (((1,), (1,)), ((), ()))
    hidden_grad = lax.dot_general(incoming, down_mat, against, preferred_element_type=jnp.float32)
    sigmoid_gate = jax.nn.sigmoid(gate_act)
    gate_grad = (
        hidden_grad * up_act * sigmoid_gate * (1.0 + gate_act * (1.0 - sigmoid_gate))
    ).astype(jnp.bfloat16)
    up_grad = (hidden_grad * gate_act * sigmoid_gate).astype(jnp.bfloat16)
    summed = lax.dot_general(gate_grad, gate_mat, against, preferred_element_type=jnp.float32)
    summed = summed + lax.dot_general(up_grad, up_mat, against, preferred_element_type=jnp.float32)
    return summed.astype(jnp.bfloat16)


def per_device_slots(
    tokens, out_grad, cluster_ids, routes, route_weights, gate_weight, up_weight, down_weight
):
    model_width = tokens.shape[1]
    cent_rows = routes.shape[0]
    fanout = routes.shape[1]
    experts = lax.axis_size("expert")
    capacity = min(cent_rows, 2 * cent_rows * fanout // experts)
    member = (cluster_ids[:, None] == jnp.arange(cent_rows, dtype=jnp.int32)[None, :]).astype(
        jnp.bfloat16
    )
    counts = jnp.sum(member.astype(jnp.float32), axis=0)
    contract = (((0,), (0,)), ((), ()))
    centroid = (
        lax.dot_general(member, tokens, contract, preferred_element_type=jnp.float32)
        / counts[:, None]
    )
    grad_sum = lax.dot_general(member, out_grad, contract, preferred_element_type=jnp.float32)
    pair_ids = routes.reshape(-1)
    matches = (pair_ids[:, None] == jnp.arange(experts, dtype=jnp.int32)[None, :]).astype(jnp.int32)
    earlier = jnp.cumsum(matches, axis=0) - matches
    position = jnp.sum(earlier * matches, axis=1)
    slot_of = (pair_ids * capacity + position).reshape(cent_rows, fanout)
    slot_range = jnp.arange(experts * capacity, dtype=jnp.int32)
    placing = jnp.any(slot_of[None, :, :] == slot_range[:, None, None], axis=2).astype(jnp.bfloat16)
    send_cent = jnp.dot(placing, centroid.astype(jnp.bfloat16), preferred_element_type=jnp.float32)
    send_cent = send_cent.astype(jnp.bfloat16).reshape(experts, capacity, model_width)
    send_grad = jnp.dot(placing, grad_sum.astype(jnp.bfloat16), preferred_element_type=jnp.float32)
    send_grad = send_grad.astype(jnp.bfloat16).reshape(experts, capacity, model_width)
    gate_mat = gate_weight[0]
    up_mat = up_weight[0]
    down_mat = down_weight[0]
    arrived = lax.all_to_all(send_cent, "expert", split_axis=0, concat_axis=0, tiled=True)
    output, gate_act, up_act = expert_forward(
        arrived.reshape(-1, model_width), gate_mat, up_mat, down_mat
    )
    results = lax.all_to_all(
        output.reshape(experts, capacity, model_width),
        "expert",
        split_axis=0,
        concat_axis=0,
        tiled=True,
    )
    arrived_grad = lax.all_to_all(send_grad, "expert", split_axis=0, concat_axis=0, tiled=True)
    input_grad = expert_backward(
        arrived_grad.reshape(-1, model_width), gate_act, up_act, gate_mat, up_mat, down_mat
    )
    results_grad = lax.all_to_all(
        input_grad.reshape(experts, capacity, model_width),
        "expert",
        split_axis=0,
        concat_axis=0,
        tiled=True,
    )
    returned = results.reshape(-1, model_width)[slot_of]
    returned_grad = results_grad.reshape(-1, model_width)[slot_of]
    combined = jnp.sum(route_weights[:, :, None] * returned.astype(jnp.float32), axis=1)
    centroid_grad = (
        jnp.sum(route_weights[:, :, None] * returned_grad.astype(jnp.float32), axis=1) - grad_sum
    )
    layer_out = tokens.astype(jnp.float32) + jnp.take(combined - centroid, cluster_ids, axis=0)
    token_grad = out_grad.astype(jnp.float32) + jnp.take(
        centroid_grad / counts[:, None], cluster_ids, axis=0
    )
    return (layer_out, token_grad)


def pick(index, options):
    chosen = options[-1]
    for position in range(len(options) - 2, -1, -1):
        chosen = jnp.where(index == position, options[position], chosen)
    return chosen


def place(pieces, lines, like):
    slot = lax.broadcasted_iota(jnp.int32, (lines,) + (1,) * like.ndim, 0)
    stacked = jnp.zeros((lines,) + like.shape, like.dtype)
    for piece, origin in pieces:
        stacked = jnp.where(slot == origin, piece[None], stacked)
    return stacked


def topo_all_gather(shard, experts):
    lines = experts // 4
    me = lax.axis_index("expert")
    line = me // 4
    swap_row = [(j, j ^ 2) for j in range(experts)]
    here = [(shard, line)]
    there = [(lax.ppermute(shard, "expert", swap_row), line)]
    ahead, behind = shard, shard
    for step in range(1, lines):
        ahead = lax.ppermute(
            ahead,
            "expert",
            [(j, j + 4) for j in range(experts) if step - 1 <= j // 4 < lines - 1],
        )
        behind = lax.ppermute(
            behind,
            "expert",
            [(j, j - 4) for j in range(experts) if 1 <= j // 4 <= lines - step],
        )
        here.append((ahead, line - step))
        here.append((behind, line + step))
        ahead_row = [(j, j ^ 2) for j in range(experts) if j // 4 >= step]
        behind_row = [(j, j ^ 2) for j in range(experts) if j // 4 <= lines - 1 - step]
        if 2 * step > lines - 1:
            in_ahead = line >= step
            got = lax.ppermute(
                jnp.where(in_ahead, ahead, behind), "expert", sorted(ahead_row + behind_row)
            )
            origin = jnp.where(in_ahead, line - step, jnp.where(line <= lines - 1 - step, line + step, -1))
            there.append((got, origin))
        else:
            there.append((lax.ppermute(ahead, "expert", ahead_row), line - step))
            there.append((lax.ppermute(behind, "expert", behind_row), line + step))
    both = jnp.stack([place(here, lines, shard), place(there, lines, shard)])
    return both.reshape((lines * 2 * shard.shape[0],) + shard.shape[1:])


def topo_reduce_scatter(blocks, experts):
    lines = experts // 4
    me = lax.axis_index("expert")
    rows = blocks.shape[0] // (2 * lines)
    plane = blocks.reshape((2, lines, rows) + blocks.shape[1:])
    keep = plane[0]
    give = plane[1]
    line = me // 4

    def row_sum(target, senders):
        mine = lax.dynamic_index_in_dim(keep, target, 0, keepdims=False)
        theirs = lax.dynamic_index_in_dim(give, target, 0, keepdims=False)
        pairs = [(j, j ^ 2) for j in range(experts) if senders(j // 4)]
        got = lax.ppermute(theirs.astype(jnp.bfloat16), "expert", pairs)
        return mine + got.astype(jnp.float32)

    if lines == 4:
        return four_line_sum(keep, give, line, row_sum)
    ahead = jnp.zeros(keep.shape[1:], jnp.float32)
    behind = jnp.zeros(keep.shape[1:], jnp.float32)
    for step in range(1, lines):
        ahead_target = jnp.clip(line + lines - step, 0, lines - 1)
        behind_target = jnp.clip(line - lines + step, 0, lines - 1)
        if 2 * step <= lines:
            in_ahead = line <= step - 1
            target = jnp.where(in_ahead, ahead_target, behind_target)
            ahead_part = row_sum(target, lambda z, s=step: z <= s - 1 or z >= lines - s)
            behind_part = ahead_part
        else:
            ahead_part = row_sum(ahead_target, lambda z, s=step: z <= s - 1)
            behind_part = row_sum(behind_target, lambda z, s=step: z >= lines - s)
        ahead = lax.ppermute(
            (ahead + ahead_part).astype(jnp.bfloat16),
            "expert",
            [(j, j + 4) for j in range(experts) if j // 4 <= step - 1],
        ).astype(jnp.float32)
        behind = lax.ppermute(
            (behind + behind_part).astype(jnp.bfloat16),
            "expert",
            [(j, j - 4) for j in range(experts) if j // 4 >= lines - step],
        ).astype(jnp.float32)
    return row_sum(line, lambda z: True) + ahead + behind


def four_line_sum(keep, give, line, row_sum):
    experts = 16
    end = (line == 0) | (line == 3)
    first = row_sum(jnp.where(end, 3 - line, line), lambda z: True)
    ahead = lax.ppermute(first.astype(jnp.bfloat16), "expert", [(j, j + 4) for j in range(4)])
    behind = lax.ppermute(first.astype(jnp.bfloat16), "expert", [(j, j - 4) for j in range(12, 16)])
    ahead, behind = ahead.astype(jnp.float32), behind.astype(jnp.float32)
    second = row_sum(jnp.where(line <= 1, line + 2, line - 2), lambda z: True)
    ahead = lax.ppermute(
        (ahead + second).astype(jnp.bfloat16), "expert", [(j, j + 4) for j in range(8)]
    ).astype(jnp.float32)
    behind = lax.ppermute(
        (behind + second).astype(jnp.bfloat16), "expert", [(j, j - 4) for j in range(8, 16)]
    ).astype(jnp.float32)
    third = row_sum(jnp.where(line <= 2, line + 1, line - 1), lambda z: True)
    fourth = row_sum(jnp.where(end, line, line - 1), lambda z: True)
    behind_part = jnp.where(line == 3, third, fourth)
    ahead = lax.ppermute(
        (ahead + third).astype(jnp.bfloat16), "expert", [(j, j + 4) for j in range(12)]
    ).astype(jnp.float32)
    behind = lax.ppermute(
        (behind + behind_part).astype(jnp.bfloat16), "expert", [(j, j - 4) for j in range(4, 16)]
    ).astype(jnp.float32)
    return jnp.where(end, fourth, first) + ahead + behind


def expert_dense(cent_in, grad_in, gate_mat, up_mat, down_mat):
    against = (((1,), (1,)), ((), ()))
    gate_act = jnp.dot(cent_in, gate_mat, preferred_element_type=jnp.float32)
    up_act = jnp.dot(cent_in, up_mat, preferred_element_type=jnp.float32)
    sigmoid_gate = jax.nn.sigmoid(gate_act)
    hidden = (gate_act * sigmoid_gate * up_act).astype(jnp.bfloat16)
    output = jnp.dot(hidden, down_mat, preferred_element_type=jnp.float32).astype(jnp.bfloat16)
    hidden_grad = lax.dot_general(grad_in, down_mat, against, preferred_element_type=jnp.float32)
    gate_grad = (
        hidden_grad * up_act * sigmoid_gate * (1.0 + gate_act * (1.0 - sigmoid_gate))
    ).astype(jnp.bfloat16)
    up_grad = (hidden_grad * gate_act * sigmoid_gate).astype(jnp.bfloat16)
    summed = lax.dot_general(gate_grad, gate_mat, against, preferred_element_type=jnp.float32)
    summed = summed + lax.dot_general(up_grad, up_mat, against, preferred_element_type=jnp.float32)
    return output, summed.astype(jnp.bfloat16)


def per_device_dense(
    tokens, out_grad, cluster_ids, routes, route_weights, gate_weight, up_weight, down_weight
):
    cent_rows = routes.shape[0]
    me = lax.axis_index("expert")
    member = (cluster_ids[:, None] == jnp.arange(cent_rows, dtype=jnp.int32)[None, :]).astype(
        jnp.bfloat16
    )
    contract = (((0,), (0,)), ((), ()))
    model_width = tokens.shape[1]
    ones = jnp.ones((tokens.shape[0], 128), jnp.bfloat16)
    sums = lax.dot_general(
        member,
        jnp.concatenate([tokens, out_grad, ones], axis=1),
        contract,
        preferred_element_type=jnp.float32,
    )
    counts = sums[:, 2 * model_width]
    centroid = sums[:, :model_width] / counts[:, None]
    grad_sum = sums[:, model_width : 2 * model_width]
    experts = lax.axis_size("expert")
    model_width = tokens.shape[1]
    picked = routes[:, :, None] == jnp.arange(experts, dtype=jnp.int32)[None, None, :]
    per_expert = jnp.sum(jnp.where(picked, route_weights[:, :, None], 0.0), axis=1)
    weight_hi = per_expert.astype(jnp.bfloat16)
    weight_lo = (per_expert - weight_hi.astype(jnp.float32)).astype(jnp.bfloat16)
    side = jnp.concatenate([weight_hi, weight_lo], axis=1)
    side_width = -(-side.shape[1] // 128) * 128
    side = jnp.pad(side, ((0, 0), (0, side_width - side.shape[1])))
    payload = jnp.concatenate(
        [centroid.astype(jnp.bfloat16), grad_sum.astype(jnp.bfloat16), side], axis=1
    )
    gathered = topo_all_gather(payload, experts)
    cent_all = gathered[:, :model_width]
    grad_all = gathered[:, model_width : 2 * model_width]
    side_all = gathered[:, 2 * model_width : 2 * model_width + 2 * experts].astype(jnp.float32)
    column = jnp.arange(experts, dtype=jnp.int32)[None, :]
    summed_side = side_all[:, :experts] + side_all[:, experts:]
    mine = jnp.sum(jnp.where(column == me, summed_side, 0.0), axis=1)
    other = jnp.sum(jnp.where(column == (me ^ 1), summed_side, 0.0), axis=1)
    swap_core = [(j, j ^ 1) for j in range(experts)]
    gate_mat, up_mat, down_mat = gate_weight[0], up_weight[0], down_weight[0]
    gate_pair = lax.ppermute(gate_mat, "expert", swap_core)
    up_pair = lax.ppermute(up_mat, "expert", swap_core)
    down_pair = lax.ppermute(down_mat, "expert", swap_core)
    output, input_grad = expert_dense(cent_all, grad_all, gate_mat, up_mat, down_mat)
    output_pair, input_grad_pair = expert_dense(cent_all, grad_all, gate_pair, up_pair, down_pair)
    weighted_out = mine[:, None] * output.astype(jnp.float32) + other[:, None] * output_pair.astype(
        jnp.float32
    )
    weighted_grad = mine[:, None] * input_grad.astype(jnp.float32) + other[
        :, None
    ] * input_grad_pair.astype(jnp.float32)
    summed = topo_reduce_scatter(jnp.concatenate([weighted_out, weighted_grad], axis=1), experts)
    combined = summed[:, :model_width]
    centroid_grad = summed[:, model_width:] - grad_sum
    table = jnp.concatenate([combined - centroid, centroid_grad / counts[:, None]], axis=1)
    spread = jnp.dot(member.astype(jnp.float32), table, precision=lax.Precision.HIGHEST)
    layer_out = tokens.astype(jnp.float32) + spread[:, :model_width]
    token_grad = out_grad.astype(jnp.float32) + spread[:, model_width:]
    return (layer_out, token_grad)


def per_device(*args):
    routes = args[3]
    cent_rows, fanout = routes.shape
    experts = lax.axis_size("expert")
    capacity = min(cent_rows, 2 * cent_rows * fanout // experts)
    if capacity == cent_rows and experts % 4 == 0:
        return per_device_dense(*args)
    return per_device_slots(*args)


def solution(mesh):
    placed = (
        P(("groups", "expert"), None),
        P(("groups", "expert"), None),
        P(("groups", "expert")),
        P(("groups", "expert"), None),
        P(("groups", "expert"), None),
        P("expert", None, None),
        P("expert", None, None),
        P("expert", None, None),
    )
    return jax.shard_map(
        per_device,
        mesh=mesh,
        in_specs=placed,
        out_specs=(P(("groups", "expert"), None), P(("groups", "expert"), None)),
        check_vma=False,
    )
```

```python
import jax
import jax.numpy as jnp
from jax import lax
from jax.sharding import PartitionSpec as P


def expert_forward(inputs, gate_mat, up_mat, down_mat):
    gate_act = jnp.dot(inputs, gate_mat, preferred_element_type=jnp.float32)
    up_act = jnp.dot(inputs, up_mat, preferred_element_type=jnp.float32)
    sigmoid_gate = jax.nn.sigmoid(gate_act)
    hidden = (gate_act * sigmoid_gate * up_act).astype(jnp.bfloat16)
    output = jnp.dot(hidden, down_mat, preferred_element_type=jnp.float32).astype(jnp.bfloat16)
    return (output, gate_act, up_act)


def expert_backward(incoming, gate_act, up_act, gate_mat, up_mat, down_mat):
    against = (((1,), (1,)), ((), ()))
    hidden_grad = lax.dot_general(incoming, down_mat, against, preferred_element_type=jnp.float32)
    sigmoid_gate = jax.nn.sigmoid(gate_act)
    gate_grad = (
        hidden_grad * up_act * sigmoid_gate * (1.0 + gate_act * (1.0 - sigmoid_gate))
    ).astype(jnp.bfloat16)
    up_grad = (hidden_grad * gate_act * sigmoid_gate).astype(jnp.bfloat16)
    summed = lax.dot_general(gate_grad, gate_mat, against, preferred_element_type=jnp.float32)
    summed = summed + lax.dot_general(up_grad, up_mat, against, preferred_element_type=jnp.float32)
    return summed.astype(jnp.bfloat16)


def per_device_slots(
    tokens, out_grad, cluster_ids, routes, route_weights, gate_weight, up_weight, down_weight
):
    model_width = tokens.shape[1]
    cent_rows = routes.shape[0]
    fanout = routes.shape[1]
    experts = lax.axis_size("expert")
    capacity = min(cent_rows, 2 * cent_rows * fanout // experts)
    member = (cluster_ids[:, None] == jnp.arange(cent_rows, dtype=jnp.int32)[None, :]).astype(
        jnp.bfloat16
    )
    counts = jnp.sum(member.astype(jnp.float32), axis=0)
    contract = (((0,), (0,)), ((), ()))
    centroid = (
        lax.dot_general(member, tokens, contract, preferred_element_type=jnp.float32)
        / counts[:, None]
    )
    grad_sum = lax.dot_general(member, out_grad, contract, preferred_element_type=jnp.float32)
    pair_ids = routes.reshape(-1)
    matches = (pair_ids[:, None] == jnp.arange(experts, dtype=jnp.int32)[None, :]).astype(jnp.int32)
    earlier = jnp.cumsum(matches, axis=0) - matches
    position = jnp.sum(earlier * matches, axis=1)
    slot_of = (pair_ids * capacity + position).reshape(cent_rows, fanout)
    slot_range = jnp.arange(experts * capacity, dtype=jnp.int32)
    placing = jnp.any(slot_of[None, :, :] == slot_range[:, None, None], axis=2).astype(jnp.bfloat16)
    send_cent = jnp.dot(placing, centroid.astype(jnp.bfloat16), preferred_element_type=jnp.float32)
    send_cent = send_cent.astype(jnp.bfloat16).reshape(experts, capacity, model_width)
    send_grad = jnp.dot(placing, grad_sum.astype(jnp.bfloat16), preferred_element_type=jnp.float32)
    send_grad = send_grad.astype(jnp.bfloat16).reshape(experts, capacity, model_width)
    gate_mat = gate_weight[0]
    up_mat = up_weight[0]
    down_mat = down_weight[0]
    arrived = lax.all_to_all(send_cent, "expert", split_axis=0, concat_axis=0, tiled=True)
    output, gate_act, up_act = expert_forward(
        arrived.reshape(-1, model_width), gate_mat, up_mat, down_mat
    )
    results = lax.all_to_all(
        output.reshape(experts, capacity, model_width),
        "expert",
        split_axis=0,
        concat_axis=0,
        tiled=True,
    )
    arrived_grad = lax.all_to_all(send_grad, "expert", split_axis=0, concat_axis=0, tiled=True)
    input_grad = expert_backward(
        arrived_grad.reshape(-1, model_width), gate_act, up_act, gate_mat, up_mat, down_mat
    )
    results_grad = lax.all_to_all(
        input_grad.reshape(experts, capacity, model_width),
        "expert",
        split_axis=0,
        concat_axis=0,
        tiled=True,
    )
    returned = results.reshape(-1, model_width)[slot_of]
    returned_grad = results_grad.reshape(-1, model_width)[slot_of]
    combined = jnp.sum(route_weights[:, :, None] * returned.astype(jnp.float32), axis=1)
    centroid_grad = (
        jnp.sum(route_weights[:, :, None] * returned_grad.astype(jnp.float32), axis=1) - grad_sum
    )
    layer_out = tokens.astype(jnp.float32) + jnp.take(combined - centroid, cluster_ids, axis=0)
    token_grad = out_grad.astype(jnp.float32) + jnp.take(
        centroid_grad / counts[:, None], cluster_ids, axis=0
    )
    return (layer_out, token_grad)


def pick(index, options):
    chosen = options[-1]
    for position in range(len(options) - 2, -1, -1):
        chosen = jnp.where(index == position, options[position], chosen)
    return chosen


def place(pieces, lines, like):
    slot = lax.broadcasted_iota(jnp.int32, (lines,) + (1,) * like.ndim, 0)
    stacked = jnp.zeros((lines,) + like.shape, like.dtype)
    for piece, origin in pieces:
        stacked = jnp.where(slot == origin, piece[None], stacked)
    return stacked


def topo_all_gather(shard, experts):
    lines = experts // 4
    me = lax.axis_index("expert")
    line = me // 4
    swap_row = [(j, j ^ 2) for j in range(experts)]
    here = [(shard, line)]
    there = [(lax.ppermute(shard, "expert", swap_row), line)]
    ahead, behind = shard, shard
    for step in range(1, lines):
        ahead = lax.ppermute(
            ahead,
            "expert",
            [(j, j + 4) for j in range(experts) if step - 1 <= j // 4 < lines - 1],
        )
        behind = lax.ppermute(
            behind,
            "expert",
            [(j, j - 4) for j in range(experts) if 1 <= j // 4 <= lines - step],
        )
        here.append((ahead, line - step))
        here.append((behind, line + step))
        ahead_row = [(j, j ^ 2) for j in range(experts) if j // 4 >= step]
        behind_row = [(j, j ^ 2) for j in range(experts) if j // 4 <= lines - 1 - step]
        if 2 * step > lines - 1:
            in_ahead = line >= step
            got = lax.ppermute(
                jnp.where(in_ahead, ahead, behind), "expert", sorted(ahead_row + behind_row)
            )
            origin = jnp.where(in_ahead, line - step, jnp.where(line <= lines - 1 - step, line + step, -1))
            there.append((got, origin))
        else:
            there.append((lax.ppermute(ahead, "expert", ahead_row), line - step))
            there.append((lax.ppermute(behind, "expert", behind_row), line + step))
    both = jnp.stack([place(here, lines, shard), place(there, lines, shard)])
    return both.reshape((lines * 2 * shard.shape[0],) + shard.shape[1:])


def topo_reduce_scatter(blocks, experts):
    lines = experts // 4
    me = lax.axis_index("expert")
    rows = blocks.shape[0] // (2 * lines)
    plane = blocks.reshape((2, lines, rows) + blocks.shape[1:])
    keep = plane[0]
    give = plane[1]
    line = me // 4

    def row_sum(target, senders):
        mine = lax.dynamic_index_in_dim(keep, target, 0, keepdims=False)
        theirs = lax.dynamic_index_in_dim(give, target, 0, keepdims=False)
        pairs = [(j, j ^ 2) for j in range(experts) if senders(j // 4)]
        got = lax.ppermute(theirs.astype(jnp.bfloat16), "expert", pairs)
        return mine + got.astype(jnp.float32)

    ahead = jnp.zeros(keep.shape[1:], jnp.float32)
    behind = jnp.zeros(keep.shape[1:], jnp.float32)
    for step in range(1, lines):
        ahead_target = jnp.clip(line + lines - step, 0, lines - 1)
        behind_target = jnp.clip(line - lines + step, 0, lines - 1)
        if 2 * step <= lines:
            in_ahead = line <= step - 1
            target = jnp.where(in_ahead, ahead_target, behind_target)
            ahead_part = row_sum(target, lambda z, s=step: z <= s - 1 or z >= lines - s)
            behind_part = ahead_part
        else:
            ahead_part = row_sum(ahead_target, lambda z, s=step: z <= s - 1)
            behind_part = row_sum(behind_target, lambda z, s=step: z >= lines - s)
        ahead = lax.ppermute(
            (ahead + ahead_part).astype(jnp.bfloat16),
            "expert",
            [(j, j + 4) for j in range(experts) if j // 4 <= step - 1],
        ).astype(jnp.float32)
        behind = lax.ppermute(
            (behind + behind_part).astype(jnp.bfloat16),
            "expert",
            [(j, j - 4) for j in range(experts) if j // 4 >= lines - step],
        ).astype(jnp.float32)
    return row_sum(line, lambda z: True) + ahead + behind


def four_line_sum(keep, give, line, row_sum):
    experts = 16
    end = (line == 0) | (line == 3)
    first = row_sum(jnp.where(end, 3 - line, line), lambda z: True)
    ahead = lax.ppermute(first.astype(jnp.bfloat16), "expert", [(j, j + 4) for j in range(4)])
    behind = lax.ppermute(first.astype(jnp.bfloat16), "expert", [(j, j - 4) for j in range(12, 16)])
    ahead, behind = ahead.astype(jnp.float32), behind.astype(jnp.float32)
    second = row_sum(jnp.where(line <= 1, line + 2, line - 2), lambda z: True)
    ahead = lax.ppermute(
        (ahead + second).astype(jnp.bfloat16), "expert", [(j, j + 4) for j in range(8)]
    ).astype(jnp.float32)
    behind = lax.ppermute(
        (behind + second).astype(jnp.bfloat16), "expert", [(j, j - 4) for j in range(8, 16)]
    ).astype(jnp.float32)
    third = row_sum(jnp.where(line <= 2, line + 1, line - 1), lambda z: True)
    fourth = row_sum(jnp.where(end, line, line - 1), lambda z: True)
    behind_part = jnp.where(line == 3, third, fourth)
    ahead = lax.ppermute(
        (ahead + third).astype(jnp.bfloat16), "expert", [(j, j + 4) for j in range(12)]
    ).astype(jnp.float32)
    behind = lax.ppermute(
        (behind + behind_part).astype(jnp.bfloat16), "expert", [(j, j - 4) for j in range(4, 16)]
    ).astype(jnp.float32)
    return jnp.where(end, fourth, first) + ahead + behind


def expert_dense(cent_in, grad_in, gate_mat, up_mat, down_mat):
    against = (((1,), (1,)), ((), ()))
    gate_act = jnp.dot(cent_in, gate_mat, preferred_element_type=jnp.float32)
    up_act = jnp.dot(cent_in, up_mat, preferred_element_type=jnp.float32)
    sigmoid_gate = jax.nn.sigmoid(gate_act)
    hidden = (gate_act * sigmoid_gate * up_act).astype(jnp.bfloat16)
    output = jnp.dot(hidden, down_mat, preferred_element_type=jnp.float32).astype(jnp.bfloat16)
    hidden_grad = lax.dot_general(grad_in, down_mat, against, preferred_element_type=jnp.float32)
    gate_grad = (
        hidden_grad * up_act * sigmoid_gate * (1.0 + gate_act * (1.0 - sigmoid_gate))
    ).astype(jnp.bfloat16)
    up_grad = (hidden_grad * gate_act * sigmoid_gate).astype(jnp.bfloat16)
    summed = lax.dot_general(gate_grad, gate_mat, against, preferred_element_type=jnp.float32)
    summed = summed + lax.dot_general(up_grad, up_mat, against, preferred_element_type=jnp.float32)
    return output, summed.astype(jnp.bfloat16)


def per_device_dense(
    tokens, out_grad, cluster_ids, routes, route_weights, gate_weight, up_weight, down_weight
):
    cent_rows = routes.shape[0]
    me = lax.axis_index("expert")
    member = (cluster_ids[:, None] == jnp.arange(cent_rows, dtype=jnp.int32)[None, :]).astype(
        jnp.bfloat16
    )
    contract = (((0,), (0,)), ((), ()))
    model_width = tokens.shape[1]
    ones = jnp.ones((tokens.shape[0], 128), jnp.bfloat16)
    sums = lax.dot_general(
        member,
        jnp.concatenate([tokens, out_grad, ones], axis=1),
        contract,
        preferred_element_type=jnp.float32,
    )
    counts = sums[:, 2 * model_width]
    centroid = sums[:, :model_width] / counts[:, None]
    grad_sum = sums[:, model_width : 2 * model_width]
    experts = lax.axis_size("expert")
    model_width = tokens.shape[1]
    picked = routes[:, :, None] == jnp.arange(experts, dtype=jnp.int32)[None, None, :]
    per_expert = jnp.sum(jnp.where(picked, route_weights[:, :, None], 0.0), axis=1)
    weight_hi = per_expert.astype(jnp.bfloat16)
    weight_lo = (per_expert - weight_hi.astype(jnp.float32)).astype(jnp.bfloat16)
    side = jnp.concatenate([weight_hi, weight_lo], axis=1)
    side_width = -(-side.shape[1] // 128) * 128
    side = jnp.pad(side, ((0, 0), (0, side_width - side.shape[1])))
    payload = jnp.concatenate(
        [centroid.astype(jnp.bfloat16), grad_sum.astype(jnp.bfloat16), side], axis=1
    )
    gathered = topo_all_gather(payload, experts)
    cent_all = gathered[:, :model_width]
    grad_all = gathered[:, model_width : 2 * model_width]
    side_all = gathered[:, 2 * model_width : 2 * model_width + 2 * experts].astype(jnp.float32)
    column = jnp.arange(experts, dtype=jnp.int32)[None, :]
    summed_side = side_all[:, :experts] + side_all[:, experts:]
    mine = jnp.sum(jnp.where(column == me, summed_side, 0.0), axis=1)
    other = jnp.sum(jnp.where(column == (me ^ 1), summed_side, 0.0), axis=1)
    swap_core = [(j, j ^ 1) for j in range(experts)]
    gate_mat, up_mat, down_mat = gate_weight[0], up_weight[0], down_weight[0]
    gate_pair = lax.ppermute(gate_mat, "expert", swap_core)
    up_pair = lax.ppermute(up_mat, "expert", swap_core)
    down_pair = lax.ppermute(down_mat, "expert", swap_core)
    output, input_grad = expert_dense(cent_all, grad_all, gate_mat, up_mat, down_mat)
    output_pair, input_grad_pair = expert_dense(cent_all, grad_all, gate_pair, up_pair, down_pair)
    weighted_out = mine[:, None] * output.astype(jnp.float32) + other[:, None] * output_pair.astype(
        jnp.float32
    )
    weighted_grad = mine[:, None] * input_grad.astype(jnp.float32) + other[
        :, None
    ] * input_grad_pair.astype(jnp.float32)
    summed = topo_reduce_scatter(jnp.concatenate([weighted_out, weighted_grad], axis=1), experts)
    combined = summed[:, :model_width]
    centroid_grad = summed[:, model_width:] - grad_sum
    table = jnp.concatenate([combined - centroid, centroid_grad / counts[:, None]], axis=1)
    spread = jnp.dot(member.astype(jnp.float32), table, precision=lax.Precision.HIGHEST)
    layer_out = tokens.astype(jnp.float32) + spread[:, :model_width]
    token_grad = out_grad.astype(jnp.float32) + spread[:, model_width:]
    return (layer_out, token_grad)


def per_device(*args):
    routes = args[3]
    cent_rows, fanout = routes.shape
    experts = lax.axis_size("expert")
    capacity = min(cent_rows, 2 * cent_rows * fanout // experts)
    if capacity == cent_rows and experts % 4 == 0:
        return per_device_dense(*args)
    return per_device_slots(*args)


def solution(mesh):
    placed = (
        P(("groups", "expert"), None),
        P(("groups", "expert"), None),
        P(("groups", "expert")),
        P(("groups", "expert"), None),
        P(("groups", "expert"), None),
        P("expert", None, None),
        P("expert", None, None),
        P("expert", None, None),
    )
    return jax.shard_map(
        per_device,
        mesh=mesh,
        in_specs=placed,
        out_specs=(P(("groups", "expert"), None), P(("groups", "expert"), None)),
        check_vma=False,
    )
```

```python
import jax
import jax.numpy as jnp
from jax import lax
from jax.sharding import PartitionSpec as P


def expert_forward(inputs, gate_mat, up_mat, down_mat):
    gate_act = jnp.dot(inputs, gate_mat, preferred_element_type=jnp.float32)
    up_act = jnp.dot(inputs, up_mat, preferred_element_type=jnp.float32)
    sigmoid_gate = jax.nn.sigmoid(gate_act)
    hidden = (gate_act * sigmoid_gate * up_act).astype(jnp.bfloat16)
    output = jnp.dot(hidden, down_mat, preferred_element_type=jnp.float32).astype(jnp.bfloat16)
    return (output, gate_act, up_act)


def expert_backward(incoming, gate_act, up_act, gate_mat, up_mat, down_mat):
    against = (((1,), (1,)), ((), ()))
    hidden_grad = lax.dot_general(incoming, down_mat, against, preferred_element_type=jnp.float32)
    sigmoid_gate = jax.nn.sigmoid(gate_act)
    gate_grad = (
        hidden_grad * up_act * sigmoid_gate * (1.0 + gate_act * (1.0 - sigmoid_gate))
    ).astype(jnp.bfloat16)
    up_grad = (hidden_grad * gate_act * sigmoid_gate).astype(jnp.bfloat16)
    summed = lax.dot_general(gate_grad, gate_mat, against, preferred_element_type=jnp.float32)
    summed = summed + lax.dot_general(up_grad, up_mat, against, preferred_element_type=jnp.float32)
    return summed.astype(jnp.bfloat16)


def per_device_slots(
    tokens, out_grad, cluster_ids, routes, route_weights, gate_weight, up_weight, down_weight
):
    model_width = tokens.shape[1]
    cent_rows = routes.shape[0]
    fanout = routes.shape[1]
    experts = lax.axis_size("expert")
    capacity = min(cent_rows, 2 * cent_rows * fanout // experts)
    member = (cluster_ids[:, None] == jnp.arange(cent_rows, dtype=jnp.int32)[None, :]).astype(
        jnp.bfloat16
    )
    counts = jnp.sum(member.astype(jnp.float32), axis=0)
    contract = (((0,), (0,)), ((), ()))
    centroid = (
        lax.dot_general(member, tokens, contract, preferred_element_type=jnp.float32)
        / counts[:, None]
    )
    grad_sum = lax.dot_general(member, out_grad, contract, preferred_element_type=jnp.float32)
    pair_ids = routes.reshape(-1)
    matches = (pair_ids[:, None] == jnp.arange(experts, dtype=jnp.int32)[None, :]).astype(jnp.int32)
    earlier = jnp.cumsum(matches, axis=0) - matches
    position = jnp.sum(earlier * matches, axis=1)
    slot_of = (pair_ids * capacity + position).reshape(cent_rows, fanout)
    slot_range = jnp.arange(experts * capacity, dtype=jnp.int32)
    placing = jnp.any(slot_of[None, :, :] == slot_range[:, None, None], axis=2).astype(jnp.bfloat16)
    send_cent = jnp.dot(placing, centroid.astype(jnp.bfloat16), preferred_element_type=jnp.float32)
    send_cent = send_cent.astype(jnp.bfloat16).reshape(experts, capacity, model_width)
    send_grad = jnp.dot(placing, grad_sum.astype(jnp.bfloat16), preferred_element_type=jnp.float32)
    send_grad = send_grad.astype(jnp.bfloat16).reshape(experts, capacity, model_width)
    gate_mat = gate_weight[0]
    up_mat = up_weight[0]
    down_mat = down_weight[0]
    arrived = lax.all_to_all(send_cent, "expert", split_axis=0, concat_axis=0, tiled=True)
    output, gate_act, up_act = expert_forward(
        arrived.reshape(-1, model_width), gate_mat, up_mat, down_mat
    )
    results = lax.all_to_all(
        output.reshape(experts, capacity, model_width),
        "expert",
        split_axis=0,
        concat_axis=0,
        tiled=True,
    )
    arrived_grad = lax.all_to_all(send_grad, "expert", split_axis=0, concat_axis=0, tiled=True)
    input_grad = expert_backward(
        arrived_grad.reshape(-1, model_width), gate_act, up_act, gate_mat, up_mat, down_mat
    )
    results_grad = lax.all_to_all(
        input_grad.reshape(experts, capacity, model_width),
        "expert",
        split_axis=0,
        concat_axis=0,
        tiled=True,
    )
    returned = results.reshape(-1, model_width)[slot_of]
    returned_grad = results_grad.reshape(-1, model_width)[slot_of]
    combined = jnp.sum(route_weights[:, :, None] * returned.astype(jnp.float32), axis=1)
    centroid_grad = (
        jnp.sum(route_weights[:, :, None] * returned_grad.astype(jnp.float32), axis=1) - grad_sum
    )
    layer_out = tokens.astype(jnp.float32) + jnp.take(combined - centroid, cluster_ids, axis=0)
    token_grad = out_grad.astype(jnp.float32) + jnp.take(
        centroid_grad / counts[:, None], cluster_ids, axis=0
    )
    return (layer_out, token_grad)


def pick(index, options):
    chosen = options[-1]
    for position in range(len(options) - 2, -1, -1):
        chosen = jnp.where(index == position, options[position], chosen)
    return chosen


def place(pieces, lines, like):
    slot = lax.broadcasted_iota(jnp.int32, (lines,) + (1,) * like.ndim, 0)
    stacked = jnp.zeros((lines,) + like.shape, like.dtype)
    for piece, origin in pieces:
        stacked = jnp.where(slot == origin, piece[None], stacked)
    return stacked


def topo_all_gather(shard, experts):
    lines = experts // 4
    me = lax.axis_index("expert")
    line = me // 4
    swap_row = [(j, j ^ 2) for j in range(experts)]
    here = [(shard, line)]
    there = [(lax.ppermute(shard, "expert", swap_row), line)]
    ahead, behind = shard, shard
    for step in range(1, lines):
        ahead = lax.ppermute(
            ahead,
            "expert",
            [(j, j + 4) for j in range(experts) if step - 1 <= j // 4 < lines - 1],
        )
        behind = lax.ppermute(
            behind,
            "expert",
            [(j, j - 4) for j in range(experts) if 1 <= j // 4 <= lines - step],
        )
        here.append((ahead, line - step))
        here.append((behind, line + step))
        ahead_row = [(j, j ^ 2) for j in range(experts) if j // 4 >= step]
        behind_row = [(j, j ^ 2) for j in range(experts) if j // 4 <= lines - 1 - step]
        if 2 * step > lines - 1:
            in_ahead = line >= step
            got = lax.ppermute(
                jnp.where(in_ahead, ahead, behind), "expert", sorted(ahead_row + behind_row)
            )
            origin = jnp.where(in_ahead, line - step, jnp.where(line <= lines - 1 - step, line + step, -1))
            there.append((got, origin))
        else:
            there.append((lax.ppermute(ahead, "expert", ahead_row), line - step))
            there.append((lax.ppermute(behind, "expert", behind_row), line + step))
    both = jnp.stack([place(here, lines, shard), place(there, lines, shard)])
    return both.reshape((lines * 2 * shard.shape[0],) + shard.shape[1:])


def topo_reduce_scatter(blocks, experts):
    lines = experts // 4
    me = lax.axis_index("expert")
    rows = blocks.shape[0] // (2 * lines)
    plane = blocks.reshape((2, lines, rows) + blocks.shape[1:])
    keep = plane[0]
    give = plane[1]
    line = me // 4

    def row_sum(target, senders):
        mine = lax.dynamic_index_in_dim(keep, target, 0, keepdims=False)
        theirs = lax.dynamic_index_in_dim(give, target, 0, keepdims=False)
        pairs = [(j, j ^ 2) for j in range(experts) if senders(j // 4)]
        got = lax.ppermute(theirs.astype(jnp.bfloat16), "expert", pairs)
        return mine + got.astype(jnp.float32)

    if lines == 4:
        return four_line_sum(keep, give, line, row_sum)
    ahead = jnp.zeros(keep.shape[1:], jnp.float32)
    behind = jnp.zeros(keep.shape[1:], jnp.float32)
    for step in range(1, lines):
        ahead_target = jnp.clip(line + lines - step, 0, lines - 1)
        behind_target = jnp.clip(line - lines + step, 0, lines - 1)
        if 2 * step <= lines:
            in_ahead = line <= step - 1
            target = jnp.where(in_ahead, ahead_target, behind_target)
            ahead_part = row_sum(target, lambda z, s=step: z <= s - 1 or z >= lines - s)
            behind_part = ahead_part
        else:
            ahead_part = row_sum(ahead_target, lambda z, s=step: z <= s - 1)
            behind_part = row_sum(behind_target, lambda z, s=step: z >= lines - s)
        ahead = lax.ppermute(
            (ahead + ahead_part).astype(jnp.bfloat16),
            "expert",
            [(j, j + 4) for j in range(experts) if j // 4 <= step - 1],
        ).astype(jnp.float32)
        behind = lax.ppermute(
            (behind + behind_part).astype(jnp.bfloat16),
            "expert",
            [(j, j - 4) for j in range(experts) if j // 4 >= lines - step],
        ).astype(jnp.float32)
    return row_sum(line, lambda z: True) + ahead + behind


def four_line_sum(keep, give, line, row_sum):
    experts = 16
    end = (line == 0) | (line == 3)
    first = row_sum(jnp.where(end, 3 - line, line), lambda z: True)
    ahead = lax.ppermute(first.astype(jnp.bfloat16), "expert", [(j, j + 4) for j in range(4)])
    behind = lax.ppermute(first.astype(jnp.bfloat16), "expert", [(j, j - 4) for j in range(12, 16)])
    ahead, behind = ahead.astype(jnp.float32), behind.astype(jnp.float32)
    second = row_sum(jnp.where(line <= 1, line + 2, line - 2), lambda z: True)
    ahead = lax.ppermute(
        (ahead + second).astype(jnp.bfloat16), "expert", [(j, j + 4) for j in range(8)]
    ).astype(jnp.float32)
    behind = lax.ppermute(
        (behind + second).astype(jnp.bfloat16), "expert", [(j, j - 4) for j in range(8, 16)]
    ).astype(jnp.float32)
    third = row_sum(jnp.where(line <= 2, line + 1, line - 1), lambda z: True)
    fourth = row_sum(jnp.where(end, line, line - 1), lambda z: True)
    behind_part = jnp.where(line == 3, third, fourth)
    ahead = lax.ppermute(
        (ahead + third).astype(jnp.bfloat16), "expert", [(j, j + 4) for j in range(12)]
    ).astype(jnp.float32)
    behind = lax.ppermute(
        (behind + behind_part).astype(jnp.bfloat16), "expert", [(j, j - 4) for j in range(4, 16)]
    ).astype(jnp.float32)
    return jnp.where(end, fourth, first) + ahead + behind


def expert_dense(cent_in, grad_in, gate_mat, up_mat, down_mat):
    against = (((1,), (1,)), ((), ()))
    gate_act = jnp.dot(cent_in, gate_mat, preferred_element_type=jnp.float32)
    up_act = jnp.dot(cent_in, up_mat, preferred_element_type=jnp.float32)
    sigmoid_gate = jax.nn.sigmoid(gate_act)
    hidden = (gate_act * sigmoid_gate * up_act).astype(jnp.bfloat16)
    output = jnp.dot(hidden, down_mat, preferred_element_type=jnp.float32).astype(jnp.bfloat16)
    hidden_grad = lax.dot_general(grad_in, down_mat, against, preferred_element_type=jnp.float32)
    gate_grad = (
        hidden_grad * up_act * sigmoid_gate * (1.0 + gate_act * (1.0 - sigmoid_gate))
    ).astype(jnp.bfloat16)
    up_grad = (hidden_grad * gate_act * sigmoid_gate).astype(jnp.bfloat16)
    summed = lax.dot_general(gate_grad, gate_mat, against, preferred_element_type=jnp.float32)
    summed = summed + lax.dot_general(up_grad, up_mat, against, preferred_element_type=jnp.float32)
    return output, summed.astype(jnp.bfloat16)


def per_device_dense(
    tokens, out_grad, cluster_ids, routes, route_weights, gate_weight, up_weight, down_weight
):
    cent_rows = routes.shape[0]
    me = lax.axis_index("expert")
    member = (cluster_ids[:, None] == jnp.arange(cent_rows, dtype=jnp.int32)[None, :]).astype(
        jnp.bfloat16
    )
    contract = (((0,), (0,)), ((), ()))
    model_width = tokens.shape[1]
    ones = jnp.ones((tokens.shape[0], 128), jnp.bfloat16)
    sums = lax.dot_general(
        member,
        jnp.concatenate([tokens, out_grad, ones], axis=1),
        contract,
        preferred_element_type=jnp.float32,
    )
    counts = sums[:, 2 * model_width]
    centroid = sums[:, :model_width] / counts[:, None]
    grad_sum = sums[:, model_width : 2 * model_width]
    experts = lax.axis_size("expert")
    model_width = tokens.shape[1]
    picked = routes[:, :, None] == jnp.arange(experts, dtype=jnp.int32)[None, None, :]
    per_expert = jnp.sum(jnp.where(picked, route_weights[:, :, None], 0.0), axis=1)
    weight_hi = per_expert.astype(jnp.bfloat16)
    weight_lo = (per_expert - weight_hi.astype(jnp.float32)).astype(jnp.bfloat16)
    side = jnp.concatenate([weight_hi, weight_lo], axis=1)
    side_width = -(-side.shape[1] // 128) * 128
    side = jnp.pad(side, ((0, 0), (0, side_width - side.shape[1])))
    payload = jnp.concatenate(
        [centroid.astype(jnp.bfloat16), grad_sum.astype(jnp.bfloat16), side], axis=1
    )
    gathered = topo_all_gather(payload, experts)
    cent_all = gathered[:, :model_width]
    grad_all = gathered[:, model_width : 2 * model_width]
    side_all = gathered[:, 2 * model_width : 2 * model_width + 2 * experts].astype(jnp.float32)
    column = jnp.arange(experts, dtype=jnp.int32)[None, :]
    summed_side = side_all[:, :experts] + side_all[:, experts:]
    mine = jnp.sum(jnp.where(column == me, summed_side, 0.0), axis=1)
    other = jnp.sum(jnp.where(column == (me ^ 1), summed_side, 0.0), axis=1)
    swap_core = [(j, j ^ 1) for j in range(experts)]
    gate_mat, up_mat, down_mat = gate_weight[0], up_weight[0], down_weight[0]
    gate_pair = lax.ppermute(gate_mat, "expert", swap_core)
    up_pair = lax.ppermute(up_mat, "expert", swap_core)
    down_pair = lax.ppermute(down_mat, "expert", swap_core)
    output, input_grad = expert_dense(cent_all, grad_all, gate_mat, up_mat, down_mat)
    output_pair, input_grad_pair = expert_dense(cent_all, grad_all, gate_pair, up_pair, down_pair)
    weighted_out = mine[:, None] * output.astype(jnp.float32) + other[:, None] * output_pair.astype(
        jnp.float32
    )
    weighted_grad = mine[:, None] * input_grad.astype(jnp.float32) + other[
        :, None
    ] * input_grad_pair.astype(jnp.float32)
    summed = topo_reduce_scatter(jnp.concatenate([weighted_out, weighted_grad], axis=1), experts)
    combined = summed[:, :model_width]
    centroid_grad = summed[:, model_width:] - grad_sum
    table = jnp.concatenate([combined - centroid, centroid_grad / counts[:, None]], axis=1)
    table_hi = table.astype(jnp.bfloat16)
    rest = table - table_hi.astype(jnp.float32)
    table_mid = rest.astype(jnp.bfloat16)
    table_lo = (rest - table_mid.astype(jnp.float32)).astype(jnp.bfloat16)
    parts = jnp.dot(
        member,
        jnp.concatenate([table_hi, table_mid, table_lo], axis=1),
        preferred_element_type=jnp.float32,
    )
    width = table.shape[1]
    spread = (parts[:, :width] + parts[:, width : 2 * width]) + parts[:, 2 * width :]
    layer_out = tokens.astype(jnp.float32) + spread[:, :model_width]
    token_grad = out_grad.astype(jnp.float32) + spread[:, model_width:]
    return (layer_out, token_grad)


def per_device(*args):
    routes = args[3]
    cent_rows, fanout = routes.shape
    experts = lax.axis_size("expert")
    capacity = min(cent_rows, 2 * cent_rows * fanout // experts)
    if capacity == cent_rows and experts % 4 == 0:
        return per_device_dense(*args)
    return per_device_slots(*args)


def solution(mesh):
    placed = (
        P(("groups", "expert"), None),
        P(("groups", "expert"), None),
        P(("groups", "expert")),
        P(("groups", "expert"), None),
        P(("groups", "expert"), None),
        P("expert", None, None),
        P("expert", None, None),
        P("expert", None, None),
    )
    return jax.shard_map(
        per_device,
        mesh=mesh,
        in_specs=placed,
        out_specs=(P(("groups", "expert"), None), P(("groups", "expert"), None)),
        check_vma=False,
    )
```
